32 devices in a mesh: gx: 8 (over z, x), gy: 4 (over y, core).
Axes of the slice: x: 2, y: 2, z: 4, core: 2. Of those that a mesh axis runs over, the one named last changes fastest.
Arguments:
- prior_basis: float32 [128, 128, 128], P('gx', 'gy'), may hold values from -6 to 6
- cond_x: float32 [128, 128], P('gx', 'gy'), may hold values from 0.5 to 5
- cond_y: float32 [128, 128], P('gx', 'gy'), may hold values from 0.5 to 5
- capacitance: float32 [128, 128], P('gx', 'gy'), may hold values from 0.05 to 1
- pad_mask: int32 [128, 128], P('gx', 'gy'), may hold values 0 or 1
- port_nodes: int32 [128], replicated, may hold values from 0 to 16383
Outputs:
- new_basis: float32 [128, 128, 128], P('gx', 'gy')
- reduced_g: float32 [128, 128], replicated
- reduced_c: float32 [128, 128], replicated
The draws below stay inside these ranges and needn't reach their ends.
Inputs may be any that keep to these rules, and one draw needn't show every extreme that they name: `port_nodes`: a row-major node index into the grid of 128 x 128 nodes.
All inputs are finite; a program needn't handle non-finite values. No bound on the sum of `pad_mask` on one device may be relied on, other than what follows from the above.
Results may differ from the reference program's by a relative error of at most 0.0003.
Values sent between devices are 32-bit elements; how exact they have to be, the bound alone decides.
No kernel may reach another device: no remote copies, remote signals or barrier semaphores. Data moves between devices by JAX's collectives and lax.ppermute only.
A program may use at most 64 MiB of HBM per device.

```python
import math
import jax
import jax.numpy as jnp
from jax import lax

P_SIZE = 128
PRIOR = 128
SWEEPS = 4
NX = 128
NY = 128


def with_ends(result, own_key, least, largest):
    longest = result.shape.index(max(result.shape))
    spots = []
    for shift in (0, 1):
        where = [jax.random.randint(jax.random.fold_in(own_key, axis), (), 0, length) for axis, length in enumerate(result.shape)]
        where[longest] = (where[longest] + shift) % result.shape[longest]
        spots.append(tuple(where))
    return result.at[spots[0]].set(least).at[spots[1]].set(largest)


def levels(key, dims, pieces, smallest, top_value):
    factor_of = 1.0
    for axis_at, parts in pieces:
        heights = jax.random.uniform(jax.random.fold_in(jax.random.fold_in(key, 6), axis_at), (parts,), jnp.float32, smallest / len(pieces), top_value / len(pieces))
        factor_of = factor_of * jnp.repeat(jnp.exp(heights), dims[axis_at] // parts).reshape((-1,) + (1,) * (len(dims) - 1 - axis_at))
    return factor_of


def scatter_about(rng, shape, deviation, limit, shards=(), held_as=jnp.bfloat16):
    drawn = deviation * jax.random.normal(rng, shape, jnp.float32)
    if shards:
        drawn = drawn * levels(rng, shape, shards, -0.22, 0.18)
    return jnp.clip(drawn, -limit, limit).astype(held_as)


def setup_inputs(seed: int = 0) -> dict:
    key_of = jax.random.split(jax.random.key(seed), 7)
    prior_basis = scatter_about(key_of[0], (NX, NY, PRIOR), 1.0, 6.0, ((0, 8), (1, 4)), jnp.float32)
    cond_x = jnp.clip(jnp.exp(math.log(5.0) - 2.3025851 * jax.random.uniform(key_of[1], (NX, NY), jnp.float32) ** levels(key_of[1], (NX, NY), ((0, 8), (1, 4)), -0.2, 0.2)), 0.5, 5.0)
    cond_y = jnp.clip(jnp.exp(math.log(5.0) - 2.3025851 * jax.random.uniform(key_of[2], (NX, NY), jnp.float32) ** levels(key_of[2], (NX, NY), ((0, 8), (1, 4)), -0.2, 0.2)), 0.5, 5.0)
    capacitance = jnp.clip(jnp.exp(math.log(1.0) - 2.9957323 * jax.random.uniform(key_of[3], (NX, NY), jnp.float32) ** levels(key_of[3], (NX, NY), ((0, 8), (1, 4)), -0.2, 0.2)), 0.05, 1.0)
    pad_mask = with_ends((jax.random.randint(key_of[4], (NX, NY), 0, 8) < 1).astype(jnp.int32), jax.random.fold_in(key_of[4], 1), 0, 1)
    port_nodes = with_ends(jax.random.randint(key_of[5], (P_SIZE,), 0, NX * NY), jax.random.fold_in(key_of[5], 1), 0, (NX * NY) - 1).astype(jnp.int32)
    return dict(prior_basis=prior_basis, cond_x=cond_x, cond_y=cond_y, capacitance=capacitance, pad_mask=pad_mask, port_nodes=port_nodes)


shift_point = 0.5
supply_conductance = 4.0
port_current = 8.0
highest = lax.Precision.HIGHEST

def coefficients(cond_x, cond_y, capacitance, pad_mask):
    rows = jnp.arange(NX)[:, None]
    cols = jnp.arange(NY)[None, :]
    cx = jnp.where(rows < NX - 1, cond_x, jnp.float32(0.0))
    cy = jnp.where(cols < NY - 1, cond_y, jnp.float32(0.0))
    cx_up = jnp.pad(cx, ((1, 0), (0, 0)))[:-1]
    cy_left = jnp.pad(cy, ((0, 0), (1, 0)))[:, :-1]
    diag_g = cx + cx_up + cy + cy_left + supply_conductance * pad_mask.astype(jnp.float32)
    return (cx, cy, cx_up, cy_left, diag_g)

def near(field, links):
    cx, cy, cx_up, cy_left = links
    ext = jnp.pad(field, ((1, 1), (1, 1), (0, 0)))
    total = cx[:, :, None] * ext[2:, 1:-1] + cx_up[:, :, None] * ext[:-2, 1:-1]
    return total + cy[:, :, None] * ext[1:-1, 2:] + cy_left[:, :, None] * ext[1:-1, :-2]

def inner(left, right, nodes):
    a = left.reshape(-1, left.shape[-1])
    b = right.reshape(-1, right.shape[-1])
    return jnp.einsum('cp,cq->pq', a.astype(jnp.float32), b.astype(jnp.float32), precision=highest, preferred_element_type=jnp.float32) / nodes

def reference(prior_basis, cond_x, cond_y, capacitance, pad_mask, port_nodes):
    cx, cy, cx_up, cy_left, diag_g = coefficients(cond_x, cond_y, capacitance, pad_mask)
    links = (cx, cy, cx_up, cy_left)
    diag = (diag_g + shift_point * capacitance)[:, :, None]
    nodes = NX * NY
    node_ids = jnp.arange(nodes, dtype=jnp.int32).reshape(NX, NY)
    onehot = (node_ids[:, :, None] == port_nodes[None, None, :]).astype(jnp.float32)
    rhs = capacitance[:, :, None] * prior_basis + port_current * onehot
    field = rhs / diag
    for sweep in range(SWEEPS):
        field = (rhs + near(field, links)) / diag
    proj = inner(prior_basis, field, nodes)
    cand = field - jnp.einsum('xyk,kp->xyp', prior_basis, proj, precision=highest)
    gram = inner(cand, cand, nodes)
    lower = jnp.linalg.cholesky(gram)
    flat = cand.reshape(-1, P_SIZE)
    basis_flat = lax.linalg.triangular_solve(lower, flat, left_side=False, lower=True, transpose_a=True)
    new_basis = basis_flat.reshape(NX, NY, P_SIZE)
    g_image = diag_g[:, :, None] * new_basis - near(new_basis, links)
    reduced_g = inner(new_basis, g_image, nodes)
    reduced_c = inner(new_basis, capacitance[:, :, None] * new_basis, nodes)
    return (new_basis, reduced_g, reduced_c)
```

```python
import jax
import jax.numpy as jnp
from jax import lax
from jax.sharding import PartitionSpec as P

SWEEPS = 4


shift_point = 0.5
supply_conductance = 4.0
port_current = 8.0
highest = lax.Precision.HIGHEST


def shifted(shard, axis, by):
    devices = lax.axis_size(axis)
    pairs = [(i, i + by) for i in range(devices) if 0 <= i + by < devices]
    return lax.ppermute(shard, axis, pairs)


def allsum(value, axes):
    for axis in axes:
        count = lax.axis_size(axis)
        if count & (count - 1):
            value = lax.psum(value, axis)
            continue
        step = 1
        while step < count:
            other = lax.ppermute(value, axis, [(i, i ^ step) for i in range(count)])
            value = value + other
            step *= 2
    return value


def halos(cells):
    above = shifted(cells[-1:], "gx", 1)
    below = shifted(cells[:1], "gx", -1)
    left = shifted(cells[:, -1:], "gy", 1)
    right = shifted(cells[:, :1], "gy", -1)
    return above, below, left, right


def neighbors(cells, links):
    cx, cy, cx_up, cy_left = links
    above, below, left, right = halos(cells)
    down = jnp.concatenate([cells[1:], below], axis=0)
    up = jnp.concatenate([above, cells[:-1]], axis=0)
    east = jnp.concatenate([cells[:, 1:], right], axis=1)
    west = jnp.concatenate([left, cells[:, :-1]], axis=1)
    total = cx[:, :, None] * down + cx_up[:, :, None] * up
    return total + cy[:, :, None] * east + cy_left[:, :, None] * west


def local_inner(left, right):
    a = left.reshape(-1, left.shape[-1])
    b = right.reshape(-1, right.shape[-1])
    return jnp.einsum("cp,cq->pq", a, b, precision=highest, preferred_element_type=jnp.float32)


def per_device(prior_basis, cond_x, cond_y, capacitance, pad_mask, port_nodes):
    rows_dev, cols_dev = cond_x.shape
    width = port_nodes.shape[0]
    count_x = lax.axis_size("gx")
    count_y = lax.axis_size("gy")
    total_rows = rows_dev * count_x
    total_cols = cols_dev * count_y
    nodes = total_rows * total_cols
    row_start = lax.axis_index("gx") * rows_dev
    col_start = lax.axis_index("gy") * cols_dev
    global_rows = row_start + jnp.arange(rows_dev, dtype=jnp.int32)[:, None]
    global_cols = col_start + jnp.arange(cols_dev, dtype=jnp.int32)[None, :]
    cx = jnp.where(global_rows < total_rows - 1, cond_x, jnp.float32(0.0))
    cy = jnp.where(global_cols < total_cols - 1, cond_y, jnp.float32(0.0))
    above = shifted(cx[-1:, :], "gx", 1)
    beside = shifted(cy[:, -1:], "gy", 1)
    cx_up = jnp.concatenate([above, cx[:-1]], axis=0)
    cy_left = jnp.concatenate([beside, cy[:, :-1]], axis=1)
    links = (cx, cy, cx_up, cy_left)
    diag_g = cx + cx_up + cy + cy_left + supply_conductance * pad_mask.astype(jnp.float32)
    diag = (diag_g + shift_point * capacitance)[:, :, None]
    node_ids = global_rows * total_cols + global_cols
    onehot = (node_ids[:, :, None] == port_nodes[None, None, :]).astype(jnp.float32)
    rhs = capacitance[:, :, None] * prior_basis + port_current * onehot

    field = rhs / diag
    for _ in range(SWEEPS):
        field = (rhs + neighbors(field, links)) / diag
    proj = allsum(local_inner(prior_basis, field), ("gy", "gx")) / nodes
    cand = field - jnp.einsum("xyk,kp->xyp", prior_basis, proj, precision=highest)
    gram = allsum(local_inner(cand, cand), ("gy", "gx")) / nodes
    lower = jnp.linalg.cholesky(gram)
    flat = cand.reshape(-1, width)
    basis_flat = lax.linalg.triangular_solve(
        lower, flat, left_side=False, lower=True, transpose_a=True
    )
    new_basis = basis_flat.reshape(rows_dev, cols_dev, width)
    g_image = diag_g[:, :, None] * new_basis - neighbors(new_basis, links)
    raw = allsum(
        jnp.stack(
            [
                local_inner(new_basis, g_image),
                local_inner(new_basis, capacitance[:, :, None] * new_basis),
            ]
        ),
        ("gy", "gx"),
    )
    reduced_g = raw[0] / nodes
    reduced_c = raw[1] / nodes
    return (new_basis, reduced_g, reduced_c)


def solution(mesh):
    placed = (P("gx", "gy", None), P("gx", "gy"), P("gx", "gy"), P("gx", "gy"), P("gx", "gy"), P())
    return jax.shard_map(
        per_device,
        mesh=mesh,
        in_specs=placed,
        out_specs=(P("gx", "gy", None), P(), P()),
        check_vma=False,
    )
```

```python
import jax
import jax.numpy as jnp
from jax import lax
from jax.sharding import PartitionSpec as P

SWEEPS = 4
HALO = 8


shift_point = 0.5
supply_conductance = 4.0
port_current = 8.0
highest = lax.Precision.HIGHEST


def shifted(shard, axis, by):
    devices = lax.axis_size(axis)
    pairs = [(i, i + by) for i in range(devices) if 0 <= i + by < devices]
    return lax.ppermute(shard, axis, pairs)


def allsum(value, axes):
    for axis in axes:
        count = lax.axis_size(axis)
        if count & (count - 1):
            value = lax.psum(value, axis)
            continue
        step = 1
        while step < count:
            other = lax.ppermute(value, axis, [(i, i ^ step) for i in range(count)])
            value = value + other
            step *= 2
    return value


def pack(block, coefs):
    width = block.shape[-1]
    flat = coefs.reshape(-1)
    spare = (-flat.shape[0]) % width
    flat = jnp.pad(flat, (0, spare))
    return jnp.concatenate([block.reshape(-1, width), flat.reshape(-1, width)], axis=0)


def unpack(packed, block_shape, coef_shape):
    count = block_shape[0] * block_shape[1]
    block = packed[:count].reshape(block_shape)
    size = coef_shape[0] * coef_shape[1] * coef_shape[2]
    coefs = packed[count:].reshape(-1)[:size].reshape(coef_shape)
    return block, coefs


def widen(block, coefs, axis, dim, depth):
    head = lax.slice_in_dim(block, 0, depth, axis=dim)
    tail = lax.slice_in_dim(block, block.shape[dim] - depth, block.shape[dim], axis=dim)
    chead = lax.slice_in_dim(coefs, 0, depth, axis=dim + 1)
    ctail = lax.slice_in_dim(coefs, coefs.shape[dim + 1] - depth, coefs.shape[dim + 1], axis=dim + 1)
    before = shifted(pack(tail, ctail), axis, 1)
    after = shifted(pack(head, chead), axis, -1)
    before_b, before_c = unpack(before, head.shape, chead.shape)
    after_b, after_c = unpack(after, head.shape, chead.shape)
    block = jnp.concatenate([before_b, block, after_b], axis=dim)
    coefs = jnp.concatenate([before_c, coefs, after_c], axis=dim + 1)
    return block, coefs


def inset(cells, by):
    if by == 0:
        return cells
    return cells[by:cells.shape[0] - by, by:cells.shape[1] - by]


def neighbors(cells, links):
    cx, cy, cx_up, cy_left = links
    total = cx[:, :, None] * cells[2:, 1:-1] + cx_up[:, :, None] * cells[:-2, 1:-1]
    return total + cy[:, :, None] * cells[1:-1, 2:] + cy_left[:, :, None] * cells[1:-1, :-2]


def local_inner(left, right):
    a = left.reshape(-1, left.shape[-1])
    b = right.reshape(-1, right.shape[-1])
    return jnp.einsum("cp,cq->pq", a, b, precision=highest, preferred_element_type=jnp.float32)


def per_device(prior_basis, cond_x, cond_y, capacitance, pad_mask, port_nodes):
    rows_dev, cols_dev = cond_x.shape
    width = port_nodes.shape[0]
    count_x = lax.axis_size("gx")
    count_y = lax.axis_size("gy")
    total_rows = rows_dev * count_x
    total_cols = cols_dev * count_y
    nodes = total_rows * total_cols
    depth = HALO

    coefs = jnp.stack([cond_x, cond_y, capacitance, pad_mask.astype(jnp.float32)])
    basis_e, coefs_e = widen(prior_basis, coefs, "gx", 0, depth)
    basis_e, coefs_e = widen(basis_e, coefs_e, "gy", 1, depth)

    row_start = lax.axis_index("gx") * rows_dev - depth
    col_start = lax.axis_index("gy") * cols_dev - depth
    shape_e = (rows_dev + 2 * depth, cols_dev + 2 * depth)
    grows = row_start + lax.broadcasted_iota(jnp.int32, shape_e, 0)
    gcols = col_start + lax.broadcasted_iota(jnp.int32, shape_e, 1)
    inside = (grows >= 0) & (grows < total_rows) & (gcols >= 0) & (gcols < total_cols)
    cx_e = jnp.where(grows < total_rows - 1, coefs_e[0], jnp.float32(0.0))
    cy_e = jnp.where(gcols < total_cols - 1, coefs_e[1], jnp.float32(0.0))
    cap_e = coefs_e[2]
    pad_e = coefs_e[3]

    def at(cells, margin):
        return inset(cells, depth - margin)

    top = depth - 1
    cx_t = at(cx_e, top)
    cy_t = at(cy_e, top)
    cx_up_t = cx_e[0:-2, 1:-1]
    cy_left_t = cy_e[1:-1, 0:-2]
    diag_g_t = cx_t + cx_up_t + cy_t + cy_left_t + supply_conductance * at(pad_e, top)
    diag_t = diag_g_t + shift_point * at(cap_e, top)
    diag_t = jnp.where(at(inside, top), diag_t, jnp.float32(1.0))

    def links_at(margin):
        cut = top - margin
        return tuple(inset(c, cut) for c in (cx_t, cy_t, cx_up_t, cy_left_t))

    first = SWEEPS + 1
    node_ids = at(grows, first) * total_cols + at(gcols, first)
    onehot = (node_ids[:, :, None] == port_nodes[None, None, :]) & at(inside, first)[:, :, None]
    rhs = at(cap_e, first)[:, :, None] * at(basis_e, first) + port_current * onehot.astype(jnp.float32)
    diag_f = inset(diag_t, top - first)[:, :, None]

    field = rhs / diag_f
    for sweep in range(SWEEPS):
        margin = first - 1 - sweep
        field = (inset(rhs, first - margin) + neighbors(field, links_at(margin))) / inset(diag_f, first - margin)

    tile_basis = at(basis_e, 0)
    proj = allsum(local_inner(tile_basis, inset(field, 1)), ("gy", "gx")) / nodes
    cand_1 = field - jnp.einsum("xyk,kp->xyp", at(basis_e, 1), proj, precision=highest)
    cand = inset(cand_1, 1)
    diag_g = inset(diag_g_t, top)[:, :, None]
    g_image = diag_g * cand - neighbors(cand_1, links_at(0))
    c_image = at(cap_e, 0)[:, :, None] * cand
    raw = allsum(
        jnp.stack([local_inner(cand, cand), local_inner(cand, g_image), local_inner(cand, c_image)]),
        ("gy", "gx"),
    ) / nodes
    lower = jnp.linalg.cholesky(raw[0])
    inverse = lax.linalg.triangular_solve(
        lower, jnp.eye(width, dtype=jnp.float32), left_side=True, lower=True
    )
    new_basis = jnp.einsum("xyp,qp->xyq", cand, inverse, precision=highest)

    def congruent(block):
        half = jnp.einsum("pk,kq->pq", inverse, block, precision=highest)
        return jnp.einsum("pk,qk->pq", half, inverse, precision=highest)

    reduced_g = congruent(raw[1])
    reduced_c = congruent(raw[2])
    return (new_basis, reduced_g, reduced_c)


def solution(mesh):
    placed = (P("gx", "gy", None), P("gx", "gy"), P("gx", "gy"), P("gx", "gy"), P("gx", "gy"), P())
    return jax.shard_map(
        per_device,
        mesh=mesh,
        in_specs=placed,
        out_specs=(P("gx", "gy", None), P(), P()),
        check_vma=False,
    )
```

```python
import jax
import jax.numpy as jnp
from jax import lax
from jax.sharding import PartitionSpec as P

SWEEPS = 4
HALO = 8


shift_point = 0.5
supply_conductance = 4.0
port_current = 8.0
highest = lax.Precision.HIGHEST


def shifted(shard, axis, by):
    devices = lax.axis_size(axis)
    pairs = [(i, i + by) for i in range(devices) if 0 <= i + by < devices]
    return lax.ppermute(shard, axis, pairs)


def allsum(value, axes):
    for axis in axes:
        count = lax.axis_size(axis)
        if count & (count - 1):
            value = lax.psum(value, axis)
            continue
        step = 1
        while step < count:
            other = lax.ppermute(value, axis, [(i, i ^ step) for i in range(count)])
            value = value + other
            step *= 2
    return value


def pack(block, coefs):
    width = block.shape[-1]
    flat = coefs.reshape(-1)
    spare = (-flat.shape[0]) % width
    flat = jnp.pad(flat, (0, spare))
    return jnp.concatenate([block.reshape(-1, width), flat.reshape(-1, width)], axis=0)


def unpack(packed, block_shape, coef_shape):
    count = block_shape[0] * block_shape[1]
    block = packed[:count].reshape(block_shape)
    size = coef_shape[0] * coef_shape[1] * coef_shape[2]
    coefs = packed[count:].reshape(-1)[:size].reshape(coef_shape)
    return block, coefs


def widen(block, coefs, axis, dim, depth):
    head = lax.slice_in_dim(block, 0, depth, axis=dim)
    tail = lax.slice_in_dim(block, block.shape[dim] - depth, block.shape[dim], axis=dim)
    chead = lax.slice_in_dim(coefs, 0, depth, axis=dim + 1)
    ctail = lax.slice_in_dim(coefs, coefs.shape[dim + 1] - depth, coefs.shape[dim + 1], axis=dim + 1)
    before = shifted(pack(tail, ctail), axis, 1)
    after = shifted(pack(head, chead), axis, -1)
    before_b, before_c = unpack(before, head.shape, chead.shape)
    after_b, after_c = unpack(after, head.shape, chead.shape)
    block = jnp.concatenate([before_b, block, after_b], axis=dim)
    coefs = jnp.concatenate([before_c, coefs, after_c], axis=dim + 1)
    return block, coefs


def inset(cells, by):
    if by == 0:
        return cells
    return cells[by:cells.shape[0] - by, by:cells.shape[1] - by]


def neighbors(cells, links):
    cx, cy, cx_up, cy_left = links
    total = cx[:, :, None] * cells[2:, 1:-1] + cx_up[:, :, None] * cells[:-2, 1:-1]
    return total + cy[:, :, None] * cells[1:-1, 2:] + cy_left[:, :, None] * cells[1:-1, :-2]


def local_inner(left, right):
    a = left.reshape(-1, left.shape[-1])
    b = right.reshape(-1, right.shape[-1])
    return jnp.einsum("cp,cq->pq", a, b, precision=highest, preferred_element_type=jnp.float32)


def fold(first, second, third):
    size = first.shape[0]
    row = lax.broadcasted_iota(jnp.int32, first.shape, 0)
    col = lax.broadcasted_iota(jnp.int32, first.shape, 1)
    upper = row <= col
    diag = jnp.diagonal(third)
    spill = jnp.where((row == size - 1) & (col < size - 1), diag[None, :], jnp.float32(0.0))
    spill = jnp.where((row == size - 2) & (col == 0), diag[size - 1], spill)
    return jnp.stack([jnp.where(upper, first, third), jnp.where(upper, second, spill)])


def unfold(packed):
    size = packed.shape[1]
    row = lax.broadcasted_iota(jnp.int32, packed.shape[1:], 0)
    col = lax.broadcasted_iota(jnp.int32, packed.shape[1:], 1)
    upper = row <= col
    strict = row < col
    one, two = packed[0], packed[1]
    first = jnp.where(upper, one, one.T)
    second = jnp.where(upper, two, two.T)
    diag = jnp.concatenate([two[size - 1, : size - 1], two[size - 2, :1]])
    low = jnp.where(strict.T, one, jnp.float32(0.0))
    third = low + low.T + jnp.where(row == col, diag[None, :], jnp.float32(0.0))
    return first, second, third


def per_device(prior_basis, cond_x, cond_y, capacitance, pad_mask, port_nodes):
    rows_dev, cols_dev = cond_x.shape
    width = port_nodes.shape[0]
    count_x = lax.axis_size("gx")
    count_y = lax.axis_size("gy")
    total_rows = rows_dev * count_x
    total_cols = cols_dev * count_y
    nodes = total_rows * total_cols
    depth = HALO

    coefs = jnp.stack([cond_x, cond_y, capacitance, pad_mask.astype(jnp.float32)])
    basis_e, coefs_e = widen(prior_basis, coefs, "gx", 0, depth)
    basis_e, coefs_e = widen(basis_e, coefs_e, "gy", 1, depth)

    row_start = lax.axis_index("gx") * rows_dev - depth
    col_start = lax.axis_index("gy") * cols_dev - depth
    shape_e = (rows_dev + 2 * depth, cols_dev + 2 * depth)
    grows = row_start + lax.broadcasted_iota(jnp.int32, shape_e, 0)
    gcols = col_start + lax.broadcasted_iota(jnp.int32, shape_e, 1)
    inside = (grows >= 0) & (grows < total_rows) & (gcols >= 0) & (gcols < total_cols)
    cx_e = jnp.where(grows < total_rows - 1, coefs_e[0], jnp.float32(0.0))
    cy_e = jnp.where(gcols < total_cols - 1, coefs_e[1], jnp.float32(0.0))
    cap_e = coefs_e[2]
    pad_e = coefs_e[3]

    def at(cells, margin):
        return inset(cells, depth - margin)

    top = depth - 1
    cx_t = at(cx_e, top)
    cy_t = at(cy_e, top)
    cx_up_t = cx_e[0:-2, 1:-1]
    cy_left_t = cy_e[1:-1, 0:-2]
    diag_g_t = cx_t + cx_up_t + cy_t + cy_left_t + supply_conductance * at(pad_e, top)
    diag_t = diag_g_t + shift_point * at(cap_e, top)
    diag_t = jnp.where(at(inside, top), diag_t, jnp.float32(1.0))

    def links_at(margin):
        cut = top - margin
        return tuple(inset(c, cut) for c in (cx_t, cy_t, cx_up_t, cy_left_t))

    first = SWEEPS + 1
    node_ids = at(grows, first) * total_cols + at(gcols, first)
    onehot = (node_ids[:, :, None] == port_nodes[None, None, :]) & at(inside, first)[:, :, None]
    rhs = at(cap_e, first)[:, :, None] * at(basis_e, first) + port_current * onehot.astype(jnp.float32)
    diag_f = inset(diag_t, top - first)[:, :, None]

    field = rhs / diag_f
    for sweep in range(SWEEPS):
        margin = first - 1 - sweep
        field = (inset(rhs, first - margin) + neighbors(field, links_at(margin))) / inset(diag_f, first - margin)

    tile_basis = at(basis_e, 0)
    proj = allsum(local_inner(tile_basis, inset(field, 1)), ("gy", "gx")) / nodes
    cand_1 = field - jnp.einsum("xyk,kp->xyp", at(basis_e, 1), proj, precision=highest)
    cand = inset(cand_1, 1)
    diag_g = inset(diag_g_t, top)[:, :, None]
    g_image = diag_g * cand - neighbors(cand_1, links_at(0))
    c_image = at(cap_e, 0)[:, :, None] * cand
    gram, g_raw, c_raw = local_inner(cand, cand), local_inner(cand, g_image), local_inner(cand, c_image)
    packed = allsum(fold(gram, g_raw, c_raw), ("gy", "gx")) / nodes
    gram, g_raw, c_raw = unfold(packed)
    lower = jnp.linalg.cholesky(gram)
    inverse = lax.linalg.triangular_solve(
        lower, jnp.eye(width, dtype=jnp.float32), left_side=True, lower=True
    )
    new_basis = jnp.einsum("xyp,qp->xyq", cand, inverse, precision=highest)

    def congruent(block):
        half = jnp.einsum("pk,kq->pq", inverse, block, precision=highest)
        return jnp.einsum("pk,qk->pq", half, inverse, precision=highest)

    reduced_g = congruent(g_raw)
    reduced_c = congruent(c_raw)
    return (new_basis, reduced_g, reduced_c)


def solution(mesh):
    placed = (P("gx", "gy", None), P("gx", "gy"), P("gx", "gy"), P("gx", "gy"), P("gx", "gy"), P())
    return jax.shard_map(
        per_device,
        mesh=mesh,
        in_specs=placed,
        out_specs=(P("gx", "gy", None), P(), P()),
        check_vma=False,
    )
```

```python
import jax
import jax.numpy as jnp
from jax import lax
from jax.experimental import pallas as pl
from jax.experimental.pallas import tpu as pltpu
from jax.sharding import PartitionSpec as P

SWEEPS = 4
HALO = 8


shift_point = 0.5
supply_conductance = 4.0
port_current = 8.0
highest = lax.Precision.HIGHEST


def shifted(shard, axis, by):
    devices = lax.axis_size(axis)
    pairs = [(i, i + by) for i in range(devices) if 0 <= i + by < devices]
    return lax.ppermute(shard, axis, pairs)


def allsum(value, axes):
    for axis in axes:
        count = lax.axis_size(axis)
        if count & (count - 1):
            value = lax.psum(value, axis)
            continue
        step = 1
        while step < count:
            other = lax.ppermute(value, axis, [(i, i ^ step) for i in range(count)])
            value = value + other
            step *= 2
    return value


def pack(block, coefs):
    width = block.shape[-1]
    flat = coefs.reshape(-1)
    spare = (-flat.shape[0]) % width
    flat = jnp.pad(flat, (0, spare))
    return jnp.concatenate([block.reshape(-1, width), flat.reshape(-1, width)], axis=0)


def unpack(packed, block_shape, coef_shape):
    count = block_shape[0] * block_shape[1]
    block = packed[:count].reshape(block_shape)
    size = coef_shape[0] * coef_shape[1] * coef_shape[2]
    coefs = packed[count:].reshape(-1)[:size].reshape(coef_shape)
    return block, coefs


def widen(block, coefs, axis, dim, depth):
    head = lax.slice_in_dim(block, 0, depth, axis=dim)
    tail = lax.slice_in_dim(block, block.shape[dim] - depth, block.shape[dim], axis=dim)
    chead = lax.slice_in_dim(coefs, 0, depth, axis=dim + 1)
    ctail = lax.slice_in_dim(coefs, coefs.shape[dim + 1] - depth, coefs.shape[dim + 1], axis=dim + 1)
    before = shifted(pack(tail, ctail), axis, 1)
    after = shifted(pack(head, chead), axis, -1)
    before_b, before_c = unpack(before, head.shape, chead.shape)
    after_b, after_c = unpack(after, head.shape, chead.shape)
    block = jnp.concatenate([before_b, block, after_b], axis=dim)
    coefs = jnp.concatenate([before_c, coefs, after_c], axis=dim + 1)
    return block, coefs


def inset(cells, by):
    if by == 0:
        return cells
    return cells[by:cells.shape[0] - by, by:cells.shape[1] - by]


def neighbors(cells, links):
    cx, cy, cx_up, cy_left = links
    total = cx[:, :, None] * cells[2:, 1:-1] + cx_up[:, :, None] * cells[:-2, 1:-1]
    return total + cy[:, :, None] * cells[1:-1, 2:] + cy_left[:, :, None] * cells[1:-1, :-2]


def local_inner(left, right):
    a = left.reshape(-1, left.shape[-1])
    b = right.reshape(-1, right.shape[-1])
    return jnp.einsum("cp,cq->pq", a, b, precision=highest, preferred_element_type=jnp.float32)


def fold(first, second, third):
    size = first.shape[0]
    row = lax.broadcasted_iota(jnp.int32, first.shape, 0)
    col = lax.broadcasted_iota(jnp.int32, first.shape, 1)
    upper = row <= col
    diag = jnp.diagonal(third)
    spill = jnp.where((row == size - 1) & (col < size - 1), diag[None, :], jnp.float32(0.0))
    spill = jnp.where((row == size - 2) & (col == 0), diag[size - 1], spill)
    return jnp.stack([jnp.where(upper, first, third), jnp.where(upper, second, spill)])


def unfold(packed):
    size = packed.shape[1]
    row = lax.broadcasted_iota(jnp.int32, packed.shape[1:], 0)
    col = lax.broadcasted_iota(jnp.int32, packed.shape[1:], 1)
    upper = row <= col
    strict = row < col
    one, two = packed[0], packed[1]
    first = jnp.where(upper, one, one.T)
    second = jnp.where(upper, two, two.T)
    diag = jnp.concatenate([two[size - 1, : size - 1], two[size - 2, :1]])
    low = jnp.where(strict.T, one, jnp.float32(0.0))
    third = low + low.T + jnp.where(row == col, diag[None, :], jnp.float32(0.0))
    return first, second, third


def _inverse_factor_kernel(gram_ref, out_ref, work_ref):
    size = gram_ref.shape[0]
    work_ref[...] = gram_ref[...]
    rows = lax.broadcasted_iota(jnp.int32, (size, size), 0)
    cols = lax.broadcasted_iota(jnp.int32, (size, size), 1)
    out_ref[...] = jnp.where(rows == cols, jnp.float32(1.0), jnp.float32(0.0))
    lane = lax.broadcasted_iota(jnp.int32, (1, size), 1)
    sub = lax.broadcasted_iota(jnp.int32, (size, 1), 0)

    def step(j, carry):
        whole = work_ref[...]
        row = work_ref[pl.ds(j, 1), :]
        column = jnp.sum(jnp.where(cols == j, whole, jnp.float32(0.0)), axis=1, keepdims=True)
        pivot = jnp.sum(jnp.where(lane == j, row, jnp.float32(0.0)), axis=1, keepdims=True)
        root = jnp.sqrt(pivot)
        right = jnp.where(lane >= j, row / root, jnp.float32(0.0))
        left = jnp.where(sub >= j, column / root, jnp.float32(0.0))
        work_ref[...] = whole - left * right
        head = out_ref[pl.ds(j, 1), :] / root
        below = jnp.where(sub > j, left, jnp.float32(0.0))
        out_ref[...] = out_ref[...] - below * head
        out_ref[pl.ds(j, 1), :] = head
        return carry

    lax.fori_loop(0, size, step, 0)


def inverse_factor(gram):
    size = gram.shape[0]
    return pl.pallas_call(
        _inverse_factor_kernel,
        out_shape=jax.ShapeDtypeStruct((size, size), jnp.float32),
        scratch_shapes=[pltpu.VMEM((size, size), jnp.float32)],
    )(gram)


def per_device(prior_basis, cond_x, cond_y, capacitance, pad_mask, port_nodes):
    rows_dev, cols_dev = cond_x.shape
    width = port_nodes.shape[0]
    count_x = lax.axis_size("gx")
    count_y = lax.axis_size("gy")
    total_rows = rows_dev * count_x
    total_cols = cols_dev * count_y
    nodes = total_rows * total_cols
    depth = HALO

    coefs = jnp.stack([cond_x, cond_y, capacitance, pad_mask.astype(jnp.float32)])
    basis_e, coefs_e = widen(prior_basis, coefs, "gx", 0, depth)
    basis_e, coefs_e = widen(basis_e, coefs_e, "gy", 1, depth)

    row_start = lax.axis_index("gx") * rows_dev - depth
    col_start = lax.axis_index("gy") * cols_dev - depth
    shape_e = (rows_dev + 2 * depth, cols_dev + 2 * depth)
    grows = row_start + lax.broadcasted_iota(jnp.int32, shape_e, 0)
    gcols = col_start + lax.broadcasted_iota(jnp.int32, shape_e, 1)
    inside = (grows >= 0) & (grows < total_rows) & (gcols >= 0) & (gcols < total_cols)
    cx_e = jnp.where(grows < total_rows - 1, coefs_e[0], jnp.float32(0.0))
    cy_e = jnp.where(gcols < total_cols - 1, coefs_e[1], jnp.float32(0.0))
    cap_e = coefs_e[2]
    pad_e = coefs_e[3]

    def at(cells, margin):
        return inset(cells, depth - margin)

    top = depth - 1
    cx_t = at(cx_e, top)
    cy_t = at(cy_e, top)
    cx_up_t = cx_e[0:-2, 1:-1]
    cy_left_t = cy_e[1:-1, 0:-2]
    diag_g_t = cx_t + cx_up_t + cy_t + cy_left_t + supply_conductance * at(pad_e, top)
    diag_t = diag_g_t + shift_point * at(cap_e, top)
    diag_t = jnp.where(at(inside, top), diag_t, jnp.float32(1.0))

    def links_at(margin):
        cut = top - margin
        return tuple(inset(c, cut) for c in (cx_t, cy_t, cx_up_t, cy_left_t))

    first = SWEEPS + 1
    node_ids = at(grows, first) * total_cols + at(gcols, first)
    onehot = (node_ids[:, :, None] == port_nodes[None, None, :]) & at(inside, first)[:, :, None]
    rhs = at(cap_e, first)[:, :, None] * at(basis_e, first) + port_current * onehot.astype(jnp.float32)
    diag_f = inset(diag_t, top - first)[:, :, None]

    field = rhs / diag_f
    for sweep in range(SWEEPS):
        margin = first - 1 - sweep
        field = (inset(rhs, first - margin) + neighbors(field, links_at(margin))) / inset(diag_f, first - margin)

    tile_basis = at(basis_e, 0)
    proj = allsum(local_inner(tile_basis, inset(field, 1)), ("gy", "gx")) / nodes
    cand_1 = field - jnp.einsum("xyk,kp->xyp", at(basis_e, 1), proj, precision=highest)
    cand = inset(cand_1, 1)
    diag_g = inset(diag_g_t, top)[:, :, None]
    g_image = diag_g * cand - neighbors(cand_1, links_at(0))
    c_image = at(cap_e, 0)[:, :, None] * cand
    gram, g_raw, c_raw = local_inner(cand, cand), local_inner(cand, g_image), local_inner(cand, c_image)
    packed = allsum(fold(gram, g_raw, c_raw), ("gy", "gx")) / nodes
    gram, g_raw, c_raw = unfold(packed)
    inverse = inverse_factor(gram)
    new_basis = jnp.einsum("xyp,qp->xyq", cand, inverse, precision=highest)

    def congruent(block):
        half = jnp.einsum("pk,kq->pq", inverse, block, precision=highest)
        return jnp.einsum("pk,qk->pq", half, inverse, precision=highest)

    reduced_g = congruent(g_raw)
    reduced_c = congruent(c_raw)
    return (new_basis, reduced_g, reduced_c)


def solution(mesh):
    placed = (P("gx", "gy", None), P("gx", "gy"), P("gx", "gy"), P("gx", "gy"), P("gx", "gy"), P())
    return jax.shard_map(
        per_device,
        mesh=mesh,
        in_specs=placed,
        out_specs=(P("gx", "gy", None), P(), P()),
        check_vma=False,
    )
```

```python
import jax
import jax.numpy as jnp
from jax import lax
from jax.experimental import pallas as pl
from jax.experimental.pallas import tpu as pltpu
from jax.sharding import PartitionSpec as P

SWEEPS = 4


shift_point = 0.5
supply_conductance = 4.0
port_current = 8.0
highest = lax.Precision.HIGHEST


def shifted(shard, axis, by):
    devices = lax.axis_size(axis)
    pairs = [(i, i + by) for i in range(devices) if 0 <= i + by < devices]
    return lax.ppermute(shard, axis, pairs)


def allsum(value, axes):
    for axis in axes:
        count = lax.axis_size(axis)
        if count & (count - 1):
            value = lax.psum(value, axis)
            continue
        step = 1
        while step < count:
            other = lax.ppermute(value, axis, [(i, i ^ step) for i in range(count)])
            value = value + other
            step *= 2
    return value


def pack(block, coefs):
    width = block.shape[-1]
    flat = coefs.reshape(-1)
    spare = (-flat.shape[0]) % width
    flat = jnp.pad(flat, (0, spare))
    return jnp.concatenate([block.reshape(-1, width), flat.reshape(-1, width)], axis=0)


def unpack(packed, block_shape, coef_shape):
    count = block_shape[0] * block_shape[1]
    block = packed[:count].reshape(block_shape)
    size = coef_shape[0] * coef_shape[1] * coef_shape[2]
    coefs = packed[count:].reshape(-1)[:size].reshape(coef_shape)
    return block, coefs


def widen(block, coefs, axis, dim, depth, cdepth):
    head = lax.slice_in_dim(block, 0, depth, axis=dim)
    tail = lax.slice_in_dim(block, block.shape[dim] - depth, block.shape[dim], axis=dim)
    chead = lax.slice_in_dim(coefs, 0, cdepth, axis=dim + 1)
    ctail = lax.slice_in_dim(coefs, coefs.shape[dim + 1] - cdepth, coefs.shape[dim + 1], axis=dim + 1)
    before = shifted(pack(tail, ctail), axis, 1)
    after = shifted(pack(head, chead), axis, -1)
    before_b, before_c = unpack(before, head.shape, chead.shape)
    after_b, after_c = unpack(after, head.shape, chead.shape)
    block = jnp.concatenate([before_b, block, after_b], axis=dim)
    coefs = jnp.concatenate([before_c, coefs, after_c], axis=dim + 1)
    return block, coefs


def inset(cells, by):
    if by == 0:
        return cells
    return cells[by:cells.shape[0] - by, by:cells.shape[1] - by]


def neighbors(cells, links):
    cx, cy, cx_up, cy_left = links
    total = cx[:, :, None] * cells[2:, 1:-1] + cx_up[:, :, None] * cells[:-2, 1:-1]
    return total + cy[:, :, None] * cells[1:-1, 2:] + cy_left[:, :, None] * cells[1:-1, :-2]


def local_inner(left, right):
    a = left.reshape(-1, left.shape[-1])
    b = right.reshape(-1, right.shape[-1])
    return jnp.einsum("cp,cq->pq", a, b, precision=highest, preferred_element_type=jnp.float32)


def fold(first, second, third):
    size = first.shape[0]
    row = lax.broadcasted_iota(jnp.int32, first.shape, 0)
    col = lax.broadcasted_iota(jnp.int32, first.shape, 1)
    upper = row <= col
    diag = jnp.sum(jnp.where(row == col, third, jnp.float32(0.0)), axis=0)
    spill = jnp.where((row == size - 1) & (col < size - 1), diag[None, :], jnp.float32(0.0))
    spill = jnp.where((row == size - 2) & (col == 0), diag[size - 1], spill)
    return jnp.stack([jnp.where(upper, first, third), jnp.where(upper, second, spill)])


def unfold(packed):
    size = packed.shape[1]
    row = lax.broadcasted_iota(jnp.int32, packed.shape[1:], 0)
    col = lax.broadcasted_iota(jnp.int32, packed.shape[1:], 1)
    upper = row <= col
    strict = row < col
    one, two = packed[0], packed[1]
    first = jnp.where(upper, one, one.T)
    second = jnp.where(upper, two, two.T)
    diag = jnp.concatenate([two[size - 1, : size - 1], two[size - 2, :1]])
    low = jnp.where(strict.T, one, jnp.float32(0.0))
    third = low + low.T + jnp.where(row == col, diag[None, :], jnp.float32(0.0))
    return first, second, third


def _inverse_factor_kernel(gram_ref, out_ref, work_ref):
    size = gram_ref.shape[0]
    work_ref[...] = gram_ref[...]
    rows = lax.broadcasted_iota(jnp.int32, (size, size), 0)
    cols = lax.broadcasted_iota(jnp.int32, (size, size), 1)
    out_ref[...] = jnp.where(rows == cols, jnp.float32(1.0), jnp.float32(0.0))
    lane = lax.broadcasted_iota(jnp.int32, (1, size), 1)
    chunk = 8
    for lo in range(0, size, chunk):
        span = size - lo
        cols_s = lax.broadcasted_iota(jnp.int32, (span, size), 1)
        sub = lo + lax.broadcasted_iota(jnp.int32, (span, 1), 0)

        def step(j, carry, lo=lo, cols_s=cols_s, sub=sub):
            whole = work_ref[lo:, :]
            row = work_ref[pl.ds(j, 1), :]
            column = jnp.sum(jnp.where(cols_s == j, whole, jnp.float32(0.0)), axis=1, keepdims=True)
            pivot = jnp.sum(jnp.where(lane == j, row, jnp.float32(0.0)), axis=1, keepdims=True)
            scale = jnp.float32(1.0) / jnp.sqrt(pivot)
            right = jnp.where(lane >= j, row * scale, jnp.float32(0.0))
            left = jnp.where(sub >= j, column * scale, jnp.float32(0.0))
            head = out_ref[pl.ds(j, 1), :] * scale
            work_ref[lo:, :] = whole - left * right
            below = jnp.where(sub > j, left, jnp.float32(0.0))
            out_ref[lo:, :] = out_ref[lo:, :] - below * head
            out_ref[pl.ds(j, 1), :] = head
            return carry

        lax.fori_loop(lo, min(lo + chunk, size), step, 0)


def inverse_factor(gram):
    size = gram.shape[0]
    return pl.pallas_call(
        _inverse_factor_kernel,
        out_shape=jax.ShapeDtypeStruct((size, size), jnp.float32),
        scratch_shapes=[pltpu.VMEM((size, size), jnp.float32)],
    )(gram)


def per_device(prior_basis, cond_x, cond_y, capacitance, pad_mask, port_nodes):
    rows_dev, cols_dev = cond_x.shape
    width = port_nodes.shape[0]
    count_x = lax.axis_size("gx")
    count_y = lax.axis_size("gy")
    total_rows = rows_dev * count_x
    total_cols = cols_dev * count_y
    nodes = total_rows * total_cols
    bdepth = SWEEPS + 1
    depth = SWEEPS + 2

    coefs = jnp.stack([cond_x, cond_y, capacitance, pad_mask.astype(jnp.float32)])
    basis_e, coefs_e = widen(prior_basis, coefs, "gx", 0, bdepth, depth)
    basis_e, coefs_e = widen(basis_e, coefs_e, "gy", 1, bdepth, depth)

    row_start = lax.axis_index("gx") * rows_dev - depth
    col_start = lax.axis_index("gy") * cols_dev - depth
    shape_e = (rows_dev + 2 * depth, cols_dev + 2 * depth)
    grows = row_start + lax.broadcasted_iota(jnp.int32, shape_e, 0)
    gcols = col_start + lax.broadcasted_iota(jnp.int32, shape_e, 1)
    inside = (grows >= 0) & (grows < total_rows) & (gcols >= 0) & (gcols < total_cols)
    cx_e = jnp.where(grows < total_rows - 1, coefs_e[0], jnp.float32(0.0))
    cy_e = jnp.where(gcols < total_cols - 1, coefs_e[1], jnp.float32(0.0))
    cap_e = coefs_e[2]
    pad_e = coefs_e[3]

    def at(cells, margin):
        return inset(cells, depth - margin)

    def at_basis(margin):
        return inset(basis_e, bdepth - margin)

    top = depth - 1
    cx_t = at(cx_e, top)
    cy_t = at(cy_e, top)
    cx_up_t = cx_e[0:-2, 1:-1]
    cy_left_t = cy_e[1:-1, 0:-2]
    diag_g_t = cx_t + cx_up_t + cy_t + cy_left_t + supply_conductance * at(pad_e, top)
    diag_t = diag_g_t + shift_point * at(cap_e, top)
    diag_t = jnp.where(at(inside, top), diag_t, jnp.float32(1.0))

    def links_at(margin):
        cut = top - margin
        return tuple(inset(c, cut) for c in (cx_t, cy_t, cx_up_t, cy_left_t))

    first = SWEEPS + 1
    node_ids = at(grows, first) * total_cols + at(gcols, first)
    onehot = (node_ids[:, :, None] == port_nodes[None, None, :]) & at(inside, first)[:, :, None]
    rhs = at(cap_e, first)[:, :, None] * at_basis(first) + port_current * onehot.astype(jnp.float32)
    diag_f = inset(diag_t, top - first)[:, :, None]

    field = rhs / diag_f
    for sweep in range(SWEEPS):
        margin = first - 1 - sweep
        field = (inset(rhs, first - margin) + neighbors(field, links_at(margin))) / inset(diag_f, first - margin)

    tile_basis = at_basis(0)
    proj = allsum(local_inner(tile_basis, inset(field, 1)), ("gy", "gx")) / nodes
    cand_1 = field - jnp.einsum("xyk,kp->xyp", at_basis(1), proj, precision=highest)
    cand = inset(cand_1, 1)
    diag_g = inset(diag_g_t, top)[:, :, None]
    g_image = diag_g * cand - neighbors(cand_1, links_at(0))
    c_image = at(cap_e, 0)[:, :, None] * cand
    gram, g_raw, c_raw = local_inner(cand, cand), local_inner(cand, g_image), local_inner(cand, c_image)
    packed = allsum(fold(gram, g_raw, c_raw), ("gy", "gx")) / nodes
    gram, g_raw, c_raw = unfold(packed)
    inverse = inverse_factor(gram)
    new_basis = jnp.einsum("xyp,qp->xyq", cand, inverse, precision=highest)

    def congruent(block):
        half = jnp.einsum("pk,kq->pq", inverse, block, precision=highest)
        return jnp.einsum("pk,qk->pq", half, inverse, precision=highest)

    reduced_g = congruent(g_raw)
    reduced_c = congruent(c_raw)
    return (new_basis, reduced_g, reduced_c)


def solution(mesh):
    placed = (P("gx", "gy", None), P("gx", "gy"), P("gx", "gy"), P("gx", "gy"), P("gx", "gy"), P())
    return jax.shard_map(
        per_device,
        mesh=mesh,
        in_specs=placed,
        out_specs=(P("gx", "gy", None), P(), P()),
        check_vma=False,
    )
```

```python
import jax
import jax.numpy as jnp
from jax import lax
from jax.experimental import pallas as pl
from jax.experimental.pallas import tpu as pltpu
from jax.sharding import PartitionSpec as P

SWEEPS = 4


shift_point = 0.5
supply_conductance = 4.0
port_current = 8.0
highest = lax.Precision.HIGHEST


def shifted(shard, axis, by):
    devices = lax.axis_size(axis)
    pairs = [(i, i + by) for i in range(devices) if 0 <= i + by < devices]
    return lax.ppermute(shard, axis, pairs)


def allsum(value, axes):
    for axis in axes:
        count = lax.axis_size(axis)
        if count & (count - 1):
            value = lax.psum(value, axis)
            continue
        step = 1
        while step < count:
            other = lax.ppermute(value, axis, [(i, i ^ step) for i in range(count)])
            value = value + other
            step *= 2
    return value


def allsum_exchange(value, axes):
    count = 1
    for axis in axes:
        count *= lax.axis_size(axis)
    flat = value.reshape(-1, value.shape[-1])
    if flat.shape[0] % count:
        return allsum(value, axes)
    parts = flat.reshape(count, -1, flat.shape[-1])
    got = lax.all_to_all(parts, axes, 0, 0, tiled=False)
    total = got[0]
    for k in range(1, count):
        total = total + got[k]
    spread = jnp.broadcast_to(total[None], (count,) + total.shape)
    back = lax.all_to_all(spread, axes, 0, 0, tiled=False)
    return back.reshape(value.shape)


def pack(block, coefs):
    width = block.shape[-1]
    flat = coefs.reshape(-1)
    spare = (-flat.shape[0]) % width
    flat = jnp.pad(flat, (0, spare))
    return jnp.concatenate([block.reshape(-1, width), flat.reshape(-1, width)], axis=0)


def unpack(packed, block_shape, coef_shape):
    count = block_shape[0] * block_shape[1]
    block = packed[:count].reshape(block_shape)
    size = coef_shape[0] * coef_shape[1] * coef_shape[2]
    coefs = packed[count:].reshape(-1)[:size].reshape(coef_shape)
    return block, coefs


def widen(block, coefs, axis, dim, depth, cdepth):
    head = lax.slice_in_dim(block, 0, depth, axis=dim)
    tail = lax.slice_in_dim(block, block.shape[dim] - depth, block.shape[dim], axis=dim)
    chead = lax.slice_in_dim(coefs, 0, cdepth, axis=dim + 1)
    ctail = lax.slice_in_dim(coefs, coefs.shape[dim + 1] - cdepth, coefs.shape[dim + 1], axis=dim + 1)
    before = shifted(pack(tail, ctail), axis, 1)
    after = shifted(pack(head, chead), axis, -1)
    before_b, before_c = unpack(before, head.shape, chead.shape)
    after_b, after_c = unpack(after, head.shape, chead.shape)
    block = jnp.concatenate([before_b, block, after_b], axis=dim)
    coefs = jnp.concatenate([before_c, coefs, after_c], axis=dim + 1)
    return block, coefs


def inset(cells, by):
    if by == 0:
        return cells
    return cells[by:cells.shape[0] - by, by:cells.shape[1] - by]


def neighbors(cells, links):
    cx, cy, cx_up, cy_left = links
    total = cx[:, :, None] * cells[2:, 1:-1] + cx_up[:, :, None] * cells[:-2, 1:-1]
    return total + cy[:, :, None] * cells[1:-1, 2:] + cy_left[:, :, None] * cells[1:-1, :-2]


def local_inner(left, right):
    a = left.reshape(-1, left.shape[-1])
    b = right.reshape(-1, right.shape[-1])
    return jnp.einsum("cp,cq->pq", a, b, precision=highest, preferred_element_type=jnp.float32)


def fold(first, second, third):
    size = first.shape[0]
    row = lax.broadcasted_iota(jnp.int32, first.shape, 0)
    col = lax.broadcasted_iota(jnp.int32, first.shape, 1)
    upper = row <= col
    diag = jnp.sum(jnp.where(row == col, third, jnp.float32(0.0)), axis=0)
    spill = jnp.where((row == size - 1) & (col < size - 1), diag[None, :], jnp.float32(0.0))
    spill = jnp.where((row == size - 2) & (col == 0), diag[size - 1], spill)
    return jnp.stack([jnp.where(upper, first, third), jnp.where(upper, second, spill)])


def unfold(packed):
    size = packed.shape[1]
    row = lax.broadcasted_iota(jnp.int32, packed.shape[1:], 0)
    col = lax.broadcasted_iota(jnp.int32, packed.shape[1:], 1)
    upper = row <= col
    strict = row < col
    one, two = packed[0], packed[1]
    first = jnp.where(upper, one, one.T)
    second = jnp.where(upper, two, two.T)
    diag = jnp.concatenate([two[size - 1, : size - 1], two[size - 2, :1]])
    low = jnp.where(strict.T, one, jnp.float32(0.0))
    third = low + low.T + jnp.where(row == col, diag[None, :], jnp.float32(0.0))
    return first, second, third


def _inverse_factor_kernel(gram_ref, out_ref, work_ref):
    size = gram_ref.shape[0]
    work_ref[...] = gram_ref[...]
    rows = lax.broadcasted_iota(jnp.int32, (size, size), 0)
    cols = lax.broadcasted_iota(jnp.int32, (size, size), 1)
    out_ref[...] = jnp.where(rows == cols, jnp.float32(1.0), jnp.float32(0.0))
    lane = lax.broadcasted_iota(jnp.int32, (1, size), 1)
    chunk = 8
    for lo in range(0, size, chunk):
        span = size - lo
        cols_s = lax.broadcasted_iota(jnp.int32, (span, size), 1)
        sub = lo + lax.broadcasted_iota(jnp.int32, (span, 1), 0)

        def step(j, carry, lo=lo, cols_s=cols_s, sub=sub):
            whole = work_ref[lo:, :]
            row = work_ref[pl.ds(j, 1), :]
            column = jnp.sum(jnp.where(cols_s == j, whole, jnp.float32(0.0)), axis=1, keepdims=True)
            pivot = jnp.sum(jnp.where(lane == j, row, jnp.float32(0.0)), axis=1, keepdims=True)
            scale = jnp.float32(1.0) / jnp.sqrt(pivot)
            right = jnp.where(lane >= j, row * scale, jnp.float32(0.0))
            left = jnp.where(sub >= j, column * scale, jnp.float32(0.0))
            head = out_ref[pl.ds(j, 1), :] * scale
            work_ref[lo:, :] = whole - left * right
            below = jnp.where(sub > j, left, jnp.float32(0.0))
            out_ref[lo:, :] = out_ref[lo:, :] - below * head
            out_ref[pl.ds(j, 1), :] = head
            return carry

        lax.fori_loop(lo, min(lo + chunk, size), step, 0)


def inverse_factor(gram):
    size = gram.shape[0]
    return pl.pallas_call(
        _inverse_factor_kernel,
        out_shape=jax.ShapeDtypeStruct((size, size), jnp.float32),
        scratch_shapes=[pltpu.VMEM((size, size), jnp.float32)],
    )(gram)


def per_device(prior_basis, cond_x, cond_y, capacitance, pad_mask, port_nodes):
    rows_dev, cols_dev = cond_x.shape
    width = port_nodes.shape[0]
    count_x = lax.axis_size("gx")
    count_y = lax.axis_size("gy")
    total_rows = rows_dev * count_x
    total_cols = cols_dev * count_y
    nodes = total_rows * total_cols
    bdepth = SWEEPS + 1
    depth = SWEEPS + 2

    coefs = jnp.stack([cond_x, cond_y, capacitance, pad_mask.astype(jnp.float32)])
    basis_e, coefs_e = widen(prior_basis, coefs, "gx", 0, bdepth, depth)
    basis_e, coefs_e = widen(basis_e, coefs_e, "gy", 1, bdepth, depth)

    row_start = lax.axis_index("gx") * rows_dev - depth
    col_start = lax.axis_index("gy") * cols_dev - depth
    shape_e = (rows_dev + 2 * depth, cols_dev + 2 * depth)
    grows = row_start + lax.broadcasted_iota(jnp.int32, shape_e, 0)
    gcols = col_start + lax.broadcasted_iota(jnp.int32, shape_e, 1)
    inside = (grows >= 0) & (grows < total_rows) & (gcols >= 0) & (gcols < total_cols)
    cx_e = jnp.where(grows < total_rows - 1, coefs_e[0], jnp.float32(0.0))
    cy_e = jnp.where(gcols < total_cols - 1, coefs_e[1], jnp.float32(0.0))
    cap_e = coefs_e[2]
    pad_e = coefs_e[3]

    def at(cells, margin):
        return inset(cells, depth - margin)

    def at_basis(margin):
        return inset(basis_e, bdepth - margin)

    top = depth - 1
    cx_t = at(cx_e, top)
    cy_t = at(cy_e, top)
    cx_up_t = cx_e[0:-2, 1:-1]
    cy_left_t = cy_e[1:-1, 0:-2]
    diag_g_t = cx_t + cx_up_t + cy_t + cy_left_t + supply_conductance * at(pad_e, top)
    diag_t = diag_g_t + shift_point * at(cap_e, top)
    diag_t = jnp.where(at(inside, top), diag_t, jnp.float32(1.0))

    def links_at(margin):
        cut = top - margin
        return tuple(inset(c, cut) for c in (cx_t, cy_t, cx_up_t, cy_left_t))

    first = SWEEPS + 1
    node_ids = at(grows, first) * total_cols + at(gcols, first)
    onehot = (node_ids[:, :, None] == port_nodes[None, None, :]) & at(inside, first)[:, :, None]
    rhs = at(cap_e, first)[:, :, None] * at_basis(first) + port_current * onehot.astype(jnp.float32)
    diag_f = inset(diag_t, top - first)[:, :, None]

    field = rhs / diag_f
    for sweep in range(SWEEPS):
        margin = first - 1 - sweep
        field = (inset(rhs, first - margin) + neighbors(field, links_at(margin))) / inset(diag_f, first - margin)

    tile_basis = at_basis(0)
    proj = allsum_exchange(local_inner(tile_basis, inset(field, 1)), ("gx", "gy")) / nodes
    cand_1 = field - jnp.einsum("xyk,kp->xyp", at_basis(1), proj, precision=highest)
    cand = inset(cand_1, 1)
    diag_g = inset(diag_g_t, top)[:, :, None]
    g_image = diag_g * cand - neighbors(cand_1, links_at(0))
    c_image = at(cap_e, 0)[:, :, None] * cand
    gram, g_raw, c_raw = local_inner(cand, cand), local_inner(cand, g_image), local_inner(cand, c_image)
    packed = allsum_exchange(fold(gram, g_raw, c_raw), ("gx", "gy")) / nodes
    gram, g_raw, c_raw = unfold(packed)
    inverse = inverse_factor(gram)
    new_basis = jnp.einsum("xyp,qp->xyq", cand, inverse, precision=highest)

    def congruent(block):
        half = jnp.einsum("pk,kq->pq", inverse, block, precision=highest)
        return jnp.einsum("pk,qk->pq", half, inverse, precision=highest)

    reduced_g = congruent(g_raw)
    reduced_c = congruent(c_raw)
    return (new_basis, reduced_g, reduced_c)


def solution(mesh):
    placed = (P("gx", "gy", None), P("gx", "gy"), P("gx", "gy"), P("gx", "gy"), P("gx", "gy"), P())
    return jax.shard_map(
        per_device,
        mesh=mesh,
        in_specs=placed,
        out_specs=(P("gx", "gy", None), P(), P()),
        check_vma=False,
    )
```

```python
import jax
import jax.numpy as jnp
from jax import lax
from jax.experimental import pallas as pl
from jax.experimental.pallas import tpu as pltpu
from jax.sharding import PartitionSpec as P

SWEEPS = 4


shift_point = 0.5
supply_conductance = 4.0
port_current = 8.0
highest = lax.Precision.HIGHEST


def shifted(shard, axis, by):
    devices = lax.axis_size(axis)
    pairs = [(i, i + by) for i in range(devices) if 0 <= i + by < devices]
    return lax.ppermute(shard, axis, pairs)


def allsum(value, axes):
    for axis in axes:
        count = lax.axis_size(axis)
        if count & (count - 1):
            value = lax.psum(value, axis)
            continue
        step = 1
        while step < count:
            other = lax.ppermute(value, axis, [(i, i ^ step) for i in range(count)])
            value = value + other
            step *= 2
    return value


def allsum_exchange(value, axes):
    count = 1
    for axis in axes:
        count *= lax.axis_size(axis)
    flat = value.reshape(-1, value.shape[-1])
    if flat.shape[0] % count:
        return allsum(value, axes)
    parts = flat.reshape(count, -1, flat.shape[-1])
    got = lax.all_to_all(parts, axes, 0, 0, tiled=False)
    total = got[0]
    for k in range(1, count):
        total = total + got[k]
    spread = jnp.broadcast_to(total[None], (count,) + total.shape)
    back = lax.all_to_all(spread, axes, 0, 0, tiled=False)
    return back.reshape(value.shape)


def pack(block, coefs):
    width = block.shape[-1]
    flat = coefs.reshape(-1)
    spare = (-flat.shape[0]) % width
    flat = jnp.pad(flat, (0, spare))
    return jnp.concatenate([block.reshape(-1, width), flat.reshape(-1, width)], axis=0)


def unpack(packed, block_shape, coef_shape):
    count = block_shape[0] * block_shape[1]
    block = packed[:count].reshape(block_shape)
    size = coef_shape[0] * coef_shape[1] * coef_shape[2]
    coefs = packed[count:].reshape(-1)[:size].reshape(coef_shape)
    return block, coefs


def widen(block, coefs, axis, dim, depth, cdepth):
    head = lax.slice_in_dim(block, 0, depth, axis=dim)
    tail = lax.slice_in_dim(block, block.shape[dim] - depth, block.shape[dim], axis=dim)
    chead = lax.slice_in_dim(coefs, 0, cdepth, axis=dim + 1)
    ctail = lax.slice_in_dim(coefs, coefs.shape[dim + 1] - cdepth, coefs.shape[dim + 1], axis=dim + 1)
    before = shifted(pack(tail, ctail), axis, 1)
    after = shifted(pack(head, chead), axis, -1)
    before_b, before_c = unpack(before, head.shape, chead.shape)
    after_b, after_c = unpack(after, head.shape, chead.shape)
    block = jnp.concatenate([before_b, block, after_b], axis=dim)
    coefs = jnp.concatenate([before_c, coefs, after_c], axis=dim + 1)
    return block, coefs


def inset(cells, by):
    if by == 0:
        return cells
    return cells[by:cells.shape[0] - by, by:cells.shape[1] - by]


def neighbors(cells, links):
    cx, cy, cx_up, cy_left = links
    total = cx[:, :, None] * cells[2:, 1:-1] + cx_up[:, :, None] * cells[:-2, 1:-1]
    return total + cy[:, :, None] * cells[1:-1, 2:] + cy_left[:, :, None] * cells[1:-1, :-2]


def local_inner(left, right):
    a = left.reshape(-1, left.shape[-1])
    b = right.reshape(-1, right.shape[-1])
    return jnp.einsum("cp,cq->pq", a, b, precision=highest, preferred_element_type=jnp.float32)


def fold(first, second, third):
    size = first.shape[0]
    row = lax.broadcasted_iota(jnp.int32, first.shape, 0)
    col = lax.broadcasted_iota(jnp.int32, first.shape, 1)
    upper = row <= col
    diag = jnp.sum(jnp.where(row == col, third, jnp.float32(0.0)), axis=0)
    spill = jnp.where((row == size - 1) & (col < size - 1), diag[None, :], jnp.float32(0.0))
    spill = jnp.where((row == size - 2) & (col == 0), diag[size - 1], spill)
    return jnp.stack([jnp.where(upper, first, third), jnp.where(upper, second, spill)])


def unfold(packed):
    size = packed.shape[1]
    row = lax.broadcasted_iota(jnp.int32, packed.shape[1:], 0)
    col = lax.broadcasted_iota(jnp.int32, packed.shape[1:], 1)
    upper = row <= col
    strict = row < col
    one, two = packed[0], packed[1]
    first = jnp.where(upper, one, one.T)
    second = jnp.where(upper, two, two.T)
    diag = jnp.concatenate([two[size - 1, : size - 1], two[size - 2, :1]])
    low = jnp.where(strict.T, one, jnp.float32(0.0))
    third = low + low.T + jnp.where(row == col, diag[None, :], jnp.float32(0.0))
    return first, second, third


def _inverse_factor_kernel(gram_ref, out_ref, work_ref):
    size = gram_ref.shape[0]
    work_ref[...] = gram_ref[...]
    rows = lax.broadcasted_iota(jnp.int32, (size, size), 0)
    cols = lax.broadcasted_iota(jnp.int32, (size, size), 1)
    out_ref[...] = jnp.where(rows == cols, jnp.float32(1.0), jnp.float32(0.0))
    lane = lax.broadcasted_iota(jnp.int32, (1, size), 1)
    chunk = 8
    for lo in range(0, size, chunk):
        span = size - lo
        cols_s = lax.broadcasted_iota(jnp.int32, (span, size), 1)
        sub = lo + lax.broadcasted_iota(jnp.int32, (span, 1), 0)

        def step(j, carry, lo=lo, cols_s=cols_s, sub=sub):
            whole = work_ref[lo:, :]
            row = work_ref[pl.ds(j, 1), :]
            column = jnp.sum(jnp.where(cols_s == j, whole, jnp.float32(0.0)), axis=1, keepdims=True)
            pivot = jnp.sum(jnp.where(lane == j, row, jnp.float32(0.0)), axis=1, keepdims=True)
            scale = jnp.float32(1.0) / jnp.sqrt(pivot)
            right = jnp.where(lane >= j, row * scale, jnp.float32(0.0))
            left = jnp.where(sub >= j, column * scale, jnp.float32(0.0))
            head = out_ref[pl.ds(j, 1), :] * scale
            work_ref[lo:, :] = whole - left * right
            below = jnp.where(sub > j, left, jnp.float32(0.0))
            out_ref[lo:, :] = out_ref[lo:, :] - below * head
            out_ref[pl.ds(j, 1), :] = head
            return carry

        lax.fori_loop(lo, min(lo + chunk, size), step, 0)


def inverse_factor(gram):
    size = gram.shape[0]
    return pl.pallas_call(
        _inverse_factor_kernel,
        out_shape=jax.ShapeDtypeStruct((size, size), jnp.float32),
        scratch_shapes=[pltpu.VMEM((size, size), jnp.float32)],
    )(gram)


def per_device(prior_basis, cond_x, cond_y, capacitance, pad_mask, port_nodes):
    rows_dev, cols_dev = cond_x.shape
    width = port_nodes.shape[0]
    count_x = lax.axis_size("gx")
    count_y = lax.axis_size("gy")
    total_rows = rows_dev * count_x
    total_cols = cols_dev * count_y
    nodes = total_rows * total_cols
    bdepth = SWEEPS + 1
    depth = SWEEPS + 2

    coefs = jnp.stack([cond_x, cond_y, capacitance, pad_mask.astype(jnp.float32)])
    basis_e, coefs_e = widen(prior_basis, coefs, "gx", 0, bdepth, depth)
    basis_e, coefs_e = widen(basis_e, coefs_e, "gy", 1, bdepth, depth)

    row_start = lax.axis_index("gx") * rows_dev - depth
    col_start = lax.axis_index("gy") * cols_dev - depth
    shape_e = (rows_dev + 2 * depth, cols_dev + 2 * depth)
    grows = row_start + lax.broadcasted_iota(jnp.int32, shape_e, 0)
    gcols = col_start + lax.broadcasted_iota(jnp.int32, shape_e, 1)
    inside = (grows >= 0) & (grows < total_rows) & (gcols >= 0) & (gcols < total_cols)
    cx_e = jnp.where(grows < total_rows - 1, coefs_e[0], jnp.float32(0.0))
    cy_e = jnp.where(gcols < total_cols - 1, coefs_e[1], jnp.float32(0.0))
    cap_e = coefs_e[2]
    pad_e = coefs_e[3]

    def at(cells, margin):
        return inset(cells, depth - margin)

    def at_basis(margin):
        return inset(basis_e, bdepth - margin)

    top = depth - 1
    cx_t = at(cx_e, top)
    cy_t = at(cy_e, top)
    cx_up_t = cx_e[0:-2, 1:-1]
    cy_left_t = cy_e[1:-1, 0:-2]
    diag_g_t = cx_t + cx_up_t + cy_t + cy_left_t + supply_conductance * at(pad_e, top)
    diag_t = diag_g_t + shift_point * at(cap_e, top)
    diag_t = jnp.where(at(inside, top), diag_t, jnp.float32(1.0))

    def links_at(margin):
        cut = top - margin
        return tuple(inset(c, cut) for c in (cx_t, cy_t, cx_up_t, cy_left_t))

    first = SWEEPS + 1
    node_ids = at(grows, first) * total_cols + at(gcols, first)
    onehot = (node_ids[:, :, None] == port_nodes[None, None, :]) & at(inside, first)[:, :, None]
    rhs = at(cap_e, first)[:, :, None] * at_basis(first) + port_current * onehot.astype(jnp.float32)
    diag_f = inset(diag_t, top - first)[:, :, None]

    field = rhs / diag_f
    for sweep in range(SWEEPS):
        margin = first - 1 - sweep
        field = (inset(rhs, first - margin) + neighbors(field, links_at(margin))) / inset(diag_f, first - margin)

    tile_basis = at_basis(0)
    proj = allsum(local_inner(tile_basis, inset(field, 1)), ("gy", "gx")) / nodes
    cand_1 = field - jnp.einsum("xyk,kp->xyp", at_basis(1), proj, precision=highest)
    cand = inset(cand_1, 1)
    diag_g = inset(diag_g_t, top)[:, :, None]
    g_image = diag_g * cand - neighbors(cand_1, links_at(0))
    c_image = at(cap_e, 0)[:, :, None] * cand
    gram, g_raw, c_raw = local_inner(cand, cand), local_inner(cand, g_image), local_inner(cand, c_image)
    packed = allsum_exchange(fold(gram, g_raw, c_raw), ("gx", "gy")) / nodes
    gram, g_raw, c_raw = unfold(packed)
    inverse = inverse_factor(gram)
    new_basis = jnp.einsum("xyp,qp->xyq", cand, inverse, precision=highest)

    def congruent(block):
        half = jnp.einsum("pk,kq->pq", inverse, block, precision=highest)
        return jnp.einsum("pk,qk->pq", half, inverse, precision=highest)

    reduced_g = congruent(g_raw)
    reduced_c = congruent(c_raw)
    return (new_basis, reduced_g, reduced_c)


def solution(mesh):
    placed = (P("gx", "gy", None), P("gx", "gy"), P("gx", "gy"), P("gx", "gy"), P("gx", "gy"), P())
    return jax.shard_map(
        per_device,
        mesh=mesh,
        in_specs=placed,
        out_specs=(P("gx", "gy", None), P(), P()),
        check_vma=False,
    )
```

```python
import jax
import jax.numpy as jnp
from jax import lax
from jax.experimental import pallas as pl
from jax.experimental.pallas import tpu as pltpu
from jax.sharding import PartitionSpec as P

SWEEPS = 4


shift_point = 0.5
supply_conductance = 4.0
port_current = 8.0
highest = lax.Precision.HIGHEST


def shifted(shard, axis, by):
    devices = lax.axis_size(axis)
    pairs = [(i, i + by) for i in range(devices) if 0 <= i + by < devices]
    return lax.ppermute(shard, axis, pairs)


def allsum(value, axes):
    for axis in axes:
        count = lax.axis_size(axis)
        if count & (count - 1):
            value = lax.psum(value, axis)
            continue
        step = 1
        while step < count:
            other = lax.ppermute(value, axis, [(i, i ^ step) for i in range(count)])
            value = value + other
            step *= 2
    return value


def allsum_exchange(value, axes):
    count = 1
    for axis in axes:
        count *= lax.axis_size(axis)
    flat = value.reshape(-1, value.shape[-1])
    if flat.shape[0] % count:
        return allsum(value, axes)
    parts = flat.reshape(count, -1, flat.shape[-1])
    got = lax.all_to_all(parts, axes, 0, 0, tiled=False)
    total = got[0]
    for k in range(1, count):
        total = total + got[k]
    spread = jnp.broadcast_to(total[None], (count,) + total.shape)
    back = lax.all_to_all(spread, axes, 0, 0, tiled=False)
    return back.reshape(value.shape)


def pack(block, coefs):
    width = block.shape[-1]
    flat = coefs.reshape(-1)
    spare = (-flat.shape[0]) % width
    flat = jnp.pad(flat, (0, spare))
    return jnp.concatenate([block.reshape(-1, width), flat.reshape(-1, width)], axis=0)


def unpack(packed, block_shape, coef_shape):
    count = block_shape[0] * block_shape[1]
    block = packed[:count].reshape(block_shape)
    size = coef_shape[0] * coef_shape[1] * coef_shape[2]
    coefs = packed[count:].reshape(-1)[:size].reshape(coef_shape)
    return block, coefs


def widen(block, coefs, axis, dim, depth, cdepth):
    head = lax.slice_in_dim(block, 0, depth, axis=dim)
    tail = lax.slice_in_dim(block, block.shape[dim] - depth, block.shape[dim], axis=dim)
    chead = lax.slice_in_dim(coefs, 0, cdepth, axis=dim + 1)
    ctail = lax.slice_in_dim(coefs, coefs.shape[dim + 1] - cdepth, coefs.shape[dim + 1], axis=dim + 1)
    before = shifted(pack(tail, ctail), axis, 1)
    after = shifted(pack(head, chead), axis, -1)
    before_b, before_c = unpack(before, head.shape, chead.shape)
    after_b, after_c = unpack(after, head.shape, chead.shape)
    block = jnp.concatenate([before_b, block, after_b], axis=dim)
    coefs = jnp.concatenate([before_c, coefs, after_c], axis=dim + 1)
    return block, coefs


def inset(cells, by):
    if by == 0:
        return cells
    return cells[by:cells.shape[0] - by, by:cells.shape[1] - by]


def neighbors(cells, links):
    cx, cy, cx_up, cy_left = links
    total = cx[:, :, None] * cells[2:, 1:-1] + cx_up[:, :, None] * cells[:-2, 1:-1]
    return total + cy[:, :, None] * cells[1:-1, 2:] + cy_left[:, :, None] * cells[1:-1, :-2]


def local_inner(left, right):
    a = left.reshape(-1, left.shape[-1])
    b = right.reshape(-1, right.shape[-1])
    return jnp.einsum("cp,cq->pq", a, b, precision=highest, preferred_element_type=jnp.float32)


def fold(first, second, third):
    size = first.shape[0]
    row = lax.broadcasted_iota(jnp.int32, first.shape, 0)
    col = lax.broadcasted_iota(jnp.int32, first.shape, 1)
    upper = row <= col
    diag = jnp.sum(jnp.where(row == col, third, jnp.float32(0.0)), axis=0)
    spill = jnp.where((row == size - 1) & (col < size - 1), diag[None, :], jnp.float32(0.0))
    spill = jnp.where((row == size - 2) & (col == 0), diag[size - 1], spill)
    return jnp.stack([jnp.where(upper, first, third), jnp.where(upper, second, spill)])


def unfold(packed):
    size = packed.shape[1]
    row = lax.broadcasted_iota(jnp.int32, packed.shape[1:], 0)
    col = lax.broadcasted_iota(jnp.int32, packed.shape[1:], 1)
    upper = row <= col
    strict = row < col
    one, two = packed[0], packed[1]
    first = jnp.where(upper, one, one.T)
    second = jnp.where(upper, two, two.T)
    diag = jnp.concatenate([two[size - 1, : size - 1], two[size - 2, :1]])
    low = jnp.where(strict.T, one, jnp.float32(0.0))
    third = low + low.T + jnp.where(row == col, diag[None, :], jnp.float32(0.0))
    return first, second, third


def _inverse_factor_kernel(gram_ref, out_ref, work_ref):
    size = gram_ref.shape[0]
    work_ref[...] = gram_ref[...]
    rows = lax.broadcasted_iota(jnp.int32, (size, size), 0)
    cols = lax.broadcasted_iota(jnp.int32, (size, size), 1)
    out_ref[...] = jnp.where(rows == cols, jnp.float32(1.0), jnp.float32(0.0))
    lane = lax.broadcasted_iota(jnp.int32, (1, size), 1)
    chunk = 8
    for lo in range(0, size, chunk):
        span = size - lo
        cols_s = lax.broadcasted_iota(jnp.int32, (span, size), 1)
        sub = lo + lax.broadcasted_iota(jnp.int32, (span, 1), 0)

        def step(j, carry, lo=lo, cols_s=cols_s, sub=sub):
            whole = work_ref[lo:, :]
            row = work_ref[pl.ds(j, 1), :]
            column = jnp.sum(jnp.where(cols_s == j, whole, jnp.float32(0.0)), axis=1, keepdims=True)
            pivot = jnp.sum(jnp.where(lane == j, row, jnp.float32(0.0)), axis=1, keepdims=True)
            scale = lax.rsqrt(pivot)
            right = jnp.where(lane >= j, row * scale, jnp.float32(0.0))
            left = jnp.where(sub >= j, column * scale, jnp.float32(0.0))
            head = out_ref[pl.ds(j, 1), :] * scale
            work_ref[lo:, :] = whole - left * right
            below = jnp.where(sub > j, left, jnp.float32(0.0))
            out_ref[lo:, :] = out_ref[lo:, :] - below * head
            out_ref[pl.ds(j, 1), :] = head
            return carry

        lax.fori_loop(lo, min(lo + chunk, size), step, 0)


def inverse_factor(gram):
    size = gram.shape[0]
    return pl.pallas_call(
        _inverse_factor_kernel,
        out_shape=jax.ShapeDtypeStruct((size, size), jnp.float32),
        scratch_shapes=[pltpu.VMEM((size, size), jnp.float32)],
    )(gram)


def per_device(prior_basis, cond_x, cond_y, capacitance, pad_mask, port_nodes):
    rows_dev, cols_dev = cond_x.shape
    width = port_nodes.shape[0]
    count_x = lax.axis_size("gx")
    count_y = lax.axis_size("gy")
    total_rows = rows_dev * count_x
    total_cols = cols_dev * count_y
    nodes = total_rows * total_cols
    bdepth = SWEEPS + 1
    depth = SWEEPS + 2

    coefs = jnp.stack([cond_x, cond_y, capacitance, pad_mask.astype(jnp.float32)])
    basis_e, coefs_e = widen(prior_basis, coefs, "gx", 0, bdepth, depth)
    basis_e, coefs_e = widen(basis_e, coefs_e, "gy", 1, bdepth, depth)

    row_start = lax.axis_index("gx") * rows_dev - depth
    col_start = lax.axis_index("gy") * cols_dev - depth
    shape_e = (rows_dev + 2 * depth, cols_dev + 2 * depth)
    grows = row_start + lax.broadcasted_iota(jnp.int32, shape_e, 0)
    gcols = col_start + lax.broadcasted_iota(jnp.int32, shape_e, 1)
    inside = (grows >= 0) & (grows < total_rows) & (gcols >= 0) & (gcols < total_cols)
    cx_e = jnp.where(grows < total_rows - 1, coefs_e[0], jnp.float32(0.0))
    cy_e = jnp.where(gcols < total_cols - 1, coefs_e[1], jnp.float32(0.0))
    cap_e = coefs_e[2]
    pad_e = coefs_e[3]

    def at(cells, margin):
        return inset(cells, depth - margin)

    def at_basis(margin):
        return inset(basis_e, bdepth - margin)

    top = depth - 1
    cx_t = at(cx_e, top)
    cy_t = at(cy_e, top)
    cx_up_t = cx_e[0:-2, 1:-1]
    cy_left_t = cy_e[1:-1, 0:-2]
    diag_g_t = cx_t + cx_up_t + cy_t + cy_left_t + supply_conductance * at(pad_e, top)
    diag_t = diag_g_t + shift_point * at(cap_e, top)
    diag_t = jnp.where(at(inside, top), diag_t, jnp.float32(1.0))

    def links_at(margin):
        cut = top - margin
        return tuple(inset(c, cut) for c in (cx_t, cy_t, cx_up_t, cy_left_t))

    first = SWEEPS + 1
    node_ids = at(grows, first) * total_cols + at(gcols, first)
    onehot = (node_ids[:, :, None] == port_nodes[None, None, :]) & at(inside, first)[:, :, None]
    rhs = at(cap_e, first)[:, :, None] * at_basis(first) + port_current * onehot.astype(jnp.float32)
    diag_f = inset(diag_t, top - first)[:, :, None]

    field = rhs / diag_f
    for sweep in range(SWEEPS):
        margin = first - 1 - sweep
        field = (inset(rhs, first - margin) + neighbors(field, links_at(margin))) / inset(diag_f, first - margin)

    tile_basis = at_basis(0)
    proj = allsum(local_inner(tile_basis, inset(field, 1)), ("gy", "gx")) / nodes
    cand_1 = field - jnp.einsum("xyk,kp->xyp", at_basis(1), proj, precision=highest)
    cand = inset(cand_1, 1)
    diag_g = inset(diag_g_t, top)[:, :, None]
    g_image = diag_g * cand - neighbors(cand_1, links_at(0))
    c_image = at(cap_e, 0)[:, :, None] * cand
    gram, g_raw, c_raw = local_inner(cand, cand), local_inner(cand, g_image), local_inner(cand, c_image)
    packed = allsum_exchange(fold(gram, g_raw, c_raw), ("gx", "gy")) / nodes
    gram, g_raw, c_raw = unfold(packed)
    inverse = inverse_factor(gram)
    new_basis = jnp.einsum("xyp,qp->xyq", cand, inverse, precision=highest)
    half = jnp.einsum("pk,skq->spq", inverse, jnp.stack([g_raw, c_raw]), precision=highest)
    both = jnp.einsum("spk,qk->spq", half, inverse, precision=highest)
    reduced_g = both[0]
    reduced_c = both[1]
    return (new_basis, reduced_g, reduced_c)


def solution(mesh):
    placed = (P("gx", "gy", None), P("gx", "gy"), P("gx", "gy"), P("gx", "gy"), P("gx", "gy"), P())
    return jax.shard_map(
        per_device,
        mesh=mesh,
        in_specs=placed,
        out_specs=(P("gx", "gy", None), P(), P()),
        check_vma=False,
    )
```

```python
import jax
import jax.numpy as jnp
from jax import lax
from jax.experimental import pallas as pl
from jax.experimental.pallas import tpu as pltpu
from jax.sharding import PartitionSpec as P

SWEEPS = 4


shift_point = 0.5
supply_conductance = 4.0
port_current = 8.0
highest = lax.Precision.HIGHEST


def shifted(shard, axis, by):
    devices = lax.axis_size(axis)
    pairs = [(i, i + by) for i in range(devices) if 0 <= i + by < devices]
    return lax.ppermute(shard, axis, pairs)


def allsum(value, axes):
    for axis in axes:
        count = lax.axis_size(axis)
        if count & (count - 1):
            value = lax.psum(value, axis)
            continue
        step = 1
        while step < count:
            other = lax.ppermute(value, axis, [(i, i ^ step) for i in range(count)])
            value = value + other
            step *= 2
    return value


def allsum_exchange(value, axes):
    count = 1
    for axis in axes:
        count *= lax.axis_size(axis)
    flat = value.reshape(-1, value.shape[-1])
    if flat.shape[0] % count:
        return allsum(value, axes)
    parts = flat.reshape(count, -1, flat.shape[-1])
    got = lax.all_to_all(parts, axes, 0, 0, tiled=False)
    total = got[0]
    for k in range(1, count):
        total = total + got[k]
    spread = jnp.broadcast_to(total[None], (count,) + total.shape)
    back = lax.all_to_all(spread, axes, 0, 0, tiled=False)
    return back.reshape(value.shape)


def allsum_quad(value, axes):
    for axis in axes:
        count = lax.axis_size(axis)
        if count & (count - 1):
            value = lax.psum(value, axis)
            continue
        index = lax.axis_index(axis)
        step = 1
        while step < count:
            if step * 4 <= count:
                own = (index // step) % 4
                got = [value] + [
                    lax.ppermute(value, axis, [(i, i ^ (k * step)) for i in range(count)])
                    for k in (1, 2, 3)
                ]
                stack = jnp.stack(got)
                total = lax.dynamic_index_in_dim(stack, own, keepdims=False)
                for member in (1, 2, 3):
                    total = total + lax.dynamic_index_in_dim(stack, own ^ member, keepdims=False)
                value = total
                step *= 4
            else:
                other = lax.ppermute(value, axis, [(i, i ^ step) for i in range(count)])
                value = value + other
                step *= 2
    return value


def pack(block, coefs):
    width = block.shape[-1]
    flat = coefs.reshape(-1)
    spare = (-flat.shape[0]) % width
    flat = jnp.pad(flat, (0, spare))
    return jnp.concatenate([block.reshape(-1, width), flat.reshape(-1, width)], axis=0)


def unpack(packed, block_shape, coef_shape):
    count = block_shape[0] * block_shape[1]
    block = packed[:count].reshape(block_shape)
    size = coef_shape[0] * coef_shape[1] * coef_shape[2]
    coefs = packed[count:].reshape(-1)[:size].reshape(coef_shape)
    return block, coefs


def widen(block, coefs, axis, dim, depth, cdepth):
    head = lax.slice_in_dim(block, 0, depth, axis=dim)
    tail = lax.slice_in_dim(block, block.shape[dim] - depth, block.shape[dim], axis=dim)
    chead = lax.slice_in_dim(coefs, 0, cdepth, axis=dim + 1)
    ctail = lax.slice_in_dim(coefs, coefs.shape[dim + 1] - cdepth, coefs.shape[dim + 1], axis=dim + 1)
    before = shifted(pack(tail, ctail), axis, 1)
    after = shifted(pack(head, chead), axis, -1)
    before_b, before_c = unpack(before, head.shape, chead.shape)
    after_b, after_c = unpack(after, head.shape, chead.shape)
    block = jnp.concatenate([before_b, block, after_b], axis=dim)
    coefs = jnp.concatenate([before_c, coefs, after_c], axis=dim + 1)
    return block, coefs


def inset(cells, by):
    if by == 0:
        return cells
    return cells[by:cells.shape[0] - by, by:cells.shape[1] - by]


def neighbors(cells, links):
    cx, cy, cx_up, cy_left = links
    total = cx[:, :, None] * cells[2:, 1:-1] + cx_up[:, :, None] * cells[:-2, 1:-1]
    return total + cy[:, :, None] * cells[1:-1, 2:] + cy_left[:, :, None] * cells[1:-1, :-2]


def local_inner(left, right):
    a = left.reshape(-1, left.shape[-1])
    b = right.reshape(-1, right.shape[-1])
    return jnp.einsum("cp,cq->pq", a, b, precision=highest, preferred_element_type=jnp.float32)


def fold(first, second, third):
    size = first.shape[0]
    row = lax.broadcasted_iota(jnp.int32, first.shape, 0)
    col = lax.broadcasted_iota(jnp.int32, first.shape, 1)
    upper = row <= col
    diag = jnp.sum(jnp.where(row == col, third, jnp.float32(0.0)), axis=0)
    spill = jnp.where((row == size - 1) & (col < size - 1), diag[None, :], jnp.float32(0.0))
    spill = jnp.where((row == size - 2) & (col == 0), diag[size - 1], spill)
    return jnp.stack([jnp.where(upper, first, third), jnp.where(upper, second, spill)])


def unfold(packed):
    size = packed.shape[1]
    row = lax.broadcasted_iota(jnp.int32, packed.shape[1:], 0)
    col = lax.broadcasted_iota(jnp.int32, packed.shape[1:], 1)
    upper = row <= col
    strict = row < col
    one, two = packed[0], packed[1]
    first = jnp.where(upper, one, one.T)
    second = jnp.where(upper, two, two.T)
    diag = jnp.concatenate([two[size - 1, : size - 1], two[size - 2, :1]])
    low = jnp.where(strict.T, one, jnp.float32(0.0))
    third = low + low.T + jnp.where(row == col, diag[None, :], jnp.float32(0.0))
    return first, second, third


def _inverse_factor_kernel(gram_ref, out_ref, work_ref):
    size = gram_ref.shape[0]
    work_ref[...] = gram_ref[...]
    rows = lax.broadcasted_iota(jnp.int32, (size, size), 0)
    cols = lax.broadcasted_iota(jnp.int32, (size, size), 1)
    out_ref[...] = jnp.where(rows == cols, jnp.float32(1.0), jnp.float32(0.0))
    lane = lax.broadcasted_iota(jnp.int32, (1, size), 1)
    chunk = 8
    for lo in range(0, size, chunk):
        span = size - lo
        cols_s = lax.broadcasted_iota(jnp.int32, (span, size), 1)
        sub = lo + lax.broadcasted_iota(jnp.int32, (span, 1), 0)

        def step(j, carry, lo=lo, cols_s=cols_s, sub=sub):
            whole = work_ref[lo:, :]
            row = work_ref[pl.ds(j, 1), :]
            column = jnp.sum(jnp.where(cols_s == j, whole, jnp.float32(0.0)), axis=1, keepdims=True)
            pivot = jnp.sum(jnp.where(lane == j, row, jnp.float32(0.0)), axis=1, keepdims=True)
            scale = lax.rsqrt(pivot)
            right = jnp.where(lane >= j, row * scale, jnp.float32(0.0))
            left = jnp.where(sub >= j, column * scale, jnp.float32(0.0))
            head = out_ref[pl.ds(j, 1), :] * scale
            work_ref[lo:, :] = whole - left * right
            below = jnp.where(sub > j, left, jnp.float32(0.0))
            out_ref[lo:, :] = out_ref[lo:, :] - below * head
            out_ref[pl.ds(j, 1), :] = head
            return carry

        lax.fori_loop(lo, min(lo + chunk, size), step, 0)


def inverse_factor(gram):
    size = gram.shape[0]
    return pl.pallas_call(
        _inverse_factor_kernel,
        out_shape=jax.ShapeDtypeStruct((size, size), jnp.float32),
        scratch_shapes=[pltpu.VMEM((size, size), jnp.float32)],
    )(gram)


def per_device(prior_basis, cond_x, cond_y, capacitance, pad_mask, port_nodes):
    rows_dev, cols_dev = cond_x.shape
    width = port_nodes.shape[0]
    count_x = lax.axis_size("gx")
    count_y = lax.axis_size("gy")
    total_rows = rows_dev * count_x
    total_cols = cols_dev * count_y
    nodes = total_rows * total_cols
    bdepth = SWEEPS + 1
    depth = SWEEPS + 2

    coefs = jnp.stack([cond_x, cond_y, capacitance, pad_mask.astype(jnp.float32)])
    basis_e, coefs_e = widen(prior_basis, coefs, "gx", 0, bdepth, depth)
    basis_e, coefs_e = widen(basis_e, coefs_e, "gy", 1, bdepth, depth)

    row_start = lax.axis_index("gx") * rows_dev - depth
    col_start = lax.axis_index("gy") * cols_dev - depth
    shape_e = (rows_dev + 2 * depth, cols_dev + 2 * depth)
    grows = row_start + lax.broadcasted_iota(jnp.int32, shape_e, 0)
    gcols = col_start + lax.broadcasted_iota(jnp.int32, shape_e, 1)
    inside = (grows >= 0) & (grows < total_rows) & (gcols >= 0) & (gcols < total_cols)
    cx_e = jnp.where(grows < total_rows - 1, coefs_e[0], jnp.float32(0.0))
    cy_e = jnp.where(gcols < total_cols - 1, coefs_e[1], jnp.float32(0.0))
    cap_e = coefs_e[2]
    pad_e = coefs_e[3]

    def at(cells, margin):
        return inset(cells, depth - margin)

    def at_basis(margin):
        return inset(basis_e, bdepth - margin)

    top = depth - 1
    cx_t = at(cx_e, top)
    cy_t = at(cy_e, top)
    cx_up_t = cx_e[0:-2, 1:-1]
    cy_left_t = cy_e[1:-1, 0:-2]
    diag_g_t = cx_t + cx_up_t + cy_t + cy_left_t + supply_conductance * at(pad_e, top)
    diag_t = diag_g_t + shift_point * at(cap_e, top)
    diag_t = jnp.where(at(inside, top), diag_t, jnp.float32(1.0))

    def links_at(margin):
        cut = top - margin
        return tuple(inset(c, cut) for c in (cx_t, cy_t, cx_up_t, cy_left_t))

    first = SWEEPS + 1
    node_ids = at(grows, first) * total_cols + at(gcols, first)
    onehot = (node_ids[:, :, None] == port_nodes[None, None, :]) & at(inside, first)[:, :, None]
    rhs = at(cap_e, first)[:, :, None] * at_basis(first) + port_current * onehot.astype(jnp.float32)
    diag_f = inset(diag_t, top - first)[:, :, None]

    field = rhs / diag_f
    for sweep in range(SWEEPS):
        margin = first - 1 - sweep
        field = (inset(rhs, first - margin) + neighbors(field, links_at(margin))) / inset(diag_f, first - margin)

    tile_basis = at_basis(0)
    proj = allsum_quad(local_inner(tile_basis, inset(field, 1)), ("gy", "gx")) / nodes
    cand_1 = field - jnp.einsum("xyk,kp->xyp", at_basis(1), proj, precision=highest)
    cand = inset(cand_1, 1)
    diag_g = inset(diag_g_t, top)[:, :, None]
    g_image = diag_g * cand - neighbors(cand_1, links_at(0))
    c_image = at(cap_e, 0)[:, :, None] * cand
    gram, g_raw, c_raw = local_inner(cand, cand), local_inner(cand, g_image), local_inner(cand, c_image)
    packed = allsum_exchange(fold(gram, g_raw, c_raw), ("gx", "gy")) / nodes
    gram, g_raw, c_raw = unfold(packed)
    inverse = inverse_factor(gram)
    new_basis = jnp.einsum("xyp,qp->xyq", cand, inverse, precision=highest)
    half = jnp.einsum("pk,skq->spq", inverse, jnp.stack([g_raw, c_raw]), precision=highest)
    both = jnp.einsum("spk,qk->spq", half, inverse, precision=highest)
    reduced_g = both[0]
    reduced_c = both[1]
    return (new_basis, reduced_g, reduced_c)


def solution(mesh):
    placed = (P("gx", "gy", None), P("gx", "gy"), P("gx", "gy"), P("gx", "gy"), P("gx", "gy"), P())
    return jax.shard_map(
        per_device,
        mesh=mesh,
        in_specs=placed,
        out_specs=(P("gx", "gy", None), P(), P()),
        check_vma=False,
    )
```

```python
import jax
import jax.numpy as jnp
from jax import lax
from jax.experimental import pallas as pl
from jax.experimental.pallas import tpu as pltpu
from jax.sharding import PartitionSpec as P

SWEEPS = 4


shift_point = 0.5
supply_conductance = 4.0
port_current = 8.0
highest = lax.Precision.HIGHEST


def shifted(shard, axis, by):
    devices = lax.axis_size(axis)
    pairs = [(i, i + by) for i in range(devices) if 0 <= i + by < devices]
    return lax.ppermute(shard, axis, pairs)


def allsum(value, axes):
    for axis in axes:
        count = lax.axis_size(axis)
        if count & (count - 1):
            value = lax.psum(value, axis)
            continue
        step = 1
        while step < count:
            other = lax.ppermute(value, axis, [(i, i ^ step) for i in range(count)])
            value = value + other
            step *= 2
    return value


def allsum_exchange(value, axes):
    count = 1
    for axis in axes:
        count *= lax.axis_size(axis)
    flat = value.reshape(-1, value.shape[-1])
    if flat.shape[0] % count:
        return allsum(value, axes)
    parts = flat.reshape(count, -1, flat.shape[-1])
    got = lax.all_to_all(parts, axes, 0, 0, tiled=False)
    total = got[0]
    for k in range(1, count):
        total = total + got[k]
    spread = jnp.broadcast_to(total[None], (count,) + total.shape)
    back = lax.all_to_all(spread, axes, 0, 0, tiled=False)
    return back.reshape(value.shape)


def allsum_quad(value, axes):
    for axis in axes:
        count = lax.axis_size(axis)
        if count & (count - 1):
            value = lax.psum(value, axis)
            continue
        index = lax.axis_index(axis)
        step = 1
        while step < count:
            if step * 4 <= count:
                own = (index // step) % 4
                got = [value] + [
                    lax.ppermute(value, axis, [(i, i ^ (k * step)) for i in range(count)])
                    for k in (1, 2, 3)
                ]
                stack = jnp.stack(got)
                total = lax.dynamic_index_in_dim(stack, own, keepdims=False)
                for member in (1, 2, 3):
                    total = total + lax.dynamic_index_in_dim(stack, own ^ member, keepdims=False)
                value = total
                step *= 4
            else:
                other = lax.ppermute(value, axis, [(i, i ^ step) for i in range(count)])
                value = value + other
                step *= 2
    return value


def pack(block, coefs):
    width = block.shape[-1]
    flat = coefs.reshape(-1)
    spare = (-flat.shape[0]) % width
    flat = jnp.pad(flat, (0, spare))
    return jnp.concatenate([block.reshape(-1, width), flat.reshape(-1, width)], axis=0)


def unpack(packed, block_shape, coef_shape):
    count = block_shape[0] * block_shape[1]
    block = packed[:count].reshape(block_shape)
    size = coef_shape[0] * coef_shape[1] * coef_shape[2]
    coefs = packed[count:].reshape(-1)[:size].reshape(coef_shape)
    return block, coefs


def widen(block, coefs, axis, dim, depth, cdepth):
    head = lax.slice_in_dim(block, 0, depth, axis=dim)
    tail = lax.slice_in_dim(block, block.shape[dim] - depth, block.shape[dim], axis=dim)
    chead = lax.slice_in_dim(coefs, 0, cdepth, axis=dim + 1)
    ctail = lax.slice_in_dim(coefs, coefs.shape[dim + 1] - cdepth, coefs.shape[dim + 1], axis=dim + 1)
    before = shifted(pack(tail, ctail), axis, 1)
    after = shifted(pack(head, chead), axis, -1)
    before_b, before_c = unpack(before, head.shape, chead.shape)
    after_b, after_c = unpack(after, head.shape, chead.shape)
    block = jnp.concatenate([before_b, block, after_b], axis=dim)
    coefs = jnp.concatenate([before_c, coefs, after_c], axis=dim + 1)
    return block, coefs


def inset(cells, by):
    if by == 0:
        return cells
    return cells[by:cells.shape[0] - by, by:cells.shape[1] - by]


def neighbors(cells, links):
    cx, cy, cx_up, cy_left = links
    total = cx[:, :, None] * cells[2:, 1:-1] + cx_up[:, :, None] * cells[:-2, 1:-1]
    return total + cy[:, :, None] * cells[1:-1, 2:] + cy_left[:, :, None] * cells[1:-1, :-2]


def local_inner(left, right):
    a = left.reshape(-1, left.shape[-1])
    b = right.reshape(-1, right.shape[-1])
    return jnp.einsum("cp,cq->pq", a, b, precision=highest, preferred_element_type=jnp.float32)


def fold(first, second, third):
    size = first.shape[0]
    row = lax.broadcasted_iota(jnp.int32, first.shape, 0)
    col = lax.broadcasted_iota(jnp.int32, first.shape, 1)
    upper = row <= col
    diag = jnp.sum(jnp.where(row == col, third, jnp.float32(0.0)), axis=0)
    spill = jnp.where((row == size - 1) & (col < size - 1), diag[None, :], jnp.float32(0.0))
    spill = jnp.where((row == size - 2) & (col == 0), diag[size - 1], spill)
    return jnp.stack([jnp.where(upper, first, third), jnp.where(upper, second, spill)])


def unfold(packed):
    size = packed.shape[1]
    row = lax.broadcasted_iota(jnp.int32, packed.shape[1:], 0)
    col = lax.broadcasted_iota(jnp.int32, packed.shape[1:], 1)
    upper = row <= col
    strict = row < col
    one, two = packed[0], packed[1]
    first = jnp.where(upper, one, one.T)
    second = jnp.where(upper, two, two.T)
    diag = jnp.concatenate([two[size - 1, : size - 1], two[size - 2, :1]])
    low = jnp.where(strict.T, one, jnp.float32(0.0))
    third = low + low.T + jnp.where(row == col, diag[None, :], jnp.float32(0.0))
    return first, second, third


def _factor_kernel(gram_ref, blocks_ref, cand_ref, basis_ref, reduced_ref, work_ref, inv_ref):
    size = gram_ref.shape[0]
    work_ref[...] = gram_ref[...]
    rows = lax.broadcasted_iota(jnp.int32, (size, size), 0)
    cols = lax.broadcasted_iota(jnp.int32, (size, size), 1)
    inv_ref[...] = jnp.where(rows == cols, jnp.float32(1.0), jnp.float32(0.0))
    lane = lax.broadcasted_iota(jnp.int32, (1, size), 1)
    chunk = 8
    for lo in range(0, size, chunk):
        span = size - lo
        cols_s = lax.broadcasted_iota(jnp.int32, (span, size), 1)
        sub = lo + lax.broadcasted_iota(jnp.int32, (span, 1), 0)

        def step(j, carry, lo=lo, cols_s=cols_s, sub=sub):
            whole = work_ref[lo:, :]
            row = work_ref[pl.ds(j, 1), :]
            column = jnp.sum(jnp.where(cols_s == j, whole, jnp.float32(0.0)), axis=1, keepdims=True)
            pivot = jnp.sum(jnp.where(lane == j, row, jnp.float32(0.0)), axis=1, keepdims=True)
            scale = lax.rsqrt(pivot)
            right = jnp.where(lane >= j, row * scale, jnp.float32(0.0))
            left = jnp.where(sub >= j, column * scale, jnp.float32(0.0))
            head = inv_ref[pl.ds(j, 1), :] * scale
            work_ref[lo:, :] = whole - left * right
            below = jnp.where(sub > j, left, jnp.float32(0.0))
            inv_ref[lo:, :] = inv_ref[lo:, :] - below * head
            inv_ref[pl.ds(j, 1), :] = head
            return carry

        lax.fori_loop(lo, min(lo + chunk, size), step, 0)

    inverse = inv_ref[...]
    by_rows = (((1,), (1,)), ((), ()))
    basis_ref[...] = lax.dot_general(
        cand_ref[...], inverse, by_rows, precision=highest, preferred_element_type=jnp.float32
    )
    for index in range(blocks_ref.shape[0]):
        half = jnp.dot(inverse, blocks_ref[index], precision=highest, preferred_element_type=jnp.float32)
        reduced_ref[index] = lax.dot_general(
            half, inverse, by_rows, precision=highest, preferred_element_type=jnp.float32
        )


def orthonormalize(gram, blocks, cand):
    size = gram.shape[0]
    return pl.pallas_call(
        _factor_kernel,
        out_shape=(
            jax.ShapeDtypeStruct(cand.shape, jnp.float32),
            jax.ShapeDtypeStruct(blocks.shape, jnp.float32),
        ),
        scratch_shapes=[pltpu.VMEM((size, size), jnp.float32), pltpu.VMEM((size, size), jnp.float32)],
    )(gram, blocks, cand)


def per_device(prior_basis, cond_x, cond_y, capacitance, pad_mask, port_nodes):
    rows_dev, cols_dev = cond_x.shape
    width = port_nodes.shape[0]
    count_x = lax.axis_size("gx")
    count_y = lax.axis_size("gy")
    total_rows = rows_dev * count_x
    total_cols = cols_dev * count_y
    nodes = total_rows * total_cols
    bdepth = SWEEPS + 1
    depth = SWEEPS + 2

    coefs = jnp.stack([cond_x, cond_y, capacitance, pad_mask.astype(jnp.float32)])
    basis_e, coefs_e = widen(prior_basis, coefs, "gx", 0, bdepth, depth)
    basis_e, coefs_e = widen(basis_e, coefs_e, "gy", 1, bdepth, depth)

    row_start = lax.axis_index("gx") * rows_dev - depth
    col_start = lax.axis_index("gy") * cols_dev - depth
    shape_e = (rows_dev + 2 * depth, cols_dev + 2 * depth)
    grows = row_start + lax.broadcasted_iota(jnp.int32, shape_e, 0)
    gcols = col_start + lax.broadcasted_iota(jnp.int32, shape_e, 1)
    inside = (grows >= 0) & (grows < total_rows) & (gcols >= 0) & (gcols < total_cols)
    cx_e = jnp.where(grows < total_rows - 1, coefs_e[0], jnp.float32(0.0))
    cy_e = jnp.where(gcols < total_cols - 1, coefs_e[1], jnp.float32(0.0))
    cap_e = coefs_e[2]
    pad_e = coefs_e[3]

    def at(cells, margin):
        return inset(cells, depth - margin)

    def at_basis(margin):
        return inset(basis_e, bdepth - margin)

    top = depth - 1
    cx_t = at(cx_e, top)
    cy_t = at(cy_e, top)
    cx_up_t = cx_e[0:-2, 1:-1]
    cy_left_t = cy_e[1:-1, 0:-2]
    diag_g_t = cx_t + cx_up_t + cy_t + cy_left_t + supply_conductance * at(pad_e, top)
    diag_t = diag_g_t + shift_point * at(cap_e, top)
    diag_t = jnp.where(at(inside, top), diag_t, jnp.float32(1.0))

    def links_at(margin):
        cut = top - margin
        return tuple(inset(c, cut) for c in (cx_t, cy_t, cx_up_t, cy_left_t))

    first = SWEEPS + 1
    node_ids = at(grows, first) * total_cols + at(gcols, first)
    onehot = (node_ids[:, :, None] == port_nodes[None, None, :]) & at(inside, first)[:, :, None]
    rhs = at(cap_e, first)[:, :, None] * at_basis(first) + port_current * onehot.astype(jnp.float32)
    diag_f = inset(diag_t, top - first)[:, :, None]

    field = rhs / diag_f
    for sweep in range(SWEEPS):
        margin = first - 1 - sweep
        field = (inset(rhs, first - margin) + neighbors(field, links_at(margin))) / inset(diag_f, first - margin)

    tile_basis = at_basis(0)
    proj = allsum_quad(local_inner(tile_basis, inset(field, 1)), ("gy", "gx")) / nodes
    cand_1 = field - jnp.einsum("xyk,kp->xyp", at_basis(1), proj, precision=highest)
    cand = inset(cand_1, 1)
    diag_g = inset(diag_g_t, top)[:, :, None]
    g_image = diag_g * cand - neighbors(cand_1, links_at(0))
    c_image = at(cap_e, 0)[:, :, None] * cand
    gram, g_raw, c_raw = local_inner(cand, cand), local_inner(cand, g_image), local_inner(cand, c_image)
    packed = allsum_exchange(fold(gram, g_raw, c_raw), ("gx", "gy")) / nodes
    gram, g_raw, c_raw = unfold(packed)
    basis_flat, reduced = orthonormalize(gram, jnp.stack([g_raw, c_raw]), cand.reshape(-1, width))
    new_basis = basis_flat.reshape(cand.shape)
    reduced_g = reduced[0]
    reduced_c = reduced[1]
    return (new_basis, reduced_g, reduced_c)


def solution(mesh):
    placed = (P("gx", "gy", None), P("gx", "gy"), P("gx", "gy"), P("gx", "gy"), P("gx", "gy"), P())
    return jax.shard_map(
        per_device,
        mesh=mesh,
        in_specs=placed,
        out_specs=(P("gx", "gy", None), P(), P()),
        check_vma=False,
    )
```

```python
import jax
import jax.numpy as jnp
from jax import lax
from jax.experimental import pallas as pl
from jax.experimental.pallas import tpu as pltpu
from jax.sharding import PartitionSpec as P

SWEEPS = 4


shift_point = 0.5
supply_conductance = 4.0
port_current = 8.0
highest = lax.Precision.HIGHEST


def shifted(shard, axis, by):
    devices = lax.axis_size(axis)
    pairs = [(i, i + by) for i in range(devices) if 0 <= i + by < devices]
    return lax.ppermute(shard, axis, pairs)


def allsum(value, axes):
    for axis in axes:
        count = lax.axis_size(axis)
        if count & (count - 1):
            value = lax.psum(value, axis)
            continue
        step = 1
        while step < count:
            other = lax.ppermute(value, axis, [(i, i ^ step) for i in range(count)])
            value = value + other
            step *= 2
    return value


def allsum_exchange(value, axes):
    count = 1
    for axis in axes:
        count *= lax.axis_size(axis)
    flat = value.reshape(-1, value.shape[-1])
    if flat.shape[0] % count:
        return allsum(value, axes)
    parts = flat.reshape(count, -1, flat.shape[-1])
    got = lax.all_to_all(parts, axes, 0, 0, tiled=False)
    total = got[0]
    for k in range(1, count):
        total = total + got[k]
    spread = jnp.broadcast_to(total[None], (count,) + total.shape)
    back = lax.all_to_all(spread, axes, 0, 0, tiled=False)
    return back.reshape(value.shape)


def allsum_quad(value, axes):
    for axis in axes:
        count = lax.axis_size(axis)
        if count & (count - 1):
            value = lax.psum(value, axis)
            continue
        index = lax.axis_index(axis)
        step = 1
        while step < count:
            if step * 4 <= count:
                own = (index // step) % 4
                got = [value] + [
                    lax.ppermute(value, axis, [(i, i ^ (k * step)) for i in range(count)])
                    for k in (1, 2, 3)
                ]
                stack = jnp.stack(got)
                total = lax.dynamic_index_in_dim(stack, own, keepdims=False)
                for member in (1, 2, 3):
                    total = total + lax.dynamic_index_in_dim(stack, own ^ member, keepdims=False)
                value = total
                step *= 4
            else:
                other = lax.ppermute(value, axis, [(i, i ^ step) for i in range(count)])
                value = value + other
                step *= 2
    return value


def pack(block, coefs):
    width = block.shape[-1]
    flat = coefs.reshape(-1)
    spare = (-flat.shape[0]) % width
    flat = jnp.pad(flat, (0, spare))
    return jnp.concatenate([block.reshape(-1, width), flat.reshape(-1, width)], axis=0)


def unpack(packed, block_shape, coef_shape):
    count = block_shape[0] * block_shape[1]
    block = packed[:count].reshape(block_shape)
    size = coef_shape[0] * coef_shape[1] * coef_shape[2]
    coefs = packed[count:].reshape(-1)[:size].reshape(coef_shape)
    return block, coefs


def widen(block, coefs, axis, dim, depth, cdepth):
    head = lax.slice_in_dim(block, 0, depth, axis=dim)
    tail = lax.slice_in_dim(block, block.shape[dim] - depth, block.shape[dim], axis=dim)
    chead = lax.slice_in_dim(coefs, 0, cdepth, axis=dim + 1)
    ctail = lax.slice_in_dim(coefs, coefs.shape[dim + 1] - cdepth, coefs.shape[dim + 1], axis=dim + 1)
    before = shifted(pack(tail, ctail), axis, 1)
    after = shifted(pack(head, chead), axis, -1)
    before_b, before_c = unpack(before, head.shape, chead.shape)
    after_b, after_c = unpack(after, head.shape, chead.shape)
    block = jnp.concatenate([before_b, block, after_b], axis=dim)
    coefs = jnp.concatenate([before_c, coefs, after_c], axis=dim + 1)
    return block, coefs


def inset(cells, by):
    if by == 0:
        return cells
    return cells[by:cells.shape[0] - by, by:cells.shape[1] - by]


def neighbors(cells, links):
    cx, cy, cx_up, cy_left = links
    total = cx[:, :, None] * cells[2:, 1:-1] + cx_up[:, :, None] * cells[:-2, 1:-1]
    return total + cy[:, :, None] * cells[1:-1, 2:] + cy_left[:, :, None] * cells[1:-1, :-2]


def local_inner(left, right):
    a = left.reshape(-1, left.shape[-1])
    b = right.reshape(-1, right.shape[-1])
    return jnp.einsum("cp,cq->pq", a, b, precision=highest, preferred_element_type=jnp.float32)


def fold(first, second, third):
    size = first.shape[0]
    row = lax.broadcasted_iota(jnp.int32, first.shape, 0)
    col = lax.broadcasted_iota(jnp.int32, first.shape, 1)
    upper = row <= col
    diag = jnp.sum(jnp.where(row == col, third, jnp.float32(0.0)), axis=0)
    spill = jnp.where((row == size - 1) & (col < size - 1), diag[None, :], jnp.float32(0.0))
    spill = jnp.where((row == size - 2) & (col == 0), diag[size - 1], spill)
    return jnp.stack([jnp.where(upper, first, third), jnp.where(upper, second, spill)])


def unfold(packed):
    size = packed.shape[1]
    row = lax.broadcasted_iota(jnp.int32, packed.shape[1:], 0)
    col = lax.broadcasted_iota(jnp.int32, packed.shape[1:], 1)
    upper = row <= col
    strict = row < col
    one, two = packed[0], packed[1]
    first = jnp.where(upper, one, one.T)
    second = jnp.where(upper, two, two.T)
    diag = jnp.concatenate([two[size - 1, : size - 1], two[size - 2, :1]])
    low = jnp.where(strict.T, one, jnp.float32(0.0))
    third = low + low.T + jnp.where(row == col, diag[None, :], jnp.float32(0.0))
    return first, second, third


def _factor_kernel(gram_ref, g_ref, c_ref, cand_ref, basis_ref, g_out_ref, c_out_ref, work_ref, inv_ref):
    size = gram_ref.shape[0]
    work_ref[...] = gram_ref[...]
    rows = lax.broadcasted_iota(jnp.int32, (size, size), 0)
    cols = lax.broadcasted_iota(jnp.int32, (size, size), 1)
    inv_ref[...] = jnp.where(rows == cols, jnp.float32(1.0), jnp.float32(0.0))
    lane = lax.broadcasted_iota(jnp.int32, (1, size), 1)
    chunk = 8
    for lo in range(0, size, chunk):
        span = size - lo
        cols_s = lax.broadcasted_iota(jnp.int32, (span, size), 1)
        sub = lo + lax.broadcasted_iota(jnp.int32, (span, 1), 0)

        def step(j, carry, lo=lo, cols_s=cols_s, sub=sub):
            whole = work_ref[lo:, :]
            row = work_ref[pl.ds(j, 1), :]
            column = jnp.sum(jnp.where(cols_s == j, whole, jnp.float32(0.0)), axis=1, keepdims=True)
            pivot = jnp.sum(jnp.where(lane == j, row, jnp.float32(0.0)), axis=1, keepdims=True)
            scale = lax.rsqrt(pivot)
            right = jnp.where(lane >= j, row * scale, jnp.float32(0.0))
            left = jnp.where(sub >= j, column * scale, jnp.float32(0.0))
            head = inv_ref[pl.ds(j, 1), :] * scale
            work_ref[lo:, :] = whole - left * right
            below = jnp.where(sub > j, left, jnp.float32(0.0))
            inv_ref[lo:, :] = inv_ref[lo:, :] - below * head
            inv_ref[pl.ds(j, 1), :] = head
            return carry

        lax.fori_loop(lo, min(lo + chunk, size), step, 0)

    inverse = inv_ref[...]
    by_rows = (((1,), (1,)), ((), ()))
    basis_ref[...] = lax.dot_general(
        cand_ref[...], inverse, by_rows, precision=highest, preferred_element_type=jnp.float32
    )
    for block_ref, out_ref in ((g_ref, g_out_ref), (c_ref, c_out_ref)):
        half = jnp.dot(inverse, block_ref[...], precision=highest, preferred_element_type=jnp.float32)
        out_ref[...] = lax.dot_general(
            half, inverse, by_rows, precision=highest, preferred_element_type=jnp.float32
        )


def orthonormalize(gram, g_block, c_block, cand):
    size = gram.shape[0]
    return pl.pallas_call(
        _factor_kernel,
        out_shape=(
            jax.ShapeDtypeStruct(cand.shape, jnp.float32),
            jax.ShapeDtypeStruct(g_block.shape, jnp.float32),
            jax.ShapeDtypeStruct(c_block.shape, jnp.float32),
        ),
        scratch_shapes=[pltpu.VMEM((size, size), jnp.float32), pltpu.VMEM((size, size), jnp.float32)],
    )(gram, g_block, c_block, cand)


def per_device(prior_basis, cond_x, cond_y, capacitance, pad_mask, port_nodes):
    rows_dev, cols_dev = cond_x.shape
    width = port_nodes.shape[0]
    count_x = lax.axis_size("gx")
    count_y = lax.axis_size("gy")
    total_rows = rows_dev * count_x
    total_cols = cols_dev * count_y
    nodes = total_rows * total_cols
    bdepth = SWEEPS + 1
    depth = SWEEPS + 2

    coefs = jnp.stack([cond_x, cond_y, capacitance, pad_mask.astype(jnp.float32)])
    basis_e, coefs_e = widen(prior_basis, coefs, "gx", 0, bdepth, depth)
    basis_e, coefs_e = widen(basis_e, coefs_e, "gy", 1, bdepth, depth)

    row_start = lax.axis_index("gx") * rows_dev - depth
    col_start = lax.axis_index("gy") * cols_dev - depth
    shape_e = (rows_dev + 2 * depth, cols_dev + 2 * depth)
    grows = row_start + lax.broadcasted_iota(jnp.int32, shape_e, 0)
    gcols = col_start + lax.broadcasted_iota(jnp.int32, shape_e, 1)
    inside = (grows >= 0) & (grows < total_rows) & (gcols >= 0) & (gcols < total_cols)
    cx_e = jnp.where(grows < total_rows - 1, coefs_e[0], jnp.float32(0.0))
    cy_e = jnp.where(gcols < total_cols - 1, coefs_e[1], jnp.float32(0.0))
    cap_e = coefs_e[2]
    pad_e = coefs_e[3]

    def at(cells, margin):
        return inset(cells, depth - margin)

    def at_basis(margin):
        return inset(basis_e, bdepth - margin)

    top = depth - 1
    cx_t = at(cx_e, top)
    cy_t = at(cy_e, top)
    cx_up_t = cx_e[0:-2, 1:-1]
    cy_left_t = cy_e[1:-1, 0:-2]
    diag_g_t = cx_t + cx_up_t + cy_t + cy_left_t + supply_conductance * at(pad_e, top)
    diag_t = diag_g_t + shift_point * at(cap_e, top)
    diag_t = jnp.where(at(inside, top), diag_t, jnp.float32(1.0))

    def links_at(margin):
        cut = top - margin
        return tuple(inset(c, cut) for c in (cx_t, cy_t, cx_up_t, cy_left_t))

    first = SWEEPS + 1
    node_ids = at(grows, first) * total_cols + at(gcols, first)
    onehot = (node_ids[:, :, None] == port_nodes[None, None, :]) & at(inside, first)[:, :, None]
    rhs = at(cap_e, first)[:, :, None] * at_basis(first) + port_current * onehot.astype(jnp.float32)
    diag_f = inset(diag_t, top - first)[:, :, None]

    field = rhs / diag_f
    for sweep in range(SWEEPS):
        margin = first - 1 - sweep
        field = (inset(rhs, first - margin) + neighbors(field, links_at(margin))) / inset(diag_f, first - margin)

    tile_basis = at_basis(0)
    proj = allsum_quad(local_inner(tile_basis, inset(field, 1)), ("gy", "gx")) / nodes
    cand_1 = field - jnp.einsum("xyk,kp->xyp", at_basis(1), proj, precision=highest)
    cand = inset(cand_1, 1)
    diag_g = inset(diag_g_t, top)[:, :, None]
    g_image = diag_g * cand - neighbors(cand_1, links_at(0))
    c_image = at(cap_e, 0)[:, :, None] * cand
    gram, g_raw, c_raw = local_inner(cand, cand), local_inner(cand, g_image), local_inner(cand, c_image)
    packed = allsum_exchange(fold(gram, g_raw, c_raw), ("gx", "gy")) / nodes
    gram, g_raw, c_raw = unfold(packed)
    basis_flat, reduced_g, reduced_c = orthonormalize(gram, g_raw, c_raw, cand.reshape(-1, width))
    new_basis = basis_flat.reshape(cand.shape)
    return (new_basis, reduced_g, reduced_c)


def solution(mesh):
    placed = (P("gx", "gy", None), P("gx", "gy"), P("gx", "gy"), P("gx", "gy"), P("gx", "gy"), P())
    return jax.shard_map(
        per_device,
        mesh=mesh,
        in_specs=placed,
        out_specs=(P("gx", "gy", None), P(), P()),
        check_vma=False,
    )
```

```python
import jax
import jax.numpy as jnp
from jax import lax
from jax.experimental import pallas as pl
from jax.experimental.pallas import tpu as pltpu
from jax.sharding import PartitionSpec as P

SWEEPS = 4


shift_point = 0.5
supply_conductance = 4.0
port_current = 8.0
highest = lax.Precision.HIGHEST


def shifted(shard, axis, by):
    devices = lax.axis_size(axis)
    pairs = [(i, i + by) for i in range(devices) if 0 <= i + by < devices]
    return lax.ppermute(shard, axis, pairs)


def allsum(value, axes):
    for axis in axes:
        count = lax.axis_size(axis)
        if count & (count - 1):
            value = lax.psum(value, axis)
            continue
        step = 1
        while step < count:
            other = lax.ppermute(value, axis, [(i, i ^ step) for i in range(count)])
            value = value + other
            step *= 2
    return value


def allsum_exchange(value, axes):
    count = 1
    for axis in axes:
        count *= lax.axis_size(axis)
    flat = value.reshape(-1, value.shape[-1])
    if flat.shape[0] % count:
        return allsum(value, axes)
    parts = flat.reshape(count, -1, flat.shape[-1])
    got = lax.all_to_all(parts, axes, 0, 0, tiled=False)
    total = got[0]
    for k in range(1, count):
        total = total + got[k]
    spread = jnp.broadcast_to(total[None], (count,) + total.shape)
    back = lax.all_to_all(spread, axes, 0, 0, tiled=False)
    return back.reshape(value.shape)


def allsum_quad(value, axes):
    for axis in axes:
        count = lax.axis_size(axis)
        if count & (count - 1):
            value = lax.psum(value, axis)
            continue
        index = lax.axis_index(axis)
        step = 1
        while step < count:
            if step * 4 <= count:
                own = (index // step) % 4
                got = [value] + [
                    lax.ppermute(value, axis, [(i, i ^ (k * step)) for i in range(count)])
                    for k in (1, 2, 3)
                ]
                stack = jnp.stack(got)
                total = lax.dynamic_index_in_dim(stack, own, keepdims=False)
                for member in (1, 2, 3):
                    total = total + lax.dynamic_index_in_dim(stack, own ^ member, keepdims=False)
                value = total
                step *= 4
            else:
                other = lax.ppermute(value, axis, [(i, i ^ step) for i in range(count)])
                value = value + other
                step *= 2
    return value


def pack(block, coefs):
    width = block.shape[-1]
    flat = coefs.reshape(-1)
    spare = (-flat.shape[0]) % width
    flat = jnp.pad(flat, (0, spare))
    return jnp.concatenate([block.reshape(-1, width), flat.reshape(-1, width)], axis=0)


def unpack(packed, block_shape, coef_shape):
    count = block_shape[0] * block_shape[1]
    block = packed[:count].reshape(block_shape)
    size = coef_shape[0] * coef_shape[1] * coef_shape[2]
    coefs = packed[count:].reshape(-1)[:size].reshape(coef_shape)
    return block, coefs


def widen(block, coefs, axis, dim, depth, cdepth):
    head = lax.slice_in_dim(block, 0, depth, axis=dim)
    tail = lax.slice_in_dim(block, block.shape[dim] - depth, block.shape[dim], axis=dim)
    chead = lax.slice_in_dim(coefs, 0, cdepth, axis=dim + 1)
    ctail = lax.slice_in_dim(coefs, coefs.shape[dim + 1] - cdepth, coefs.shape[dim + 1], axis=dim + 1)
    before = shifted(pack(tail, ctail), axis, 1)
    after = shifted(pack(head, chead), axis, -1)
    before_b, before_c = unpack(before, head.shape, chead.shape)
    after_b, after_c = unpack(after, head.shape, chead.shape)
    block = jnp.concatenate([before_b, block, after_b], axis=dim)
    coefs = jnp.concatenate([before_c, coefs, after_c], axis=dim + 1)
    return block, coefs


def inset(cells, by):
    if by == 0:
        return cells
    return cells[by:cells.shape[0] - by, by:cells.shape[1] - by]


def neighbors(cells, links):
    cx, cy, cx_up, cy_left = links
    total = cx[:, :, None] * cells[2:, 1:-1] + cx_up[:, :, None] * cells[:-2, 1:-1]
    return total + cy[:, :, None] * cells[1:-1, 2:] + cy_left[:, :, None] * cells[1:-1, :-2]


def local_inner(left, right):
    a = left.reshape(-1, left.shape[-1])
    b = right.reshape(-1, right.shape[-1])
    return jnp.einsum("cp,cq->pq", a, b, precision=highest, preferred_element_type=jnp.float32)


def fold(first, second, third):
    size = first.shape[0]
    row = lax.broadcasted_iota(jnp.int32, first.shape, 0)
    col = lax.broadcasted_iota(jnp.int32, first.shape, 1)
    upper = row <= col
    on_diag = jnp.where(row == col, third, jnp.float32(0.0))
    across = jnp.sum(on_diag, axis=0, keepdims=True)
    down = jnp.sum(on_diag, axis=1, keepdims=True)
    spill = jnp.where(row == col + 1, across, jnp.float32(0.0))
    spill = jnp.where((row == size - 1) & (col == 0), down, spill)
    return jnp.stack([jnp.where(upper, first, third), jnp.where(upper, second, spill)])


def unfold(one, two):
    size = one.shape[0]
    row = lax.broadcasted_iota(jnp.int32, one.shape, 0)
    col = lax.broadcasted_iota(jnp.int32, one.shape, 1)
    upper = row <= col
    first = jnp.where(upper, one, jnp.transpose(one))
    second = jnp.where(upper, two, jnp.transpose(two))
    low = jnp.where(row > col, one, jnp.float32(0.0))
    across = jnp.sum(jnp.where(row == col + 1, two, jnp.float32(0.0)), axis=0, keepdims=True)
    lane = lax.broadcasted_iota(jnp.int32, (1, size), 1)
    across = jnp.where(lane == size - 1, two[size - 1:size, 0:1], across)
    third = low + jnp.transpose(low) + jnp.where(row == col, across, jnp.float32(0.0))
    return first, second, third


def _factor_kernel(packed_ref, cand_ref, basis_ref, g_out_ref, c_out_ref, work_ref, inv_ref):
    size = packed_ref.shape[1]
    gram, g_block, c_block = unfold(packed_ref[0], packed_ref[1])
    work_ref[...] = gram
    rows = lax.broadcasted_iota(jnp.int32, (size, size), 0)
    cols = lax.broadcasted_iota(jnp.int32, (size, size), 1)
    inv_ref[...] = jnp.where(rows == cols, jnp.float32(1.0), jnp.float32(0.0))
    lane = lax.broadcasted_iota(jnp.int32, (1, size), 1)
    chunk = 8
    for lo in range(0, size, chunk):
        span = size - lo
        cols_s = lax.broadcasted_iota(jnp.int32, (span, size), 1)
        sub = lo + lax.broadcasted_iota(jnp.int32, (span, 1), 0)

        def step(j, carry, lo=lo, cols_s=cols_s, sub=sub):
            whole = work_ref[lo:, :]
            row = work_ref[pl.ds(j, 1), :]
            column = jnp.sum(jnp.where(cols_s == j, whole, jnp.float32(0.0)), axis=1, keepdims=True)
            pivot = jnp.sum(jnp.where(lane == j, row, jnp.float32(0.0)), axis=1, keepdims=True)
            scale = lax.rsqrt(pivot)
            right = jnp.where(lane >= j, row * scale, jnp.float32(0.0))
            left = jnp.where(sub >= j, column * scale, jnp.float32(0.0))
            head = inv_ref[pl.ds(j, 1), :] * scale
            work_ref[lo:, :] = whole - left * right
            below = jnp.where(sub > j, left, jnp.float32(0.0))
            inv_ref[lo:, :] = inv_ref[lo:, :] - below * head
            inv_ref[pl.ds(j, 1), :] = head
            return carry

        lax.fori_loop(lo, min(lo + chunk, size), step, 0)

    inverse = inv_ref[...]
    by_rows = (((1,), (1,)), ((), ()))
    basis_ref[...] = lax.dot_general(
        cand_ref[...], inverse, by_rows, precision=highest, preferred_element_type=jnp.float32
    )
    for block, out_ref in ((g_block, g_out_ref), (c_block, c_out_ref)):
        half = jnp.dot(inverse, block, precision=highest, preferred_element_type=jnp.float32)
        out_ref[...] = lax.dot_general(
            half, inverse, by_rows, precision=highest, preferred_element_type=jnp.float32
        )


def orthonormalize(packed, cand):
    size = packed.shape[1]
    return pl.pallas_call(
        _factor_kernel,
        out_shape=(
            jax.ShapeDtypeStruct(cand.shape, jnp.float32),
            jax.ShapeDtypeStruct((size, size), jnp.float32),
            jax.ShapeDtypeStruct((size, size), jnp.float32),
        ),
        scratch_shapes=[pltpu.VMEM((size, size), jnp.float32), pltpu.VMEM((size, size), jnp.float32)],
    )(packed, cand)


def per_device(prior_basis, cond_x, cond_y, capacitance, pad_mask, port_nodes):
    rows_dev, cols_dev = cond_x.shape
    width = port_nodes.shape[0]
    count_x = lax.axis_size("gx")
    count_y = lax.axis_size("gy")
    total_rows = rows_dev * count_x
    total_cols = cols_dev * count_y
    nodes = total_rows * total_cols
    bdepth = SWEEPS + 1
    depth = SWEEPS + 2

    coefs = jnp.stack([cond_x, cond_y, capacitance, pad_mask.astype(jnp.float32)])
    basis_e, coefs_e = widen(prior_basis, coefs, "gx", 0, bdepth, depth)
    basis_e, coefs_e = widen(basis_e, coefs_e, "gy", 1, bdepth, depth)

    row_start = lax.axis_index("gx") * rows_dev - depth
    col_start = lax.axis_index("gy") * cols_dev - depth
    shape_e = (rows_dev + 2 * depth, cols_dev + 2 * depth)
    grows = row_start + lax.broadcasted_iota(jnp.int32, shape_e, 0)
    gcols = col_start + lax.broadcasted_iota(jnp.int32, shape_e, 1)
    inside = (grows >= 0) & (grows < total_rows) & (gcols >= 0) & (gcols < total_cols)
    cx_e = jnp.where(grows < total_rows - 1, coefs_e[0], jnp.float32(0.0))
    cy_e = jnp.where(gcols < total_cols - 1, coefs_e[1], jnp.float32(0.0))
    cap_e = coefs_e[2]
    pad_e = coefs_e[3]

    def at(cells, margin):
        return inset(cells, depth - margin)

    def at_basis(margin):
        return inset(basis_e, bdepth - margin)

    top = depth - 1
    cx_t = at(cx_e, top)
    cy_t = at(cy_e, top)
    cx_up_t = cx_e[0:-2, 1:-1]
    cy_left_t = cy_e[1:-1, 0:-2]
    diag_g_t = cx_t + cx_up_t + cy_t + cy_left_t + supply_conductance * at(pad_e, top)
    diag_t = diag_g_t + shift_point * at(cap_e, top)
    diag_t = jnp.where(at(inside, top), diag_t, jnp.float32(1.0))

    def links_at(margin):
        cut = top - margin
        return tuple(inset(c, cut) for c in (cx_t, cy_t, cx_up_t, cy_left_t))

    first = SWEEPS + 1
    node_ids = at(grows, first) * total_cols + at(gcols, first)
    onehot = (node_ids[:, :, None] == port_nodes[None, None, :]) & at(inside, first)[:, :, None]
    rhs = at(cap_e, first)[:, :, None] * at_basis(first) + port_current * onehot.astype(jnp.float32)
    diag_f = inset(diag_t, top - first)[:, :, None]

    field = rhs / diag_f
    for sweep in range(SWEEPS):
        margin = first - 1 - sweep
        field = (inset(rhs, first - margin) + neighbors(field, links_at(margin))) / inset(diag_f, first - margin)

    tile_basis = at_basis(0)
    proj = allsum_quad(local_inner(tile_basis, inset(field, 1)), ("gy", "gx")) / nodes
    cand_1 = field - jnp.einsum("xyk,kp->xyp", at_basis(1), proj, precision=highest)
    cand = inset(cand_1, 1)
    diag_g = inset(diag_g_t, top)[:, :, None]
    g_image = diag_g * cand - neighbors(cand_1, links_at(0))
    c_image = at(cap_e, 0)[:, :, None] * cand
    gram, g_raw, c_raw = local_inner(cand, cand), local_inner(cand, g_image), local_inner(cand, c_image)
    packed = allsum_exchange(fold(gram, g_raw, c_raw), ("gx", "gy")) / nodes
    basis_flat, reduced_g, reduced_c = orthonormalize(packed, cand.reshape(-1, width))
    new_basis = basis_flat.reshape(cand.shape)
    return (new_basis, reduced_g, reduced_c)


def solution(mesh):
    placed = (P("gx", "gy", None), P("gx", "gy"), P("gx", "gy"), P("gx", "gy"), P("gx", "gy"), P())
    return jax.shard_map(
        per_device,
        mesh=mesh,
        in_specs=placed,
        out_specs=(P("gx", "gy", None), P(), P()),
        check_vma=False,
    )
```

```python
import functools

import jax
import jax.numpy as jnp
from jax import lax
from jax.experimental import pallas as pl
from jax.experimental.pallas import tpu as pltpu
from jax.sharding import PartitionSpec as P

SWEEPS = 4


shift_point = 0.5
supply_conductance = 4.0
port_current = 8.0
highest = lax.Precision.HIGHEST


def shifted(shard, axis, by):
    devices = lax.axis_size(axis)
    pairs = [(i, i + by) for i in range(devices) if 0 <= i + by < devices]
    return lax.ppermute(shard, axis, pairs)


def allsum(value, axes):
    for axis in axes:
        count = lax.axis_size(axis)
        if count & (count - 1):
            value = lax.psum(value, axis)
            continue
        step = 1
        while step < count:
            other = lax.ppermute(value, axis, [(i, i ^ step) for i in range(count)])
            value = value + other
            step *= 2
    return value


def allsum_exchange(value, axes):
    count = 1
    for axis in axes:
        count *= lax.axis_size(axis)
    flat = value.reshape(-1, value.shape[-1])
    if flat.shape[0] % count:
        return allsum(value, axes)
    parts = flat.reshape(count, -1, flat.shape[-1])
    got = lax.all_to_all(parts, axes, 0, 0, tiled=False)
    total = got[0]
    for k in range(1, count):
        total = total + got[k]
    spread = jnp.broadcast_to(total[None], (count,) + total.shape)
    back = lax.all_to_all(spread, axes, 0, 0, tiled=False)
    return back.reshape(value.shape)


def allsum_quad(value, axes):
    for axis in axes:
        count = lax.axis_size(axis)
        if count & (count - 1):
            value = lax.psum(value, axis)
            continue
        index = lax.axis_index(axis)
        step = 1
        while step < count:
            if step * 4 <= count:
                own = (index // step) % 4
                got = [value] + [
                    lax.ppermute(value, axis, [(i, i ^ (k * step)) for i in range(count)])
                    for k in (1, 2, 3)
                ]
                stack = jnp.stack(got)
                total = lax.dynamic_index_in_dim(stack, own, keepdims=False)
                for member in (1, 2, 3):
                    total = total + lax.dynamic_index_in_dim(stack, own ^ member, keepdims=False)
                value = total
                step *= 4
            else:
                other = lax.ppermute(value, axis, [(i, i ^ step) for i in range(count)])
                value = value + other
                step *= 2
    return value


def pack(block, coefs):
    width = block.shape[-1]
    flat = jnp.concatenate([c.reshape(-1) for c in coefs])
    spare = (-flat.shape[0]) % width
    flat = jnp.pad(flat, (0, spare))
    return jnp.concatenate([block.reshape(-1, width), flat.reshape(-1, width)], axis=0)


def unpack(packed, block_shape, coef_shape, count):
    rows = block_shape[0] * block_shape[1]
    block = packed[:rows].reshape(block_shape)
    size = coef_shape[0] * coef_shape[1]
    flat = packed[rows:].reshape(-1)
    coefs = [flat[k * size:(k + 1) * size].reshape(coef_shape) for k in range(count)]
    return block, coefs


def widen(block, coefs, axis, dim, depth, cdepth):
    head = lax.slice_in_dim(block, 0, depth, axis=dim)
    tail = lax.slice_in_dim(block, block.shape[dim] - depth, block.shape[dim], axis=dim)
    cheads = [lax.slice_in_dim(c, 0, cdepth, axis=dim) for c in coefs]
    ctails = [lax.slice_in_dim(c, c.shape[dim] - cdepth, c.shape[dim], axis=dim) for c in coefs]
    before = shifted(pack(tail, ctails), axis, 1)
    after = shifted(pack(head, cheads), axis, -1)
    before_b, before_c = unpack(before, head.shape, cheads[0].shape, len(coefs))
    after_b, after_c = unpack(after, head.shape, cheads[0].shape, len(coefs))
    block = jnp.concatenate([before_b, block, after_b], axis=dim)
    coefs = [jnp.concatenate([x, c, y], axis=dim) for x, c, y in zip(before_c, coefs, after_c)]
    return block, coefs


def inset(cells, by):
    if by == 0:
        return cells
    return cells[by:cells.shape[0] - by, by:cells.shape[1] - by]


def neighbors(cells, links):
    cx, cy, cx_up, cy_left = links
    total = cx[:, :, None] * cells[2:, 1:-1] + cx_up[:, :, None] * cells[:-2, 1:-1]
    return total + cy[:, :, None] * cells[1:-1, 2:] + cy_left[:, :, None] * cells[1:-1, :-2]


def local_inner(left, right):
    a = left.reshape(-1, left.shape[-1])
    b = right.reshape(-1, right.shape[-1])
    return jnp.einsum("cp,cq->pq", a, b, precision=highest, preferred_element_type=jnp.float32)


def fold(first, second, third):
    size = first.shape[0]
    row = lax.broadcasted_iota(jnp.int32, first.shape, 0)
    col = lax.broadcasted_iota(jnp.int32, first.shape, 1)
    upper = row <= col
    on_diag = jnp.where(row == col, third, jnp.float32(0.0))
    across = jnp.sum(on_diag, axis=0, keepdims=True)
    down = jnp.sum(on_diag, axis=1, keepdims=True)
    spill = jnp.where(row == col + 1, across, jnp.float32(0.0))
    spill = jnp.where((row == size - 1) & (col == 0), down, spill)
    return jnp.stack([jnp.where(upper, first, third), jnp.where(upper, second, spill)])


def unfold(one, two):
    size = one.shape[0]
    row = lax.broadcasted_iota(jnp.int32, one.shape, 0)
    col = lax.broadcasted_iota(jnp.int32, one.shape, 1)
    upper = row <= col
    first = jnp.where(upper, one, jnp.transpose(one))
    second = jnp.where(upper, two, jnp.transpose(two))
    low = jnp.where(row > col, one, jnp.float32(0.0))
    across = jnp.sum(jnp.where(row == col + 1, two, jnp.float32(0.0)), axis=0, keepdims=True)
    lane = lax.broadcasted_iota(jnp.int32, (1, size), 1)
    across = jnp.where(lane == size - 1, two[size - 1:size, 0:1], across)
    third = low + jnp.transpose(low) + jnp.where(row == col, across, jnp.float32(0.0))
    return first, second, third


def _factor_kernel(packed_ref, cand_ref, basis_ref, g_out_ref, c_out_ref, work_ref, inv_ref, nodes):
    size = packed_ref.shape[1]
    gram, g_block, c_block = unfold(packed_ref[0] / nodes, packed_ref[1] / nodes)
    work_ref[...] = gram
    rows = lax.broadcasted_iota(jnp.int32, (size, size), 0)
    cols = lax.broadcasted_iota(jnp.int32, (size, size), 1)
    inv_ref[...] = jnp.where(rows == cols, jnp.float32(1.0), jnp.float32(0.0))
    lane = lax.broadcasted_iota(jnp.int32, (1, size), 1)
    chunk = 8
    for lo in range(0, size, chunk):
        span = size - lo
        cols_s = lax.broadcasted_iota(jnp.int32, (span, size), 1)
        sub = lo + lax.broadcasted_iota(jnp.int32, (span, 1), 0)

        def step(j, carry, lo=lo, cols_s=cols_s, sub=sub):
            whole = work_ref[lo:, :]
            row = work_ref[pl.ds(j, 1), :]
            column = jnp.sum(jnp.where(cols_s == j, whole, jnp.float32(0.0)), axis=1, keepdims=True)
            pivot = jnp.sum(jnp.where(lane == j, row, jnp.float32(0.0)), axis=1, keepdims=True)
            scale = lax.rsqrt(pivot)
            right = jnp.where(lane >= j, row * scale, jnp.float32(0.0))
            left = jnp.where(sub >= j, column * scale, jnp.float32(0.0))
            head = inv_ref[pl.ds(j, 1), :] * scale
            work_ref[lo:, :] = whole - left * right
            below = jnp.where(sub > j, left, jnp.float32(0.0))
            inv_ref[lo:, :] = inv_ref[lo:, :] - below * head
            inv_ref[pl.ds(j, 1), :] = head
            return carry

        lax.fori_loop(lo, min(lo + chunk, size), step, 0)

    inverse = inv_ref[...]
    by_rows = (((1,), (1,)), ((), ()))
    basis_ref[...] = lax.dot_general(
        cand_ref[...], inverse, by_rows, precision=highest, preferred_element_type=jnp.float32
    )
    for block, out_ref in ((g_block, g_out_ref), (c_block, c_out_ref)):
        half = jnp.dot(inverse, block, precision=highest, preferred_element_type=jnp.float32)
        out_ref[...] = lax.dot_general(
            half, inverse, by_rows, precision=highest, preferred_element_type=jnp.float32
        )


def orthonormalize(packed, cand, nodes):
    size = packed.shape[1]
    return pl.pallas_call(
        functools.partial(_factor_kernel, nodes=float(nodes)),
        out_shape=(
            jax.ShapeDtypeStruct(cand.shape, jnp.float32),
            jax.ShapeDtypeStruct((size, size), jnp.float32),
            jax.ShapeDtypeStruct((size, size), jnp.float32),
        ),
        scratch_shapes=[pltpu.VMEM((size, size), jnp.float32), pltpu.VMEM((size, size), jnp.float32)],
    )(packed, cand)


def per_device(prior_basis, cond_x, cond_y, capacitance, pad_mask, port_nodes):
    rows_dev, cols_dev = cond_x.shape
    width = port_nodes.shape[0]
    count_x = lax.axis_size("gx")
    count_y = lax.axis_size("gy")
    total_rows = rows_dev * count_x
    total_cols = cols_dev * count_y
    nodes = total_rows * total_cols
    bdepth = SWEEPS + 1
    depth = SWEEPS + 2

    coefs = [cond_x, cond_y, capacitance, pad_mask.astype(jnp.float32)]
    basis_e, coefs_e = widen(prior_basis, coefs, "gx", 0, bdepth, depth)
    basis_e, coefs_e = widen(basis_e, coefs_e, "gy", 1, bdepth, depth)

    row_start = lax.axis_index("gx") * rows_dev - depth
    col_start = lax.axis_index("gy") * cols_dev - depth
    shape_e = (rows_dev + 2 * depth, cols_dev + 2 * depth)
    grows = row_start + lax.broadcasted_iota(jnp.int32, shape_e, 0)
    gcols = col_start + lax.broadcasted_iota(jnp.int32, shape_e, 1)
    inside = (grows >= 0) & (grows < total_rows) & (gcols >= 0) & (gcols < total_cols)
    cx_e = jnp.where(grows < total_rows - 1, coefs_e[0], jnp.float32(0.0))
    cy_e = jnp.where(gcols < total_cols - 1, coefs_e[1], jnp.float32(0.0))
    cap_e = coefs_e[2]
    pad_e = coefs_e[3]

    def at(cells, margin):
        return inset(cells, depth - margin)

    def at_basis(margin):
        return inset(basis_e, bdepth - margin)

    top = depth - 1
    cx_t = at(cx_e, top)
    cy_t = at(cy_e, top)
    cx_up_t = cx_e[0:-2, 1:-1]
    cy_left_t = cy_e[1:-1, 0:-2]
    diag_g_t = cx_t + cx_up_t + cy_t + cy_left_t + supply_conductance * at(pad_e, top)
    diag_t = diag_g_t + shift_point * at(cap_e, top)
    diag_t = jnp.where(at(inside, top), diag_t, jnp.float32(1.0))

    def links_at(margin):
        cut = top - margin
        return tuple(inset(c, cut) for c in (cx_t, cy_t, cx_up_t, cy_left_t))

    first = SWEEPS + 1
    node_ids = at(grows, first) * total_cols + at(gcols, first)
    onehot = (node_ids[:, :, None] == port_nodes[None, None, :]) & at(inside, first)[:, :, None]
    rhs = at(cap_e, first)[:, :, None] * at_basis(first) + port_current * onehot.astype(jnp.float32)
    diag_f = inset(diag_t, top - first)[:, :, None]

    field = rhs / diag_f
    for sweep in range(SWEEPS):
        margin = first - 1 - sweep
        field = (inset(rhs, first - margin) + neighbors(field, links_at(margin))) / inset(diag_f, first - margin)

    tile_basis = at_basis(0)
    proj = allsum_quad(local_inner(tile_basis, inset(field, 1)), ("gy", "gx")) / nodes
    cand_1 = field - jnp.einsum("xyk,kp->xyp", at_basis(1), proj, precision=highest)
    cand = inset(cand_1, 1)
    diag_g = inset(diag_g_t, top)[:, :, None]
    g_image = diag_g * cand - neighbors(cand_1, links_at(0))
    c_image = at(cap_e, 0)[:, :, None] * cand
    gram, g_raw, c_raw = local_inner(cand, cand), local_inner(cand, g_image), local_inner(cand, c_image)
    packed = allsum_exchange(fold(gram, g_raw, c_raw), ("gx", "gy"))
    basis_flat, reduced_g, reduced_c = orthonormalize(packed, cand.reshape(-1, width), nodes)
    new_basis = basis_flat.reshape(cand.shape)
    return (new_basis, reduced_g, reduced_c)


def solution(mesh):
    placed = (P("gx", "gy", None), P("gx", "gy"), P("gx", "gy"), P("gx", "gy"), P("gx", "gy"), P())
    return jax.shard_map(
        per_device,
        mesh=mesh,
        in_specs=placed,
        out_specs=(P("gx", "gy", None), P(), P()),
        check_vma=False,
    )
```

```python
import jax
import jax.numpy as jnp
from jax import lax
from jax.experimental import pallas as pl
from jax.experimental.pallas import tpu as pltpu
from jax.sharding import PartitionSpec as P

SWEEPS = 4


shift_point = 0.5
supply_conductance = 4.0
port_current = 8.0
highest = lax.Precision.HIGHEST


def shifted(shard, axis, by):
    devices = lax.axis_size(axis)
    pairs = [(i, i + by) for i in range(devices) if 0 <= i + by < devices]
    return lax.ppermute(shard, axis, pairs)


def allsum(value, axes):
    for axis in axes:
        count = lax.axis_size(axis)
        if count & (count - 1):
            value = lax.psum(value, axis)
            continue
        step = 1
        while step < count:
            other = lax.ppermute(value, axis, [(i, i ^ step) for i in range(count)])
            value = value + other
            step *= 2
    return value


def allsum_exchange(value, axes):
    count = 1
    for axis in axes:
        count *= lax.axis_size(axis)
    flat = value.reshape(-1, value.shape[-1])
    if flat.shape[0] % count:
        return allsum(value, axes)
    parts = flat.reshape(count, -1, flat.shape[-1])
    got = lax.all_to_all(parts, axes, 0, 0, tiled=False)
    total = got[0]
    for k in range(1, count):
        total = total + got[k]
    spread = jnp.broadcast_to(total[None], (count,) + total.shape)
    back = lax.all_to_all(spread, axes, 0, 0, tiled=False)
    return back.reshape(value.shape)


def allsum_quad(value, axes):
    for axis in axes:
        count = lax.axis_size(axis)
        if count & (count - 1):
            value = lax.psum(value, axis)
            continue
        index = lax.axis_index(axis)
        step = 1
        while step < count:
            if step * 4 <= count:
                own = (index // step) % 4
                got = [value] + [
                    lax.ppermute(value, axis, [(i, i ^ (k * step)) for i in range(count)])
                    for k in (1, 2, 3)
                ]
                stack = jnp.stack(got)
                total = lax.dynamic_index_in_dim(stack, own, keepdims=False)
                for member in (1, 2, 3):
                    total = total + lax.dynamic_index_in_dim(stack, own ^ member, keepdims=False)
                value = total
                step *= 4
            else:
                other = lax.ppermute(value, axis, [(i, i ^ step) for i in range(count)])
                value = value + other
                step *= 2
    return value


def pack(block, coefs):
    width = block.shape[-1]
    flat = coefs.reshape(-1)
    spare = (-flat.shape[0]) % width
    flat = jnp.pad(flat, (0, spare))
    return jnp.concatenate([block.reshape(-1, width), flat.reshape(-1, width)], axis=0)


def unpack(packed, block_shape, coef_shape):
    count = block_shape[0] * block_shape[1]
    block = packed[:count].reshape(block_shape)
    size = coef_shape[0] * coef_shape[1] * coef_shape[2]
    coefs = packed[count:].reshape(-1)[:size].reshape(coef_shape)
    return block, coefs


def widen(block, coefs, axis, dim, depth, cdepth):
    head = lax.slice_in_dim(block, 0, depth, axis=dim)
    tail = lax.slice_in_dim(block, block.shape[dim] - depth, block.shape[dim], axis=dim)
    chead = lax.slice_in_dim(coefs, 0, cdepth, axis=dim + 1)
    ctail = lax.slice_in_dim(coefs, coefs.shape[dim + 1] - cdepth, coefs.shape[dim + 1], axis=dim + 1)
    before = shifted(pack(tail, ctail), axis, 1)
    after = shifted(pack(head, chead), axis, -1)
    before_b, before_c = unpack(before, head.shape, chead.shape)
    after_b, after_c = unpack(after, head.shape, chead.shape)
    block = jnp.concatenate([before_b, block, after_b], axis=dim)
    coefs = jnp.concatenate([before_c, coefs, after_c], axis=dim + 1)
    return block, coefs


def inset(cells, by):
    if by == 0:
        return cells
    return cells[by:cells.shape[0] - by, by:cells.shape[1] - by]


def neighbors(cells, links):
    cx, cy, cx_up, cy_left = links
    total = cx[:, :, None] * cells[2:, 1:-1] + cx_up[:, :, None] * cells[:-2, 1:-1]
    return total + cy[:, :, None] * cells[1:-1, 2:] + cy_left[:, :, None] * cells[1:-1, :-2]


def local_inner(left, right):
    a = left.reshape(-1, left.shape[-1])
    b = right.reshape(-1, right.shape[-1])
    return jnp.einsum("cp,cq->pq", a, b, precision=highest, preferred_element_type=jnp.float32)


def fold(first, second, third):
    size = first.shape[0]
    row = lax.broadcasted_iota(jnp.int32, first.shape, 0)
    col = lax.broadcasted_iota(jnp.int32, first.shape, 1)
    upper = row <= col
    on_diag = jnp.where(row == col, third, jnp.float32(0.0))
    across = jnp.sum(on_diag, axis=0, keepdims=True)
    down = jnp.sum(on_diag, axis=1, keepdims=True)
    spill = jnp.where(row == col + 1, across, jnp.float32(0.0))
    spill = jnp.where((row == size - 1) & (col == 0), down, spill)
    return jnp.stack([jnp.where(upper, first, third), jnp.where(upper, second, spill)])


def unfold(one, two):
    size = one.shape[0]
    row = lax.broadcasted_iota(jnp.int32, one.shape, 0)
    col = lax.broadcasted_iota(jnp.int32, one.shape, 1)
    upper = row <= col
    first = jnp.where(upper, one, jnp.transpose(one))
    second = jnp.where(upper, two, jnp.transpose(two))
    low = jnp.where(row > col, one, jnp.float32(0.0))
    across = jnp.sum(jnp.where(row == col + 1, two, jnp.float32(0.0)), axis=0, keepdims=True)
    lane = lax.broadcasted_iota(jnp.int32, (1, size), 1)
    across = jnp.where(lane == size - 1, two[size - 1:size, 0:1], across)
    third = low + jnp.transpose(low) + jnp.where(row == col, across, jnp.float32(0.0))
    return first, second, third


def _factor_kernel(packed_ref, cand_ref, basis_ref, g_out_ref, c_out_ref, work_ref, inv_ref):
    size = packed_ref.shape[1]
    gram, g_block, c_block = unfold(packed_ref[0], packed_ref[1])
    work_ref[...] = gram
    rows = lax.broadcasted_iota(jnp.int32, (size, size), 0)
    cols = lax.broadcasted_iota(jnp.int32, (size, size), 1)
    inv_ref[...] = jnp.where(rows == cols, jnp.float32(1.0), jnp.float32(0.0))
    lane = lax.broadcasted_iota(jnp.int32, (1, size), 1)
    chunk = 8
    for lo in range(0, size, chunk):
        span = size - lo
        cols_s = lax.broadcasted_iota(jnp.int32, (span, size), 1)
        sub = lo + lax.broadcasted_iota(jnp.int32, (span, 1), 0)

        def step(j, carry, lo=lo, cols_s=cols_s, sub=sub):
            whole = work_ref[lo:, :]
            row = work_ref[pl.ds(j, 1), :]
            column = jnp.sum(jnp.where(cols_s == j, whole, jnp.float32(0.0)), axis=1, keepdims=True)
            pivot = jnp.sum(jnp.where(lane == j, row, jnp.float32(0.0)), axis=1, keepdims=True)
            scale = lax.rsqrt(pivot)
            right = jnp.where(lane >= j, row * scale, jnp.float32(0.0))
            left = jnp.where(sub >= j, column * scale, jnp.float32(0.0))
            head = inv_ref[pl.ds(j, 1), :] * scale
            work_ref[lo:, :] = whole - left * right
            below = jnp.where(sub > j, left, jnp.float32(0.0))
            inv_ref[lo:, :] = inv_ref[lo:, :] - below * head
            inv_ref[pl.ds(j, 1), :] = head
            return carry

        lax.fori_loop(lo, min(lo + chunk, size), step, 0)

    inverse = inv_ref[...]
    by_rows = (((1,), (1,)), ((), ()))
    basis_ref[...] = lax.dot_general(
        cand_ref[...], inverse, by_rows, precision=highest, preferred_element_type=jnp.float32
    )
    for block, out_ref in ((g_block, g_out_ref), (c_block, c_out_ref)):
        half = jnp.dot(inverse, block, precision=highest, preferred_element_type=jnp.float32)
        out_ref[...] = lax.dot_general(
            half, inverse, by_rows, precision=highest, preferred_element_type=jnp.float32
        )


def orthonormalize(packed, cand):
    size = packed.shape[1]
    return pl.pallas_call(
        _factor_kernel,
        out_shape=(
            jax.ShapeDtypeStruct(cand.shape, jnp.float32),
            jax.ShapeDtypeStruct((size, size), jnp.float32),
            jax.ShapeDtypeStruct((size, size), jnp.float32),
        ),
        scratch_shapes=[pltpu.VMEM((size, size), jnp.float32), pltpu.VMEM((size, size), jnp.float32)],
    )(packed, cand)


def per_device(prior_basis, cond_x, cond_y, capacitance, pad_mask, port_nodes):
    rows_dev, cols_dev = cond_x.shape
    width = port_nodes.shape[0]
    count_x = lax.axis_size("gx")
    count_y = lax.axis_size("gy")
    total_rows = rows_dev * count_x
    total_cols = cols_dev * count_y
    nodes = total_rows * total_cols
    bdepth = SWEEPS + 1
    depth = SWEEPS + 2

    coefs = jnp.stack([cond_x, cond_y, capacitance, pad_mask.astype(jnp.float32)])
    basis_e, coefs_e = widen(prior_basis, coefs, "gy", 1, bdepth, depth)
    basis_e, coefs_e = widen(basis_e, coefs_e, "gx", 0, bdepth, depth)

    row_start = lax.axis_index("gx") * rows_dev - depth
    col_start = lax.axis_index("gy") * cols_dev - depth
    shape_e = (rows_dev + 2 * depth, cols_dev + 2 * depth)
    grows = row_start + lax.broadcasted_iota(jnp.int32, shape_e, 0)
    gcols = col_start + lax.broadcasted_iota(jnp.int32, shape_e, 1)
    inside = (grows >= 0) & (grows < total_rows) & (gcols >= 0) & (gcols < total_cols)
    cx_e = jnp.where(grows < total_rows - 1, coefs_e[0], jnp.float32(0.0))
    cy_e = jnp.where(gcols < total_cols - 1, coefs_e[1], jnp.float32(0.0))
    cap_e = coefs_e[2]
    pad_e = coefs_e[3]

    def at(cells, margin):
        return inset(cells, depth - margin)

    def at_basis(margin):
        return inset(basis_e, bdepth - margin)

    top = depth - 1
    cx_t = at(cx_e, top)
    cy_t = at(cy_e, top)
    cx_up_t = cx_e[0:-2, 1:-1]
    cy_left_t = cy_e[1:-1, 0:-2]
    diag_g_t = cx_t + cx_up_t + cy_t + cy_left_t + supply_conductance * at(pad_e, top)
    diag_t = diag_g_t + shift_point * at(cap_e, top)
    diag_t = jnp.where(at(inside, top), diag_t, jnp.float32(1.0))

    def links_at(margin):
        cut = top - margin
        return tuple(inset(c, cut) for c in (cx_t, cy_t, cx_up_t, cy_left_t))

    first = SWEEPS + 1
    node_ids = at(grows, first) * total_cols + at(gcols, first)
    onehot = (node_ids[:, :, None] == port_nodes[None, None, :]) & at(inside, first)[:, :, None]
    rhs = at(cap_e, first)[:, :, None] * at_basis(first) + port_current * onehot.astype(jnp.float32)
    diag_f = inset(diag_t, top - first)[:, :, None]

    field = rhs / diag_f
    for sweep in range(SWEEPS):
        margin = first - 1 - sweep
        field = (inset(rhs, first - margin) + neighbors(field, links_at(margin))) / inset(diag_f, first - margin)

    tile_basis = at_basis(0)
    proj = allsum_quad(local_inner(tile_basis, inset(field, 1)), ("gy", "gx")) / nodes
    cand_1 = field - jnp.einsum("xyk,kp->xyp", at_basis(1), proj, precision=highest)
    cand = inset(cand_1, 1)
    diag_g = inset(diag_g_t, top)[:, :, None]
    g_image = diag_g * cand - neighbors(cand_1, links_at(0))
    c_image = at(cap_e, 0)[:, :, None] * cand
    gram, g_raw, c_raw = local_inner(cand, cand), local_inner(cand, g_image), local_inner(cand, c_image)
    packed = allsum_exchange(fold(gram, g_raw, c_raw), ("gx", "gy")) / nodes
    basis_flat, reduced_g, reduced_c = orthonormalize(packed, cand.reshape(-1, width))
    new_basis = basis_flat.reshape(cand.shape)
    return (new_basis, reduced_g, reduced_c)


def solution(mesh):
    placed = (P("gx", "gy", None), P("gx", "gy"), P("gx", "gy"), P("gx", "gy"), P("gx", "gy"), P())
    return jax.shard_map(
        per_device,
        mesh=mesh,
        in_specs=placed,
        out_specs=(P("gx", "gy", None), P(), P()),
        check_vma=False,
    )
```

```python
import jax
import jax.numpy as jnp
from jax import lax
from jax.experimental import pallas as pl
from jax.experimental.pallas import tpu as pltpu
from jax.sharding import PartitionSpec as P

SWEEPS = 4


shift_point = 0.5
supply_conductance = 4.0
port_current = 8.0
highest = lax.Precision.HIGHEST


def shifted(shard, axis, by):
    devices = lax.axis_size(axis)
    pairs = [(i, i + by) for i in range(devices) if 0 <= i + by < devices]
    return lax.ppermute(shard, axis, pairs)


def allsum(value, axes):
    for axis in axes:
        count = lax.axis_size(axis)
        if count & (count - 1):
            value = lax.psum(value, axis)
            continue
        step = 1
        while step < count:
            other = lax.ppermute(value, axis, [(i, i ^ step) for i in range(count)])
            value = value + other
            step *= 2
    return value


def allsum_exchange(value, axes):
    count = 1
    for axis in axes:
        count *= lax.axis_size(axis)
    flat = value.reshape(-1, value.shape[-1])
    if flat.shape[0] % count:
        return allsum(value, axes)
    parts = flat.reshape(count, -1, flat.shape[-1])
    got = lax.all_to_all(parts, axes, 0, 0, tiled=False)
    total = got[0]
    for k in range(1, count):
        total = total + got[k]
    spread = jnp.broadcast_to(total[None], (count,) + total.shape)
    back = lax.all_to_all(spread, axes, 0, 0, tiled=False)
    return back.reshape(value.shape)


def allsum_quad(value, axes):
    for axis in axes:
        count = lax.axis_size(axis)
        if count & (count - 1):
            value = lax.psum(value, axis)
            continue
        index = lax.axis_index(axis)
        step = 1
        while step < count:
            if step * 4 <= count:
                own = (index // step) % 4
                got = [value] + [
                    lax.ppermute(value, axis, [(i, i ^ (k * step)) for i in range(count)])
                    for k in (1, 2, 3)
                ]
                stack = jnp.stack(got)
                total = lax.dynamic_index_in_dim(stack, own, keepdims=False)
                for member in (1, 2, 3):
                    total = total + lax.dynamic_index_in_dim(stack, own ^ member, keepdims=False)
                value = total
                step *= 4
            else:
                other = lax.ppermute(value, axis, [(i, i ^ step) for i in range(count)])
                value = value + other
                step *= 2
    return value


def pack(block, coefs):
    width = block.shape[-1]
    flat = coefs.reshape(-1)
    spare = (-flat.shape[0]) % width
    flat = jnp.pad(flat, (0, spare))
    return jnp.concatenate([block.reshape(-1, width), flat.reshape(-1, width)], axis=0)


def unpack(packed, block_shape, coef_shape):
    count = block_shape[0] * block_shape[1]
    block = packed[:count].reshape(block_shape)
    size = coef_shape[0] * coef_shape[1] * coef_shape[2]
    coefs = packed[count:].reshape(-1)[:size].reshape(coef_shape)
    return block, coefs


def widen(block, coefs, axis, dim, depth, cdepth):
    head = lax.slice_in_dim(block, 0, depth, axis=dim)
    tail = lax.slice_in_dim(block, block.shape[dim] - depth, block.shape[dim], axis=dim)
    chead = lax.slice_in_dim(coefs, 0, cdepth, axis=dim + 1)
    ctail = lax.slice_in_dim(coefs, coefs.shape[dim + 1] - cdepth, coefs.shape[dim + 1], axis=dim + 1)
    before = shifted(pack(tail, ctail), axis, 1)
    after = shifted(pack(head, chead), axis, -1)
    before_b, before_c = unpack(before, head.shape, chead.shape)
    after_b, after_c = unpack(after, head.shape, chead.shape)
    block = jnp.concatenate([before_b, block, after_b], axis=dim)
    coefs = jnp.concatenate([before_c, coefs, after_c], axis=dim + 1)
    return block, coefs


def inset(cells, by):
    if by == 0:
        return cells
    return cells[by:cells.shape[0] - by, by:cells.shape[1] - by]


def neighbors(cells, links):
    cx, cy, cx_up, cy_left = links
    total = cx[:, :, None] * cells[2:, 1:-1] + cx_up[:, :, None] * cells[:-2, 1:-1]
    return total + cy[:, :, None] * cells[1:-1, 2:] + cy_left[:, :, None] * cells[1:-1, :-2]


def local_inner(left, right):
    a = left.reshape(-1, left.shape[-1])
    b = right.reshape(-1, right.shape[-1])
    return jnp.einsum("cp,cq->pq", a, b, precision=highest, preferred_element_type=jnp.float32)


def fold(first, second, third):
    size = first.shape[0]
    row = lax.broadcasted_iota(jnp.int32, first.shape, 0)
    col = lax.broadcasted_iota(jnp.int32, first.shape, 1)
    upper = row <= col
    on_diag = jnp.where(row == col, third, jnp.float32(0.0))
    across = jnp.sum(on_diag, axis=0, keepdims=True)
    down = jnp.sum(on_diag, axis=1, keepdims=True)
    spill = jnp.where(row == col + 1, across, jnp.float32(0.0))
    spill = jnp.where((row == size - 1) & (col == 0), down, spill)
    return jnp.stack([jnp.where(upper, first, third), jnp.where(upper, second, spill)])


def unfold(one, two):
    size = one.shape[0]
    row = lax.broadcasted_iota(jnp.int32, one.shape, 0)
    col = lax.broadcasted_iota(jnp.int32, one.shape, 1)
    upper = row <= col
    first = jnp.where(upper, one, jnp.transpose(one))
    second = jnp.where(upper, two, jnp.transpose(two))
    low = jnp.where(row > col, one, jnp.float32(0.0))
    across = jnp.sum(jnp.where(row == col + 1, two, jnp.float32(0.0)), axis=0, keepdims=True)
    lane = lax.broadcasted_iota(jnp.int32, (1, size), 1)
    across = jnp.where(lane == size - 1, two[size - 1:size, 0:1], across)
    third = low + jnp.transpose(low) + jnp.where(row == col, across, jnp.float32(0.0))
    return first, second, third


def _factor_kernel(packed_ref, cand_ref, basis_ref, g_out_ref, c_out_ref, work_ref, inv_ref):
    size = packed_ref.shape[1]
    gram, g_block, c_block = unfold(packed_ref[0], packed_ref[1])
    work_ref[...] = gram
    rows = lax.broadcasted_iota(jnp.int32, (size, size), 0)
    cols = lax.broadcasted_iota(jnp.int32, (size, size), 1)
    inv_ref[...] = jnp.where(rows == cols, jnp.float32(1.0), jnp.float32(0.0))
    lane = lax.broadcasted_iota(jnp.int32, (1, size), 1)
    chunk = 8
    for lo in range(0, size, chunk):
        span = size - lo
        cols_s = lax.broadcasted_iota(jnp.int32, (span, size), 1)
        sub = lo + lax.broadcasted_iota(jnp.int32, (span, 1), 0)

        def step(j, carry, lo=lo, cols_s=cols_s, sub=sub):
            whole = work_ref[lo:, :]
            row = work_ref[pl.ds(j, 1), :]
            column = jnp.sum(jnp.where(cols_s == j, whole, jnp.float32(0.0)), axis=1, keepdims=True)
            pivot = jnp.sum(jnp.where(lane == j, row, jnp.float32(0.0)), axis=1, keepdims=True)
            scale = lax.rsqrt(pivot)
            right = jnp.where(lane >= j, row * scale, jnp.float32(0.0))
            left = jnp.where(sub >= j, column * scale, jnp.float32(0.0))
            head = inv_ref[pl.ds(j, 1), :] * scale
            work_ref[lo:, :] = whole - left * right
            inv_ref[lo:, :] = inv_ref[lo:, :] - left * head
            inv_ref[pl.ds(j, 1), :] = head
            return carry

        lax.fori_loop(lo, min(lo + chunk, size), step, 0)

    inverse = inv_ref[...]
    by_rows = (((1,), (1,)), ((), ()))
    basis_ref[...] = lax.dot_general(
        cand_ref[...], inverse, by_rows, precision=highest, preferred_element_type=jnp.float32
    )
    for block, out_ref in ((g_block, g_out_ref), (c_block, c_out_ref)):
        half = jnp.dot(inverse, block, precision=highest, preferred_element_type=jnp.float32)
        out_ref[...] = lax.dot_general(
            half, inverse, by_rows, precision=highest, preferred_element_type=jnp.float32
        )


def orthonormalize(packed, cand):
    size = packed.shape[1]
    return pl.pallas_call(
        _factor_kernel,
        out_shape=(
            jax.ShapeDtypeStruct(cand.shape, jnp.float32),
            jax.ShapeDtypeStruct((size, size), jnp.float32),
            jax.ShapeDtypeStruct((size, size), jnp.float32),
        ),
        scratch_shapes=[pltpu.VMEM((size, size), jnp.float32), pltpu.VMEM((size, size), jnp.float32)],
    )(packed, cand)


def per_device(prior_basis, cond_x, cond_y, capacitance, pad_mask, port_nodes):
    rows_dev, cols_dev = cond_x.shape
    width = port_nodes.shape[0]
    count_x = lax.axis_size("gx")
    count_y = lax.axis_size("gy")
    total_rows = rows_dev * count_x
    total_cols = cols_dev * count_y
    nodes = total_rows * total_cols
    bdepth = SWEEPS + 1
    depth = SWEEPS + 2

    coefs = jnp.stack([cond_x, cond_y, capacitance, pad_mask.astype(jnp.float32)])
    basis_e, coefs_e = widen(prior_basis, coefs, "gx", 0, bdepth, depth)
    basis_e, coefs_e = widen(basis_e, coefs_e, "gy", 1, bdepth, depth)

    row_start = lax.axis_index("gx") * rows_dev - depth
    col_start = lax.axis_index("gy") * cols_dev - depth
    shape_e = (rows_dev + 2 * depth, cols_dev + 2 * depth)
    grows = row_start + lax.broadcasted_iota(jnp.int32, shape_e, 0)
    gcols = col_start + lax.broadcasted_iota(jnp.int32, shape_e, 1)
    inside = (grows >= 0) & (grows < total_rows) & (gcols >= 0) & (gcols < total_cols)
    cx_e = jnp.where(grows < total_rows - 1, coefs_e[0], jnp.float32(0.0))
    cy_e = jnp.where(gcols < total_cols - 1, coefs_e[1], jnp.float32(0.0))
    cap_e = coefs_e[2]
    pad_e = coefs_e[3]

    def at(cells, margin):
        return inset(cells, depth - margin)

    def at_basis(margin):
        return inset(basis_e, bdepth - margin)

    top = depth - 1
    cx_t = at(cx_e, top)
    cy_t = at(cy_e, top)
    cx_up_t = cx_e[0:-2, 1:-1]
    cy_left_t = cy_e[1:-1, 0:-2]
    diag_g_t = cx_t + cx_up_t + cy_t + cy_left_t + supply_conductance * at(pad_e, top)
    diag_t = diag_g_t + shift_point * at(cap_e, top)
    diag_t = jnp.where(at(inside, top), diag_t, jnp.float32(1.0))

    def links_at(margin):
        cut = top - margin
        return tuple(inset(c, cut) for c in (cx_t, cy_t, cx_up_t, cy_left_t))

    first = SWEEPS + 1
    node_ids = at(grows, first) * total_cols + at(gcols, first)
    onehot = (node_ids[:, :, None] == port_nodes[None, None, :]) & at(inside, first)[:, :, None]
    rhs = at(cap_e, first)[:, :, None] * at_basis(first) + port_current * onehot.astype(jnp.float32)
    diag_f = inset(diag_t, top - first)[:, :, None]

    field = rhs / diag_f
    for sweep in range(SWEEPS):
        margin = first - 1 - sweep
        field = (inset(rhs, first - margin) + neighbors(field, links_at(margin))) / inset(diag_f, first - margin)

    tile_basis = at_basis(0)
    proj = allsum_quad(local_inner(tile_basis, inset(field, 1)), ("gy", "gx")) / nodes
    cand_1 = field - jnp.einsum("xyk,kp->xyp", at_basis(1), proj, precision=highest)
    cand = inset(cand_1, 1)
    diag_g = inset(diag_g_t, top)[:, :, None]
    g_image = diag_g * cand - neighbors(cand_1, links_at(0))
    c_image = at(cap_e, 0)[:, :, None] * cand
    images = local_inner(cand, jnp.concatenate([cand, g_image, c_image], axis=-1))
    gram, g_raw, c_raw = images[:, :width], images[:, width:2 * width], images[:, 2 * width:]
    packed = allsum_exchange(fold(gram, g_raw, c_raw), ("gx", "gy")) / nodes
    basis_flat, reduced_g, reduced_c = orthonormalize(packed, cand.reshape(-1, width))
    new_basis = basis_flat.reshape(cand.shape)
    return (new_basis, reduced_g, reduced_c)


def solution(mesh):
    placed = (P("gx", "gy", None), P("gx", "gy"), P("gx", "gy"), P("gx", "gy"), P("gx", "gy"), P())
    return jax.shard_map(
        per_device,
        mesh=mesh,
        in_specs=placed,
        out_specs=(P("gx", "gy", None), P(), P()),
        check_vma=False,
    )
```

```python
import jax
import jax.numpy as jnp
from jax import lax
from jax.experimental import pallas as pl
from jax.experimental.pallas import tpu as pltpu
from jax.sharding import PartitionSpec as P

SWEEPS = 4


shift_point = 0.5
supply_conductance = 4.0
port_current = 8.0
highest = lax.Precision.HIGHEST


def shifted(shard, axis, by):
    devices = lax.axis_size(axis)
    pairs = [(i, i + by) for i in range(devices) if 0 <= i + by < devices]
    return lax.ppermute(shard, axis, pairs)


def allsum(value, axes):
    for axis in axes:
        count = lax.axis_size(axis)
        if count & (count - 1):
            value = lax.psum(value, axis)
            continue
        step = 1
        while step < count:
            other = lax.ppermute(value, axis, [(i, i ^ step) for i in range(count)])
            value = value + other
            step *= 2
    return value


def allsum_exchange(value, axes):
    count = 1
    for axis in axes:
        count *= lax.axis_size(axis)
    flat = value.reshape(-1, value.shape[-1])
    if flat.shape[0] % count:
        return allsum(value, axes)
    parts = flat.reshape(count, -1, flat.shape[-1])
    got = lax.all_to_all(parts, axes, 0, 0, tiled=False)
    total = got[0]
    for k in range(1, count):
        total = total + got[k]
    spread = jnp.broadcast_to(total[None], (count,) + total.shape)
    back = lax.all_to_all(spread, axes, 0, 0, tiled=False)
    return back.reshape(value.shape)


def allsum_quad(value, axes):
    for axis in axes:
        count = lax.axis_size(axis)
        if count & (count - 1):
            value = lax.psum(value, axis)
            continue
        index = lax.axis_index(axis)
        step = 1
        while step < count:
            if step * 4 <= count:
                own = (index // step) % 4
                got = [value] + [
                    lax.ppermute(value, axis, [(i, i ^ (k * step)) for i in range(count)])
                    for k in (1, 2, 3)
                ]
                stack = jnp.stack(got)
                total = lax.dynamic_index_in_dim(stack, own, keepdims=False)
                for member in (1, 2, 3):
                    total = total + lax.dynamic_index_in_dim(stack, own ^ member, keepdims=False)
                value = total
                step *= 4
            else:
                other = lax.ppermute(value, axis, [(i, i ^ step) for i in range(count)])
                value = value + other
                step *= 2
    return value


def pack(block, coefs):
    width = block.shape[-1]
    flat = coefs.reshape(-1)
    spare = (-flat.shape[0]) % width
    flat = jnp.pad(flat, (0, spare))
    return jnp.concatenate([block.reshape(-1, width), flat.reshape(-1, width)], axis=0)


def unpack(packed, block_shape, coef_shape):
    count = block_shape[0] * block_shape[1]
    block = packed[:count].reshape(block_shape)
    size = coef_shape[0] * coef_shape[1] * coef_shape[2]
    coefs = packed[count:].reshape(-1)[:size].reshape(coef_shape)
    return block, coefs


def widen(block, coefs, axis, dim, depth, cdepth):
    head = lax.slice_in_dim(block, 0, depth, axis=dim)
    tail = lax.slice_in_dim(block, block.shape[dim] - depth, block.shape[dim], axis=dim)
    chead = lax.slice_in_dim(coefs, 0, cdepth, axis=dim + 1)
    ctail = lax.slice_in_dim(coefs, coefs.shape[dim + 1] - cdepth, coefs.shape[dim + 1], axis=dim + 1)
    before = shifted(pack(tail, ctail), axis, 1)
    after = shifted(pack(head, chead), axis, -1)
    before_b, before_c = unpack(before, head.shape, chead.shape)
    after_b, after_c = unpack(after, head.shape, chead.shape)
    block = jnp.concatenate([before_b, block, after_b], axis=dim)
    coefs = jnp.concatenate([before_c, coefs, after_c], axis=dim + 1)
    return block, coefs


def inset(cells, by):
    if by == 0:
        return cells
    return cells[by:cells.shape[0] - by, by:cells.shape[1] - by]


def neighbors(cells, links):
    cx, cy, cx_up, cy_left = links
    total = cx[:, :, None] * cells[2:, 1:-1] + cx_up[:, :, None] * cells[:-2, 1:-1]
    return total + cy[:, :, None] * cells[1:-1, 2:] + cy_left[:, :, None] * cells[1:-1, :-2]


def local_inner(left, right):
    a = left.reshape(-1, left.shape[-1])
    b = right.reshape(-1, right.shape[-1])
    return jnp.einsum("cp,cq->pq", a, b, precision=highest, preferred_element_type=jnp.float32)


def fold(first, second, third):
    size = first.shape[0]
    row = lax.broadcasted_iota(jnp.int32, first.shape, 0)
    col = lax.broadcasted_iota(jnp.int32, first.shape, 1)
    upper = row <= col
    on_diag = jnp.where(row == col, third, jnp.float32(0.0))
    across = jnp.sum(on_diag, axis=0, keepdims=True)
    down = jnp.sum(on_diag, axis=1, keepdims=True)
    spill = jnp.where(row == col + 1, across, jnp.float32(0.0))
    spill = jnp.where((row == size - 1) & (col == 0), down, spill)
    return jnp.stack([jnp.where(upper, first, third), jnp.where(upper, second, spill)])


def unfold(one, two):
    size = one.shape[0]
    row = lax.broadcasted_iota(jnp.int32, one.shape, 0)
    col = lax.broadcasted_iota(jnp.int32, one.shape, 1)
    upper = row <= col
    first = jnp.where(upper, one, jnp.transpose(one))
    second = jnp.where(upper, two, jnp.transpose(two))
    low = jnp.where(row > col, one, jnp.float32(0.0))
    across = jnp.sum(jnp.where(row == col + 1, two, jnp.float32(0.0)), axis=0, keepdims=True)
    lane = lax.broadcasted_iota(jnp.int32, (1, size), 1)
    across = jnp.where(lane == size - 1, two[size - 1:size, 0:1], across)
    third = low + jnp.transpose(low) + jnp.where(row == col, across, jnp.float32(0.0))
    return first, second, third


def _factor_kernel(packed_ref, cand_ref, basis_ref, g_out_ref, c_out_ref, work_ref, inv_ref):
    size = packed_ref.shape[1]
    gram, g_block, c_block = unfold(packed_ref[0], packed_ref[1])
    work_ref[...] = gram
    rows = lax.broadcasted_iota(jnp.int32, (size, size), 0)
    cols = lax.broadcasted_iota(jnp.int32, (size, size), 1)
    inv_ref[...] = jnp.where(rows == cols, jnp.float32(1.0), jnp.float32(0.0))
    lane = lax.broadcasted_iota(jnp.int32, (1, size), 1)
    chunk = 8
    for lo in range(0, size, chunk):
        span = size - lo
        cols_s = lax.broadcasted_iota(jnp.int32, (span, size), 1)
        sub = lo + lax.broadcasted_iota(jnp.int32, (span, 1), 0)

        def step(j, carry, lo=lo, cols_s=cols_s, sub=sub):
            whole = work_ref[lo:, :]
            row = work_ref[pl.ds(j, 1), :]
            column = jnp.sum(jnp.where(cols_s == j, whole, jnp.float32(0.0)), axis=1, keepdims=True)
            pivot = jnp.sum(jnp.where(lane == j, row, jnp.float32(0.0)), axis=1, keepdims=True)
            scale = lax.rsqrt(pivot)
            right = jnp.where(lane >= j, row * scale, jnp.float32(0.0))
            left = jnp.where(sub >= j, column * scale, jnp.float32(0.0))
            head = inv_ref[pl.ds(j, 1), :] * scale
            work_ref[lo:, :] = whole - left * right
            inv_ref[lo:, :] = inv_ref[lo:, :] - left * head
            inv_ref[pl.ds(j, 1), :] = head
            return carry

        lax.fori_loop(lo, min(lo + chunk, size), step, 0)

    inverse = inv_ref[...]
    by_rows = (((1,), (1,)), ((), ()))
    basis_ref[...] = lax.dot_general(
        cand_ref[...], inverse, by_rows, precision=highest, preferred_element_type=jnp.float32
    )
    for block, out_ref in ((g_block, g_out_ref), (c_block, c_out_ref)):
        half = jnp.dot(inverse, block, precision=highest, preferred_element_type=jnp.float32)
        out_ref[...] = lax.dot_general(
            half, inverse, by_rows, precision=highest, preferred_element_type=jnp.float32
        )


def orthonormalize(packed, cand):
    size = packed.shape[1]
    return pl.pallas_call(
        _factor_kernel,
        out_shape=(
            jax.ShapeDtypeStruct(cand.shape, jnp.float32),
            jax.ShapeDtypeStruct((size, size), jnp.float32),
            jax.ShapeDtypeStruct((size, size), jnp.float32),
        ),
        scratch_shapes=[pltpu.VMEM((size, size), jnp.float32), pltpu.VMEM((size, size), jnp.float32)],
    )(packed, cand)


def per_device(prior_basis, cond_x, cond_y, capacitance, pad_mask, port_nodes):
    rows_dev, cols_dev = cond_x.shape
    width = port_nodes.shape[0]
    count_x = lax.axis_size("gx")
    count_y = lax.axis_size("gy")
    total_rows = rows_dev * count_x
    total_cols = cols_dev * count_y
    nodes = total_rows * total_cols
    bdepth = SWEEPS + 1
    depth = SWEEPS + 2

    coefs = jnp.stack([cond_x, cond_y, capacitance, pad_mask.astype(jnp.float32)])
    basis_e, coefs_e = widen(prior_basis, coefs, "gx", 0, bdepth, depth)
    basis_e, coefs_e = widen(basis_e, coefs_e, "gy", 1, bdepth, depth)

    row_start = lax.axis_index("gx") * rows_dev - depth
    col_start = lax.axis_index("gy") * cols_dev - depth
    shape_e = (rows_dev + 2 * depth, cols_dev + 2 * depth)
    grows = row_start + lax.broadcasted_iota(jnp.int32, shape_e, 0)
    gcols = col_start + lax.broadcasted_iota(jnp.int32, shape_e, 1)
    inside = (grows >= 0) & (grows < total_rows) & (gcols >= 0) & (gcols < total_cols)
    cx_e = jnp.where(grows < total_rows - 1, coefs_e[0], jnp.float32(0.0))
    cy_e = jnp.where(gcols < total_cols - 1, coefs_e[1], jnp.float32(0.0))
    cap_e = coefs_e[2]
    pad_e = coefs_e[3]

    def at(cells, margin):
        return inset(cells, depth - margin)

    def at_basis(margin):
        return inset(basis_e, bdepth - margin)

    top = depth - 1
    cx_t = at(cx_e, top)
    cy_t = at(cy_e, top)
    cx_up_t = cx_e[0:-2, 1:-1]
    cy_left_t = cy_e[1:-1, 0:-2]
    diag_g_t = cx_t + cx_up_t + cy_t + cy_left_t + supply_conductance * at(pad_e, top)
    diag_t = diag_g_t + shift_point * at(cap_e, top)
    diag_t = jnp.where(at(inside, top), diag_t, jnp.float32(1.0))

    def links_at(margin):
        cut = top - margin
        return tuple(inset(c, cut) for c in (cx_t, cy_t, cx_up_t, cy_left_t))

    first = SWEEPS + 1
    node_ids = at(grows, first) * total_cols + at(gcols, first)
    onehot = (node_ids[:, :, None] == port_nodes[None, None, :]) & at(inside, first)[:, :, None]
    rhs = at(cap_e, first)[:, :, None] * at_basis(first) + port_current * onehot.astype(jnp.float32)
    diag_f = inset(diag_t, top - first)[:, :, None]

    field = rhs / diag_f
    for sweep in range(SWEEPS):
        margin = first - 1 - sweep
        field = (inset(rhs, first - margin) + neighbors(field, links_at(margin))) / inset(diag_f, first - margin)

    tile_basis = at_basis(0)
    proj = allsum_quad(local_inner(tile_basis, inset(field, 1)), ("gy", "gx")) / nodes
    cand_1 = field - jnp.einsum("xyk,kp->xyp", at_basis(1), proj, precision=highest)
    cand = inset(cand_1, 1)
    diag_g = inset(diag_g_t, top)[:, :, None]
    g_image = diag_g * cand - neighbors(cand_1, links_at(0))
    c_image = at(cap_e, 0)[:, :, None] * cand
    images = local_inner(cand, jnp.concatenate([cand, g_image, c_image], axis=-1)) / nodes
    gram, g_raw, c_raw = images[:, :width], images[:, width:2 * width], images[:, 2 * width:]
    packed = allsum_exchange(fold(gram, g_raw, c_raw), ("gx", "gy"))
    basis_flat, reduced_g, reduced_c = orthonormalize(packed, cand.reshape(-1, width))
    new_basis = basis_flat.reshape(cand.shape)
    return (new_basis, reduced_g, reduced_c)


def solution(mesh):
    placed = (P("gx", "gy", None), P("gx", "gy"), P("gx", "gy"), P("gx", "gy"), P("gx", "gy"), P())
    return jax.shard_map(
        per_device,
        mesh=mesh,
        in_specs=placed,
        out_specs=(P("gx", "gy", None), P(), P()),
        check_vma=False,
    )
```

```python
import jax
import jax.numpy as jnp
from jax import lax
from jax.experimental import pallas as pl
from jax.experimental.pallas import tpu as pltpu
from jax.sharding import PartitionSpec as P

SWEEPS = 4


shift_point = 0.5
supply_conductance = 4.0
port_current = 8.0
highest = lax.Precision.HIGHEST


def shifted(shard, axis, by):
    devices = lax.axis_size(axis)
    pairs = [(i, i + by) for i in range(devices) if 0 <= i + by < devices]
    return lax.ppermute(shard, axis, pairs)


def allsum(value, axes):
    for axis in axes:
        count = lax.axis_size(axis)
        if count & (count - 1):
            value = lax.psum(value, axis)
            continue
        step = 1
        while step < count:
            other = lax.ppermute(value, axis, [(i, i ^ step) for i in range(count)])
            value = value + other
            step *= 2
    return value


def allsum_exchange(value, axes):
    count = 1
    for axis in axes:
        count *= lax.axis_size(axis)
    flat = value.reshape(-1, value.shape[-1])
    if flat.shape[0] % count:
        return allsum(value, axes)
    parts = flat.reshape(count, -1, flat.shape[-1])
    got = lax.all_to_all(parts, axes, 0, 0, tiled=False)
    total = got[0]
    for k in range(1, count):
        total = total + got[k]
    spread = jnp.broadcast_to(total[None], (count,) + total.shape)
    back = lax.all_to_all(spread, axes, 0, 0, tiled=False)
    return back.reshape(value.shape)


def allsum_quad(value, axes):
    for axis in axes:
        count = lax.axis_size(axis)
        if count & (count - 1):
            value = lax.psum(value, axis)
            continue
        index = lax.axis_index(axis)
        step = 1
        while step < count:
            if step * 4 <= count:
                own = (index // step) % 4
                got = [value] + [
                    lax.ppermute(value, axis, [(i, i ^ (k * step)) for i in range(count)])
                    for k in (1, 2, 3)
                ]
                stack = jnp.stack(got)
                total = lax.dynamic_index_in_dim(stack, own, keepdims=False)
                for member in (1, 2, 3):
                    total = total + lax.dynamic_index_in_dim(stack, own ^ member, keepdims=False)
                value = total
                step *= 4
            else:
                other = lax.ppermute(value, axis, [(i, i ^ step) for i in range(count)])
                value = value + other
                step *= 2
    return value


def pack(block, coefs):
    width = block.shape[-1]
    flat = coefs.reshape(-1)
    spare = (-flat.shape[0]) % width
    flat = jnp.pad(flat, (0, spare))
    return jnp.concatenate([block.reshape(-1, width), flat.reshape(-1, width)], axis=0)


def unpack(packed, block_shape, coef_shape):
    count = block_shape[0] * block_shape[1]
    block = packed[:count].reshape(block_shape)
    size = coef_shape[0] * coef_shape[1] * coef_shape[2]
    coefs = packed[count:].reshape(-1)[:size].reshape(coef_shape)
    return block, coefs


def widen(block, coefs, axis, dim, depth, cdepth):
    head = lax.slice_in_dim(block, 0, depth, axis=dim)
    tail = lax.slice_in_dim(block, block.shape[dim] - depth, block.shape[dim], axis=dim)
    chead = lax.slice_in_dim(coefs, 0, cdepth, axis=dim + 1)
    ctail = lax.slice_in_dim(coefs, coefs.shape[dim + 1] - cdepth, coefs.shape[dim + 1], axis=dim + 1)
    before = shifted(pack(tail, ctail), axis, 1)
    after = shifted(pack(head, chead), axis, -1)
    before_b, before_c = unpack(before, head.shape, chead.shape)
    after_b, after_c = unpack(after, head.shape, chead.shape)
    block = jnp.concatenate([before_b, block, after_b], axis=dim)
    coefs = jnp.concatenate([before_c, coefs, after_c], axis=dim + 1)
    return block, coefs


def inset(cells, by):
    if by == 0:
        return cells
    return cells[by:cells.shape[0] - by, by:cells.shape[1] - by]


def neighbors(cells, links):
    cx, cy, cx_up, cy_left = links
    total = cx[:, :, None] * cells[2:, 1:-1] + cx_up[:, :, None] * cells[:-2, 1:-1]
    return total + cy[:, :, None] * cells[1:-1, 2:] + cy_left[:, :, None] * cells[1:-1, :-2]


def local_inner(left, right):
    a = left.reshape(-1, left.shape[-1])
    b = right.reshape(-1, right.shape[-1])
    return jnp.einsum("cp,cq->pq", a, b, precision=highest, preferred_element_type=jnp.float32)


def fold(first, second, third):
    size = first.shape[0]
    row = lax.broadcasted_iota(jnp.int32, first.shape, 0)
    col = lax.broadcasted_iota(jnp.int32, first.shape, 1)
    upper = row <= col
    on_diag = jnp.where(row == col, third, jnp.float32(0.0))
    across = jnp.sum(on_diag, axis=0, keepdims=True)
    down = jnp.sum(on_diag, axis=1, keepdims=True)
    spill = jnp.where(row == col + 1, across, jnp.float32(0.0))
    spill = jnp.where((row == size - 1) & (col == 0), down, spill)
    return jnp.stack([jnp.where(upper, first, third), jnp.where(upper, second, spill)])


def unfold(one, two):
    size = one.shape[0]
    row = lax.broadcasted_iota(jnp.int32, one.shape, 0)
    col = lax.broadcasted_iota(jnp.int32, one.shape, 1)
    upper = row <= col
    first = jnp.where(upper, one, jnp.transpose(one))
    second = jnp.where(upper, two, jnp.transpose(two))
    low = jnp.where(row > col, one, jnp.float32(0.0))
    across = jnp.sum(jnp.where(row == col + 1, two, jnp.float32(0.0)), axis=0, keepdims=True)
    lane = lax.broadcasted_iota(jnp.int32, (1, size), 1)
    across = jnp.where(lane == size - 1, two[size - 1:size, 0:1], across)
    third = low + jnp.transpose(low) + jnp.where(row == col, across, jnp.float32(0.0))
    return first, second, third


def _factor_kernel(packed_ref, cand_ref, basis_ref, g_out_ref, c_out_ref, work_ref, inv_ref):
    size = packed_ref.shape[1]
    gram, g_block, c_block = unfold(packed_ref[0], packed_ref[1])
    work_ref[...] = gram
    rows = lax.broadcasted_iota(jnp.int32, (size, size), 0)
    cols = lax.broadcasted_iota(jnp.int32, (size, size), 1)
    inv_ref[...] = jnp.where(rows == cols, jnp.float32(1.0), jnp.float32(0.0))
    lane = lax.broadcasted_iota(jnp.int32, (1, size), 1)
    chunk = 8
    for lo in range(0, size, chunk):
        span = size - lo
        cols_s = lax.broadcasted_iota(jnp.int32, (span, size), 1)
        sub = lo + lax.broadcasted_iota(jnp.int32, (span, 1), 0)

        def step(j, carry, lo=lo, cols_s=cols_s, sub=sub):
            whole = work_ref[lo:, :]
            row = work_ref[pl.ds(j, 1), :]
            column = jnp.sum(jnp.where(cols_s == j, whole, jnp.float32(0.0)), axis=1, keepdims=True)
            pivot = jnp.sum(jnp.where(lane == j, row, jnp.float32(0.0)), axis=1, keepdims=True)
            scale = lax.rsqrt(pivot)
            right = jnp.where(lane >= j, row * scale, jnp.float32(0.0))
            left = jnp.where(sub >= j, column * scale, jnp.float32(0.0))
            head = inv_ref[pl.ds(j, 1), :] * scale
            work_ref[lo:, :] = whole - left * right
            inv_ref[lo:, :] = inv_ref[lo:, :] - left * head
            inv_ref[pl.ds(j, 1), :] = head
            return carry

        lax.fori_loop(lo, min(lo + chunk, size), step, 0)

    inverse = inv_ref[...]
    by_rows = (((1,), (1,)), ((), ()))
    basis_ref[...] = lax.dot_general(
        cand_ref[...], inverse, by_rows, precision=highest, preferred_element_type=jnp.float32
    )
    for block, out_ref in ((g_block, g_out_ref), (c_block, c_out_ref)):
        half = jnp.dot(inverse, block, precision=highest, preferred_element_type=jnp.float32)
        out_ref[...] = lax.dot_general(
            half, inverse, by_rows, precision=highest, preferred_element_type=jnp.float32
        )


def orthonormalize(packed, cand):
    size = packed.shape[1]
    return pl.pallas_call(
        _factor_kernel,
        out_shape=(
            jax.ShapeDtypeStruct(cand.shape, jnp.float32),
            jax.ShapeDtypeStruct((size, size), jnp.float32),
            jax.ShapeDtypeStruct((size, size), jnp.float32),
        ),
        scratch_shapes=[pltpu.VMEM((size, size), jnp.float32), pltpu.VMEM((size, size), jnp.float32)],
    )(packed, cand)


def per_device(prior_basis, cond_x, cond_y, capacitance, pad_mask, port_nodes):
    rows_dev, cols_dev = cond_x.shape
    width = port_nodes.shape[0]
    count_x = lax.axis_size("gx")
    count_y = lax.axis_size("gy")
    total_rows = rows_dev * count_x
    total_cols = cols_dev * count_y
    nodes = total_rows * total_cols
    bdepth = SWEEPS + 1
    depth = SWEEPS + 2

    coefs = jnp.stack([cond_x, cond_y, capacitance, pad_mask.astype(jnp.float32)])
    basis_e, coefs_e = widen(prior_basis, coefs, "gx", 0, bdepth, depth)
    basis_e, coefs_e = widen(basis_e, coefs_e, "gy", 1, bdepth, depth)

    row_start = lax.axis_index("gx") * rows_dev - depth
    col_start = lax.axis_index("gy") * cols_dev - depth
    shape_e = (rows_dev + 2 * depth, cols_dev + 2 * depth)
    grows = row_start + lax.broadcasted_iota(jnp.int32, shape_e, 0)
    gcols = col_start + lax.broadcasted_iota(jnp.int32, shape_e, 1)
    inside = (grows >= 0) & (grows < total_rows) & (gcols >= 0) & (gcols < total_cols)
    cx_e = jnp.where(grows < total_rows - 1, coefs_e[0], jnp.float32(0.0))
    cy_e = jnp.where(gcols < total_cols - 1, coefs_e[1], jnp.float32(0.0))
    cap_e = coefs_e[2]
    pad_e = coefs_e[3]

    def at(cells, margin):
        return inset(cells, depth - margin)

    def at_basis(margin):
        return inset(basis_e, bdepth - margin)

    top = depth - 1
    cx_t = at(cx_e, top)
    cy_t = at(cy_e, top)
    cx_up_t = cx_e[0:-2, 1:-1]
    cy_left_t = cy_e[1:-1, 0:-2]
    diag_g_t = cx_t + cx_up_t + cy_t + cy_left_t + supply_conductance * at(pad_e, top)
    diag_t = diag_g_t + shift_point * at(cap_e, top)
    diag_t = jnp.where(at(inside, top), diag_t, jnp.float32(1.0))

    def links_at(margin):
        cut = top - margin
        return tuple(inset(c, cut) for c in (cx_t, cy_t, cx_up_t, cy_left_t))

    first = SWEEPS + 1
    node_ids = at(grows, first) * total_cols + at(gcols, first)
    onehot = (node_ids[:, :, None] == port_nodes[None, None, :]) & at(inside, first)[:, :, None]
    rhs = at(cap_e, first)[:, :, None] * at_basis(first) + port_current * onehot.astype(jnp.float32)
    diag_f = inset(diag_t, top - first)[:, :, None]

    cx_f, cy_f, cx_up_f, cy_left_f = links_at(first - 1)
    start = cx_f[:, :, None] * (rhs[2:, 1:-1] / diag_f[2:, 1:-1])
    start = start + cx_up_f[:, :, None] * (rhs[:-2, 1:-1] / diag_f[:-2, 1:-1])
    start = start + cy_f[:, :, None] * (rhs[1:-1, 2:] / diag_f[1:-1, 2:])
    start = start + cy_left_f[:, :, None] * (rhs[1:-1, :-2] / diag_f[1:-1, :-2])
    field = (inset(rhs, 1) + start) / inset(diag_f, 1)
    for sweep in range(1, SWEEPS):
        margin = first - 1 - sweep
        field = (inset(rhs, first - margin) + neighbors(field, links_at(margin))) / inset(diag_f, first - margin)

    tile_basis = at_basis(0)
    proj = allsum_quad(local_inner(tile_basis, inset(field, 1)), ("gy", "gx")) / nodes
    cand_1 = field - jnp.einsum("xyk,kp->xyp", at_basis(1), proj, precision=highest)
    cand = inset(cand_1, 1)
    diag_g = inset(diag_g_t, top)[:, :, None]
    g_image = diag_g * cand - neighbors(cand_1, links_at(0))
    c_image = at(cap_e, 0)[:, :, None] * cand
    images = local_inner(cand, jnp.concatenate([cand, g_image, c_image], axis=-1))
    gram, g_raw, c_raw = images[:, :width], images[:, width:2 * width], images[:, 2 * width:]
    packed = allsum_exchange(fold(gram, g_raw, c_raw), ("gx", "gy")) / nodes
    basis_flat, reduced_g, reduced_c = orthonormalize(packed, cand.reshape(-1, width))
    new_basis = basis_flat.reshape(cand.shape)
    return (new_basis, reduced_g, reduced_c)


def solution(mesh):
    placed = (P("gx", "gy", None), P("gx", "gy"), P("gx", "gy"), P("gx", "gy"), P("gx", "gy"), P())
    return jax.shard_map(
        per_device,
        mesh=mesh,
        in_specs=placed,
        out_specs=(P("gx", "gy", None), P(), P()),
        check_vma=False,
    )
```

```python
import jax
import jax.numpy as jnp
from jax import lax
from jax.experimental import pallas as pl
from jax.experimental.pallas import tpu as pltpu
from jax.sharding import PartitionSpec as P

SWEEPS = 4


shift_point = 0.5
supply_conductance = 4.0
port_current = 8.0
highest = lax.Precision.HIGHEST


def shifted(shard, axis, by):
    devices = lax.axis_size(axis)
    pairs = [(i, i + by) for i in range(devices) if 0 <= i + by < devices]
    return lax.ppermute(shard, axis, pairs)


def allsum(value, axes):
    for axis in axes:
        count = lax.axis_size(axis)
        if count & (count - 1):
            value = lax.psum(value, axis)
            continue
        step = 1
        while step < count:
            other = lax.ppermute(value, axis, [(i, i ^ step) for i in range(count)])
            value = value + other
            step *= 2
    return value


def allsum_exchange(value, axes):
    count = 1
    for axis in axes:
        count *= lax.axis_size(axis)
    flat = value.reshape(-1, value.shape[-1])
    if flat.shape[0] % count:
        return allsum(value, axes)
    parts = flat.reshape(count, -1, flat.shape[-1])
    got = lax.all_to_all(parts, axes, 0, 0, tiled=False)
    total = got[0]
    for k in range(1, count):
        total = total + got[k]
    spread = jnp.broadcast_to(total[None], (count,) + total.shape)
    back = lax.all_to_all(spread, axes, 0, 0, tiled=False)
    return back.reshape(value.shape)


def allsum_quad(value, axes):
    for axis in axes:
        count = lax.axis_size(axis)
        if count & (count - 1):
            value = lax.psum(value, axis)
            continue
        index = lax.axis_index(axis)
        step = 1
        while step < count:
            if step * 4 <= count:
                own = (index // step) % 4
                got = [value] + [
                    lax.ppermute(value, axis, [(i, i ^ (k * step)) for i in range(count)])
                    for k in (1, 2, 3)
                ]
                stack = jnp.stack(got)
                total = lax.dynamic_index_in_dim(stack, own, keepdims=False)
                for member in (1, 2, 3):
                    total = total + lax.dynamic_index_in_dim(stack, own ^ member, keepdims=False)
                value = total
                step *= 4
            else:
                other = lax.ppermute(value, axis, [(i, i ^ step) for i in range(count)])
                value = value + other
                step *= 2
    return value


def pack(block, coefs):
    width = block.shape[-1]
    flat = coefs.reshape(-1)
    spare = (-flat.shape[0]) % width
    flat = jnp.pad(flat, (0, spare))
    return jnp.concatenate([block.reshape(-1, width), flat.reshape(-1, width)], axis=0)


def unpack(packed, block_shape, coef_shape):
    count = block_shape[0] * block_shape[1]
    block = packed[:count].reshape(block_shape)
    size = coef_shape[0] * coef_shape[1] * coef_shape[2]
    coefs = packed[count:].reshape(-1)[:size].reshape(coef_shape)
    return block, coefs


def widen(block, coefs, axis, dim, depth, cdepth):
    head = lax.slice_in_dim(block, 0, depth, axis=dim)
    tail = lax.slice_in_dim(block, block.shape[dim] - depth, block.shape[dim], axis=dim)
    chead = lax.slice_in_dim(coefs, 0, cdepth, axis=dim + 1)
    ctail = lax.slice_in_dim(coefs, coefs.shape[dim + 1] - cdepth, coefs.shape[dim + 1], axis=dim + 1)
    before = shifted(pack(tail, ctail), axis, 1)
    after = shifted(pack(head, chead), axis, -1)
    before_b, before_c = unpack(before, head.shape, chead.shape)
    after_b, after_c = unpack(after, head.shape, chead.shape)
    block = jnp.concatenate([before_b, block, after_b], axis=dim)
    coefs = jnp.concatenate([before_c, coefs, after_c], axis=dim + 1)
    return block, coefs


def inset(cells, by):
    if by == 0:
        return cells
    return cells[by:cells.shape[0] - by, by:cells.shape[1] - by]


def neighbors(cells, links):
    cx, cy, cx_up, cy_left = links
    total = cx[:, :, None] * cells[2:, 1:-1] + cx_up[:, :, None] * cells[:-2, 1:-1]
    return total + cy[:, :, None] * cells[1:-1, 2:] + cy_left[:, :, None] * cells[1:-1, :-2]


def local_inner(left, right):
    a = left.reshape(-1, left.shape[-1])
    b = right.reshape(-1, right.shape[-1])
    return jnp.einsum("cp,cq->pq", a, b, precision=highest, preferred_element_type=jnp.float32)


def fold(first, second, third):
    size = first.shape[0]
    row = lax.broadcasted_iota(jnp.int32, first.shape, 0)
    col = lax.broadcasted_iota(jnp.int32, first.shape, 1)
    upper = row <= col
    on_diag = jnp.where(row == col, third, jnp.float32(0.0))
    across = jnp.sum(on_diag, axis=0, keepdims=True)
    down = jnp.sum(on_diag, axis=1, keepdims=True)
    spill = jnp.where(row == col + 1, across, jnp.float32(0.0))
    spill = jnp.where((row == size - 1) & (col == 0), down, spill)
    return jnp.stack([jnp.where(upper, first, third), jnp.where(upper, second, spill)])


def unfold(one, two):
    size = one.shape[0]
    row = lax.broadcasted_iota(jnp.int32, one.shape, 0)
    col = lax.broadcasted_iota(jnp.int32, one.shape, 1)
    upper = row <= col
    first = jnp.where(upper, one, jnp.transpose(one))
    second = jnp.where(upper, two, jnp.transpose(two))
    low = jnp.where(row > col, one, jnp.float32(0.0))
    across = jnp.sum(jnp.where(row == col + 1, two, jnp.float32(0.0)), axis=0, keepdims=True)
    lane = lax.broadcasted_iota(jnp.int32, (1, size), 1)
    across = jnp.where(lane == size - 1, two[size - 1:size, 0:1], across)
    third = low + jnp.transpose(low) + jnp.where(row == col, across, jnp.float32(0.0))
    return first, second, third


def _factor_kernel(packed_ref, cand_ref, basis_ref, g_out_ref, c_out_ref, work_ref, inv_ref):
    size = packed_ref.shape[1]
    gram, g_block, c_block = unfold(packed_ref[0], packed_ref[1])
    work_ref[...] = gram
    rows = lax.broadcasted_iota(jnp.int32, (size, size), 0)
    cols = lax.broadcasted_iota(jnp.int32, (size, size), 1)
    inv_ref[...] = jnp.where(rows == cols, jnp.float32(1.0), jnp.float32(0.0))
    lane = lax.broadcasted_iota(jnp.int32, (1, size), 1)
    chunk = 8
    for lo in range(0, size, chunk):
        span = size - lo
        cols_s = lax.broadcasted_iota(jnp.int32, (span, size), 1)
        sub = lo + lax.broadcasted_iota(jnp.int32, (span, 1), 0)

        def step(j, carry, lo=lo, cols_s=cols_s, sub=sub):
            whole = work_ref[lo:, :]
            row = work_ref[pl.ds(j, 1), :]
            column = jnp.sum(jnp.where(cols_s == j, whole, jnp.float32(0.0)), axis=1, keepdims=True)
            pivot = jnp.sum(jnp.where(lane == j, row, jnp.float32(0.0)), axis=1, keepdims=True)
            scale = lax.rsqrt(pivot)
            right = jnp.where(lane >= j, row * scale, jnp.float32(0.0))
            left = jnp.where(sub >= j, column * scale, jnp.float32(0.0))
            head = inv_ref[pl.ds(j, 1), :] * scale
            work_ref[lo:, :] = whole - left * right
            inv_ref[lo:, :] = inv_ref[lo:, :] - left * head
            inv_ref[pl.ds(j, 1), :] = head
            return carry

        lax.fori_loop(lo, min(lo + chunk, size), step, 0)

    inverse = inv_ref[...]
    by_rows = (((1,), (1,)), ((), ()))
    basis_ref[...] = lax.dot_general(
        cand_ref[...], inverse, by_rows, precision=highest, preferred_element_type=jnp.float32
    )
    for block, out_ref in ((g_block, g_out_ref), (c_block, c_out_ref)):
        half = jnp.dot(inverse, block, precision=highest, preferred_element_type=jnp.float32)
        out_ref[...] = lax.dot_general(
            half, inverse, by_rows, precision=highest, preferred_element_type=jnp.float32
        )


def orthonormalize(packed, cand):
    size = packed.shape[1]
    return pl.pallas_call(
        _factor_kernel,
        out_shape=(
            jax.ShapeDtypeStruct(cand.shape, jnp.float32),
            jax.ShapeDtypeStruct((size, size), jnp.float32),
            jax.ShapeDtypeStruct((size, size), jnp.float32),
        ),
        scratch_shapes=[pltpu.VMEM((size, size), jnp.float32), pltpu.VMEM((size, size), jnp.float32)],
    )(packed, cand)


def per_device(prior_basis, cond_x, cond_y, capacitance, pad_mask, port_nodes):
    rows_dev, cols_dev = cond_x.shape
    width = port_nodes.shape[0]
    count_x = lax.axis_size("gx")
    count_y = lax.axis_size("gy")
    total_rows = rows_dev * count_x
    total_cols = cols_dev * count_y
    nodes = total_rows * total_cols
    bdepth = SWEEPS + 1
    depth = SWEEPS + 2

    coefs = jnp.stack([cond_x, cond_y, capacitance, pad_mask.astype(jnp.float32)])
    basis_e, coefs_e = widen(prior_basis, coefs, "gx", 0, bdepth, depth)
    basis_e, coefs_e = widen(basis_e, coefs_e, "gy", 1, bdepth, depth)

    row_start = lax.axis_index("gx") * rows_dev - depth
    col_start = lax.axis_index("gy") * cols_dev - depth
    shape_e = (rows_dev + 2 * depth, cols_dev + 2 * depth)
    grows = row_start + lax.broadcasted_iota(jnp.int32, shape_e, 0)
    gcols = col_start + lax.broadcasted_iota(jnp.int32, shape_e, 1)
    inside = (grows >= 0) & (grows < total_rows) & (gcols >= 0) & (gcols < total_cols)
    cx_e = jnp.where(grows < total_rows - 1, coefs_e[0], jnp.float32(0.0))
    cy_e = jnp.where(gcols < total_cols - 1, coefs_e[1], jnp.float32(0.0))
    cap_e = coefs_e[2]
    pad_e = coefs_e[3]

    def at(cells, margin):
        return inset(cells, depth - margin)

    def at_basis(margin):
        return inset(basis_e, bdepth - margin)

    top = depth - 1
    cx_t = at(cx_e, top)
    cy_t = at(cy_e, top)
    cx_up_t = cx_e[0:-2, 1:-1]
    cy_left_t = cy_e[1:-1, 0:-2]
    diag_g_t = cx_t + cx_up_t + cy_t + cy_left_t + supply_conductance * at(pad_e, top)
    diag_t = diag_g_t + shift_point * at(cap_e, top)
    diag_t = jnp.where(at(inside, top), diag_t, jnp.float32(1.0))

    def links_at(margin):
        cut = top - margin
        return tuple(inset(c, cut) for c in (cx_t, cy_t, cx_up_t, cy_left_t))

    first = SWEEPS + 1
    node_ids = at(grows, first) * total_cols + at(gcols, first)
    onehot = (node_ids[:, :, None] == port_nodes[None, None, :]) & at(inside, first)[:, :, None]
    rhs = at(cap_e, first)[:, :, None] * at_basis(first) + port_current * onehot.astype(jnp.float32)
    diag_f = inset(diag_t, top - first)[:, :, None]

    field = rhs / diag_f
    for sweep in range(SWEEPS):
        margin = first - 1 - sweep
        field = (inset(rhs, first - margin) + neighbors(field, links_at(margin))) / inset(diag_f, first - margin)

    tile_basis = at_basis(0)
    proj = allsum_exchange(allsum_quad(local_inner(tile_basis, inset(field, 1)), ("gy",)), ("gx",)) / nodes
    cand_1 = field - jnp.einsum("xyk,kp->xyp", at_basis(1), proj, precision=highest)
    cand = inset(cand_1, 1)
    diag_g = inset(diag_g_t, top)[:, :, None]
    g_image = diag_g * cand - neighbors(cand_1, links_at(0))
    c_image = at(cap_e, 0)[:, :, None] * cand
    images = local_inner(cand, jnp.concatenate([cand, g_image, c_image], axis=-1))
    gram, g_raw, c_raw = images[:, :width], images[:, width:2 * width], images[:, 2 * width:]
    packed = allsum_exchange(fold(gram, g_raw, c_raw), ("gx", "gy")) / nodes
    basis_flat, reduced_g, reduced_c = orthonormalize(packed, cand.reshape(-1, width))
    new_basis = basis_flat.reshape(cand.shape)
    return (new_basis, reduced_g, reduced_c)


def solution(mesh):
    placed = (P("gx", "gy", None), P("gx", "gy"), P("gx", "gy"), P("gx", "gy"), P("gx", "gy"), P())
    return jax.shard_map(
        per_device,
        mesh=mesh,
        in_specs=placed,
        out_specs=(P("gx", "gy", None), P(), P()),
        check_vma=False,
    )
```

```python
import jax
import jax.numpy as jnp
from jax import lax
from jax.experimental import pallas as pl
from jax.experimental.pallas import tpu as pltpu
from jax.sharding import PartitionSpec as P

SWEEPS = 4


shift_point = 0.5
supply_conductance = 4.0
port_current = 8.0
highest = lax.Precision.HIGHEST


def shifted(shard, axis, by):
    devices = lax.axis_size(axis)
    pairs = [(i, i + by) for i in range(devices) if 0 <= i + by < devices]
    return lax.ppermute(shard, axis, pairs)


def allsum(value, axes):
    for axis in axes:
        count = lax.axis_size(axis)
        if count & (count - 1):
            value = lax.psum(value, axis)
            continue
        step = 1
        while step < count:
            other = lax.ppermute(value, axis, [(i, i ^ step) for i in range(count)])
            value = value + other
            step *= 2
    return value


def allsum_exchange(value, axes):
    count = 1
    for axis in axes:
        count *= lax.axis_size(axis)
    flat = value.reshape(-1, value.shape[-1])
    if flat.shape[0] % count:
        return allsum(value, axes)
    parts = flat.reshape(count, -1, flat.shape[-1])
    got = lax.all_to_all(parts, axes, 0, 0, tiled=False)
    total = got[0]
    for k in range(1, count):
        total = total + got[k]
    spread = jnp.broadcast_to(total[None], (count,) + total.shape)
    back = lax.all_to_all(spread, axes, 0, 0, tiled=False)
    return back.reshape(value.shape)


def allsum_quad(value, axes):
    for axis in axes:
        count = lax.axis_size(axis)
        if count & (count - 1):
            value = lax.psum(value, axis)
            continue
        index = lax.axis_index(axis)
        step = 1
        while step < count:
            if step * 4 <= count:
                own = (index // step) % 4
                got = [value] + [
                    lax.ppermute(value, axis, [(i, i ^ (k * step)) for i in range(count)])
                    for k in (1, 2, 3)
                ]
                stack = jnp.stack(got)
                total = lax.dynamic_index_in_dim(stack, own, keepdims=False)
                for member in (1, 2, 3):
                    total = total + lax.dynamic_index_in_dim(stack, own ^ member, keepdims=False)
                value = total
                step *= 4
            else:
                other = lax.ppermute(value, axis, [(i, i ^ step) for i in range(count)])
                value = value + other
                step *= 2
    return value


def pack(block, coefs):
    width = block.shape[-1]
    flat = coefs.reshape(-1)
    spare = (-flat.shape[0]) % width
    flat = jnp.pad(flat, (0, spare))
    return jnp.concatenate([block.reshape(-1, width), flat.reshape(-1, width)], axis=0)


def unpack(packed, block_shape, coef_shape):
    count = block_shape[0] * block_shape[1]
    block = packed[:count].reshape(block_shape)
    size = coef_shape[0] * coef_shape[1] * coef_shape[2]
    coefs = packed[count:].reshape(-1)[:size].reshape(coef_shape)
    return block, coefs


def widen(block, coefs, axis, dim, depth, cdepth):
    head = lax.slice_in_dim(block, 0, depth, axis=dim)
    tail = lax.slice_in_dim(block, block.shape[dim] - depth, block.shape[dim], axis=dim)
    chead = lax.slice_in_dim(coefs, 0, cdepth, axis=dim + 1)
    ctail = lax.slice_in_dim(coefs, coefs.shape[dim + 1] - cdepth, coefs.shape[dim + 1], axis=dim + 1)
    before = shifted(pack(tail, ctail), axis, 1)
    after = shifted(pack(head, chead), axis, -1)
    before_b, before_c = unpack(before, head.shape, chead.shape)
    after_b, after_c = unpack(after, head.shape, chead.shape)
    block = jnp.concatenate([before_b, block, after_b], axis=dim)
    coefs = jnp.concatenate([before_c, coefs, after_c], axis=dim + 1)
    return block, coefs


def inset(cells, by):
    if by == 0:
        return cells
    return cells[by:cells.shape[0] - by, by:cells.shape[1] - by]


def neighbors(cells, links):
    cx, cy, cx_up, cy_left = links
    total = cx[:, :, None] * cells[2:, 1:-1] + cx_up[:, :, None] * cells[:-2, 1:-1]
    return total + cy[:, :, None] * cells[1:-1, 2:] + cy_left[:, :, None] * cells[1:-1, :-2]


def local_inner(left, right):
    a = left.reshape(-1, left.shape[-1])
    b = right.reshape(-1, right.shape[-1])
    return jnp.einsum("cp,cq->pq", a, b, precision=highest, preferred_element_type=jnp.float32)


def fold(first, second, third):
    size = first.shape[0]
    row = lax.broadcasted_iota(jnp.int32, first.shape, 0)
    col = lax.broadcasted_iota(jnp.int32, first.shape, 1)
    upper = row <= col
    on_diag = jnp.where(row == col, third, jnp.float32(0.0))
    across = jnp.sum(on_diag, axis=0, keepdims=True)
    down = jnp.sum(on_diag, axis=1, keepdims=True)
    spill = jnp.where(row == col + 1, across, jnp.float32(0.0))
    spill = jnp.where((row == size - 1) & (col == 0), down, spill)
    return jnp.stack([jnp.where(upper, first, third), jnp.where(upper, second, spill)])


def unfold(one, two):
    size = one.shape[0]
    row = lax.broadcasted_iota(jnp.int32, one.shape, 0)
    col = lax.broadcasted_iota(jnp.int32, one.shape, 1)
    upper = row <= col
    first = jnp.where(upper, one, jnp.transpose(one))
    second = jnp.where(upper, two, jnp.transpose(two))
    low = jnp.where(row > col, one, jnp.float32(0.0))
    across = jnp.sum(jnp.where(row == col + 1, two, jnp.float32(0.0)), axis=0, keepdims=True)
    lane = lax.broadcasted_iota(jnp.int32, (1, size), 1)
    across = jnp.where(lane == size - 1, two[size - 1:size, 0:1], across)
    third = low + jnp.transpose(low) + jnp.where(row == col, across, jnp.float32(0.0))
    return first, second, third


def _factor_kernel(packed_ref, cand_ref, basis_ref, g_out_ref, c_out_ref, work_ref, inv_ref):
    size = packed_ref.shape[1]
    gram, g_block, c_block = unfold(packed_ref[0], packed_ref[1])
    work_ref[...] = gram
    rows = lax.broadcasted_iota(jnp.int32, (size, size), 0)
    cols = lax.broadcasted_iota(jnp.int32, (size, size), 1)
    inv_ref[...] = jnp.where(rows == cols, jnp.float32(1.0), jnp.float32(0.0))
    lane = lax.broadcasted_iota(jnp.int32, (1, size), 1)
    chunk = 4
    for lo in range(0, size, chunk):
        span = size - lo
        cols_s = lax.broadcasted_iota(jnp.int32, (span, size), 1)
        sub = lo + lax.broadcasted_iota(jnp.int32, (span, 1), 0)

        def step(j, carry, lo=lo, cols_s=cols_s, sub=sub):
            whole = work_ref[lo:, :]
            row = work_ref[pl.ds(j, 1), :]
            column = jnp.sum(jnp.where(cols_s == j, whole, jnp.float32(0.0)), axis=1, keepdims=True)
            pivot = jnp.sum(jnp.where(lane == j, row, jnp.float32(0.0)), axis=1, keepdims=True)
            scale = lax.rsqrt(pivot)
            right = jnp.where(lane >= j, row * scale, jnp.float32(0.0))
            left = jnp.where(sub >= j, column * scale, jnp.float32(0.0))
            head = inv_ref[pl.ds(j, 1), :] * scale
            work_ref[lo:, :] = whole - left * right
            inv_ref[lo:, :] = inv_ref[lo:, :] - left * head
            inv_ref[pl.ds(j, 1), :] = head
            return carry

        lax.fori_loop(lo, min(lo + chunk, size), step, 0)

    inverse = inv_ref[...]
    by_rows = (((1,), (1,)), ((), ()))
    basis_ref[...] = lax.dot_general(
        cand_ref[...], inverse, by_rows, precision=highest, preferred_element_type=jnp.float32
    )
    for block, out_ref in ((g_block, g_out_ref), (c_block, c_out_ref)):
        half = jnp.dot(inverse, block, precision=highest, preferred_element_type=jnp.float32)
        out_ref[...] = lax.dot_general(
            half, inverse, by_rows, precision=highest, preferred_element_type=jnp.float32
        )


def orthonormalize(packed, cand):
    size = packed.shape[1]
    return pl.pallas_call(
        _factor_kernel,
        out_shape=(
            jax.ShapeDtypeStruct(cand.shape, jnp.float32),
            jax.ShapeDtypeStruct((size, size), jnp.float32),
            jax.ShapeDtypeStruct((size, size), jnp.float32),
        ),
        scratch_shapes=[pltpu.VMEM((size, size), jnp.float32), pltpu.VMEM((size, size), jnp.float32)],
    )(packed, cand)


def per_device(prior_basis, cond_x, cond_y, capacitance, pad_mask, port_nodes):
    rows_dev, cols_dev = cond_x.shape
    width = port_nodes.shape[0]
    count_x = lax.axis_size("gx")
    count_y = lax.axis_size("gy")
    total_rows = rows_dev * count_x
    total_cols = cols_dev * count_y
    nodes = total_rows * total_cols
    bdepth = SWEEPS + 1
    depth = SWEEPS + 2

    coefs = jnp.stack([cond_x, cond_y, capacitance, pad_mask.astype(jnp.float32)])
    basis_e, coefs_e = widen(prior_basis, coefs, "gx", 0, bdepth, depth)
    basis_e, coefs_e = widen(basis_e, coefs_e, "gy", 1, bdepth, depth)

    row_start = lax.axis_index("gx") * rows_dev - depth
    col_start = lax.axis_index("gy") * cols_dev - depth
    shape_e = (rows_dev + 2 * depth, cols_dev + 2 * depth)
    grows = row_start + lax.broadcasted_iota(jnp.int32, shape_e, 0)
    gcols = col_start + lax.broadcasted_iota(jnp.int32, shape_e, 1)
    inside = (grows >= 0) & (grows < total_rows) & (gcols >= 0) & (gcols < total_cols)
    cx_e = jnp.where(grows < total_rows - 1, coefs_e[0], jnp.float32(0.0))
    cy_e = jnp.where(gcols < total_cols - 1, coefs_e[1], jnp.float32(0.0))
    cap_e = coefs_e[2]
    pad_e = coefs_e[3]

    def at(cells, margin):
        return inset(cells, depth - margin)

    def at_basis(margin):
        return inset(basis_e, bdepth - margin)

    top = depth - 1
    cx_t = at(cx_e, top)
    cy_t = at(cy_e, top)
    cx_up_t = cx_e[0:-2, 1:-1]
    cy_left_t = cy_e[1:-1, 0:-2]
    diag_g_t = cx_t + cx_up_t + cy_t + cy_left_t + supply_conductance * at(pad_e, top)
    diag_t = diag_g_t + shift_point * at(cap_e, top)
    diag_t = jnp.where(at(inside, top), diag_t, jnp.float32(1.0))

    def links_at(margin):
        cut = top - margin
        return tuple(inset(c, cut) for c in (cx_t, cy_t, cx_up_t, cy_left_t))

    first = SWEEPS + 1
    node_ids = at(grows, first) * total_cols + at(gcols, first)
    onehot = (node_ids[:, :, None] == port_nodes[None, None, :]) & at(inside, first)[:, :, None]
    rhs = at(cap_e, first)[:, :, None] * at_basis(first) + port_current * onehot.astype(jnp.float32)
    diag_f = inset(diag_t, top - first)[:, :, None]

    field = rhs / diag_f
    for sweep in range(SWEEPS):
        margin = first - 1 - sweep
        field = (inset(rhs, first - margin) + neighbors(field, links_at(margin))) / inset(diag_f, first - margin)

    tile_basis = at_basis(0)
    proj = allsum_quad(local_inner(tile_basis, inset(field, 1)), ("gy", "gx")) / nodes
    cand_1 = field - jnp.einsum("xyk,kp->xyp", at_basis(1), proj, precision=highest)
    cand = inset(cand_1, 1)
    diag_g = inset(diag_g_t, top)[:, :, None]
    g_image = diag_g * cand - neighbors(cand_1, links_at(0))
    c_image = at(cap_e, 0)[:, :, None] * cand
    images = local_inner(cand, jnp.concatenate([cand, g_image, c_image], axis=-1))
    gram, g_raw, c_raw = images[:, :width], images[:, width:2 * width], images[:, 2 * width:]
    packed = allsum_exchange(fold(gram, g_raw, c_raw), ("gx", "gy")) / nodes
    basis_flat, reduced_g, reduced_c = orthonormalize(packed, cand.reshape(-1, width))
    new_basis = basis_flat.reshape(cand.shape)
    return (new_basis, reduced_g, reduced_c)


def solution(mesh):
    placed = (P("gx", "gy", None), P("gx", "gy"), P("gx", "gy"), P("gx", "gy"), P("gx", "gy"), P())
    return jax.shard_map(
        per_device,
        mesh=mesh,
        in_specs=placed,
        out_specs=(P("gx", "gy", None), P(), P()),
        check_vma=False,
    )
```

```python
import jax
import jax.numpy as jnp
from jax import lax
from jax.experimental import pallas as pl
from jax.experimental.pallas import tpu as pltpu
from jax.sharding import PartitionSpec as P

SWEEPS = 4


shift_point = 0.5
supply_conductance = 4.0
port_current = 8.0
highest = lax.Precision.HIGHEST


def shifted(shard, axis, by):
    devices = lax.axis_size(axis)
    pairs = [(i, i + by) for i in range(devices) if 0 <= i + by < devices]
    return lax.ppermute(shard, axis, pairs)


def allsum(value, axes):
    for axis in axes:
        count = lax.axis_size(axis)
        if count & (count - 1):
            value = lax.psum(value, axis)
            continue
        step = 1
        while step < count:
            other = lax.ppermute(value, axis, [(i, i ^ step) for i in range(count)])
            value = value + other
            step *= 2
    return value


def allsum_exchange(value, axes):
    count = 1
    for axis in axes:
        count *= lax.axis_size(axis)
    flat = value.reshape(-1, value.shape[-1])
    if flat.shape[0] % count:
        return allsum(value, axes)
    parts = flat.reshape(count, -1, flat.shape[-1])
    got = lax.all_to_all(parts, axes, 0, 0, tiled=False)
    total = got[0]
    for k in range(1, count):
        total = total + got[k]
    spread = jnp.broadcast_to(total[None], (count,) + total.shape)
    back = lax.all_to_all(spread, axes, 0, 0, tiled=False)
    return back.reshape(value.shape)


def allsum_quad(value, axes):
    for axis in axes:
        count = lax.axis_size(axis)
        if count & (count - 1):
            value = lax.psum(value, axis)
            continue
        index = lax.axis_index(axis)
        step = 1
        while step < count:
            if step * 4 <= count:
                own = (index // step) % 4
                got = [value] + [
                    lax.ppermute(value, axis, [(i, i ^ (k * step)) for i in range(count)])
                    for k in (1, 2, 3)
                ]
                stack = jnp.stack(got)
                total = lax.dynamic_index_in_dim(stack, own, keepdims=False)
                for member in (1, 2, 3):
                    total = total + lax.dynamic_index_in_dim(stack, own ^ member, keepdims=False)
                value = total
                step *= 4
            else:
                other = lax.ppermute(value, axis, [(i, i ^ step) for i in range(count)])
                value = value + other
                step *= 2
    return value


def pack(block, coefs):
    width = block.shape[-1]
    flat = coefs.reshape(-1)
    spare = (-flat.shape[0]) % width
    flat = jnp.pad(flat, (0, spare))
    return jnp.concatenate([block.reshape(-1, width), flat.reshape(-1, width)], axis=0)


def unpack(packed, block_shape, coef_shape):
    count = block_shape[0] * block_shape[1]
    block = packed[:count].reshape(block_shape)
    size = coef_shape[0] * coef_shape[1] * coef_shape[2]
    coefs = packed[count:].reshape(-1)[:size].reshape(coef_shape)
    return block, coefs


def widen(block, coefs, axis, dim, depth, cdepth):
    head = lax.slice_in_dim(block, 0, depth, axis=dim)
    tail = lax.slice_in_dim(block, block.shape[dim] - depth, block.shape[dim], axis=dim)
    chead = lax.slice_in_dim(coefs, 0, cdepth, axis=dim + 1)
    ctail = lax.slice_in_dim(coefs, coefs.shape[dim + 1] - cdepth, coefs.shape[dim + 1], axis=dim + 1)
    before = shifted(pack(tail, ctail), axis, 1)
    after = shifted(pack(head, chead), axis, -1)
    before_b, before_c = unpack(before, head.shape, chead.shape)
    after_b, after_c = unpack(after, head.shape, chead.shape)
    block = jnp.concatenate([before_b, block, after_b], axis=dim)
    coefs = jnp.concatenate([before_c, coefs, after_c], axis=dim + 1)
    return block, coefs


def inset(cells, by):
    if by == 0:
        return cells
    return cells[by:cells.shape[0] - by, by:cells.shape[1] - by]


def neighbors(cells, links):
    cx, cy, cx_up, cy_left = links
    total = cx[:, :, None] * cells[2:, 1:-1] + cx_up[:, :, None] * cells[:-2, 1:-1]
    return total + cy[:, :, None] * cells[1:-1, 2:] + cy_left[:, :, None] * cells[1:-1, :-2]


def local_inner(left, right):
    a = left.reshape(-1, left.shape[-1])
    b = right.reshape(-1, right.shape[-1])
    return jnp.einsum("cp,cq->pq", a, b, precision=highest, preferred_element_type=jnp.float32)


def fold(first, second, third):
    size = first.shape[0]
    row = lax.broadcasted_iota(jnp.int32, first.shape, 0)
    col = lax.broadcasted_iota(jnp.int32, first.shape, 1)
    upper = row <= col
    on_diag = jnp.where(row == col, third, jnp.float32(0.0))
    across = jnp.sum(on_diag, axis=0, keepdims=True)
    down = jnp.sum(on_diag, axis=1, keepdims=True)
    spill = jnp.where(row == col + 1, across, jnp.float32(0.0))
    spill = jnp.where((row == size - 1) & (col == 0), down, spill)
    return jnp.stack([jnp.where(upper, first, third), jnp.where(upper, second, spill)])


def unfold(one, two):
    size = one.shape[0]
    row = lax.broadcasted_iota(jnp.int32, one.shape, 0)
    col = lax.broadcasted_iota(jnp.int32, one.shape, 1)
    upper = row <= col
    first = jnp.where(upper, one, jnp.transpose(one))
    second = jnp.where(upper, two, jnp.transpose(two))
    low = jnp.where(row > col, one, jnp.float32(0.0))
    across = jnp.sum(jnp.where(row == col + 1, two, jnp.float32(0.0)), axis=0, keepdims=True)
    lane = lax.broadcasted_iota(jnp.int32, (1, size), 1)
    across = jnp.where(lane == size - 1, two[size - 1:size, 0:1], across)
    third = low + jnp.transpose(low) + jnp.where(row == col, across, jnp.float32(0.0))
    return first, second, third


def _factor_kernel(packed_ref, cand_ref, basis_ref, g_out_ref, c_out_ref, work_ref, inv_ref):
    size = packed_ref.shape[1]
    gram, g_block, c_block = unfold(packed_ref[0], packed_ref[1])
    work_ref[...] = gram
    rows = lax.broadcasted_iota(jnp.int32, (size, size), 0)
    cols = lax.broadcasted_iota(jnp.int32, (size, size), 1)
    inv_ref[...] = jnp.where(rows == cols, jnp.float32(1.0), jnp.float32(0.0))
    lane = lax.broadcasted_iota(jnp.int32, (1, size), 1)
    chunk = 8
    for lo in range(0, size, chunk):
        span = size - lo
        cols_s = lax.broadcasted_iota(jnp.int32, (span, size), 1)
        sub = lo + lax.broadcasted_iota(jnp.int32, (span, 1), 0)

        def step(j, carry, lo=lo, cols_s=cols_s, sub=sub):
            whole = work_ref[lo:, :]
            row = work_ref[pl.ds(j, 1), :]
            column = jnp.sum(jnp.where(cols_s == j, whole, jnp.float32(0.0)), axis=1, keepdims=True)
            pivot = jnp.sum(jnp.where(lane == j, row, jnp.float32(0.0)), axis=1, keepdims=True)
            scale = lax.rsqrt(pivot)
            right = jnp.where(lane >= j, row * scale, jnp.float32(0.0))
            left = jnp.where(sub >= j, column * scale, jnp.float32(0.0))
            head = inv_ref[pl.ds(j, 1), :] * scale
            work_ref[lo:, :] = whole - left * right
            inv_ref[lo:, :] = inv_ref[lo:, :] - left * head
            inv_ref[pl.ds(j, 1), :] = head
            return carry

        lax.fori_loop(lo, min(lo + chunk, size), step, 0)

    inverse = inv_ref[...]
    by_rows = (((1,), (1,)), ((), ()))
    basis_ref[...] = lax.dot_general(
        cand_ref[...], inverse, by_rows, precision=highest, preferred_element_type=jnp.float32
    )
    for block, out_ref in ((g_block, g_out_ref), (c_block, c_out_ref)):
        half = jnp.dot(inverse, block, precision=highest, preferred_element_type=jnp.float32)
        out_ref[...] = lax.dot_general(
            half, inverse, by_rows, precision=highest, preferred_element_type=jnp.float32
        )


def orthonormalize(packed, cand):
    size = packed.shape[1]
    return pl.pallas_call(
        _factor_kernel,
        out_shape=(
            jax.ShapeDtypeStruct(cand.shape, jnp.float32),
            jax.ShapeDtypeStruct((size, size), jnp.float32),
            jax.ShapeDtypeStruct((size, size), jnp.float32),
        ),
        scratch_shapes=[pltpu.VMEM((size, size), jnp.float32), pltpu.VMEM((size, size), jnp.float32)],
    )(packed, cand)


def per_device(prior_basis, cond_x, cond_y, capacitance, pad_mask, port_nodes):
    rows_dev, cols_dev = cond_x.shape
    width = port_nodes.shape[0]
    count_x = lax.axis_size("gx")
    count_y = lax.axis_size("gy")
    total_rows = rows_dev * count_x
    total_cols = cols_dev * count_y
    nodes = total_rows * total_cols
    bdepth = SWEEPS + 1
    depth = SWEEPS + 2

    coefs = jnp.stack([cond_x, cond_y, capacitance, pad_mask.astype(jnp.float32)])
    basis_e, coefs_e = widen(prior_basis, coefs, "gx", 0, bdepth, depth)
    basis_e, coefs_e = widen(basis_e, coefs_e, "gy", 1, bdepth, depth)

    row_start = lax.axis_index("gx") * rows_dev - depth
    col_start = lax.axis_index("gy") * cols_dev - depth
    shape_e = (rows_dev + 2 * depth, cols_dev + 2 * depth)
    grows = row_start + lax.broadcasted_iota(jnp.int32, shape_e, 0)
    gcols = col_start + lax.broadcasted_iota(jnp.int32, shape_e, 1)
    inside = (grows >= 0) & (grows < total_rows) & (gcols >= 0) & (gcols < total_cols)
    cx_e = jnp.where(grows < total_rows - 1, coefs_e[0], jnp.float32(0.0))
    cy_e = jnp.where(gcols < total_cols - 1, coefs_e[1], jnp.float32(0.0))
    cap_e = coefs_e[2]
    pad_e = coefs_e[3]

    def at(cells, margin):
        return inset(cells, depth - margin)

    def at_basis(margin):
        return inset(basis_e, bdepth - margin)

    top = depth - 1
    cx_t = at(cx_e, top)
    cy_t = at(cy_e, top)
    cx_up_t = cx_e[0:-2, 1:-1]
    cy_left_t = cy_e[1:-1, 0:-2]
    diag_g_t = cx_t + cx_up_t + cy_t + cy_left_t + supply_conductance * at(pad_e, top)
    diag_t = diag_g_t + shift_point * at(cap_e, top)
    diag_t = jnp.where(at(inside, top), diag_t, jnp.float32(1.0))

    def links_at(margin):
        cut = top - margin
        return tuple(inset(c, cut) for c in (cx_t, cy_t, cx_up_t, cy_left_t))

    first = SWEEPS + 1
    node_ids = at(grows, first) * total_cols + at(gcols, first)
    onehot = (node_ids[:, :, None] == port_nodes[None, None, :]) & at(inside, first)[:, :, None]
    rhs = at(cap_e, first)[:, :, None] * at_basis(first) + port_current * onehot.astype(jnp.float32)
    diag_f = inset(diag_t, top - first)[:, :, None]

    field = rhs / diag_f
    for sweep in range(SWEEPS):
        margin = first - 1 - sweep
        field = (inset(rhs, first - margin) + neighbors(field, links_at(margin))) / inset(diag_f, first - margin)

    tile_basis = at_basis(0)
    proj = allsum_quad(local_inner(tile_basis, inset(field, 1)), ("gx", "gy")) / nodes
    cand_1 = field - jnp.einsum("xyk,kp->xyp", at_basis(1), proj, precision=highest)
    cand = inset(cand_1, 1)
    diag_g = inset(diag_g_t, top)[:, :, None]
    g_image = diag_g * cand - neighbors(cand_1, links_at(0))
    c_image = at(cap_e, 0)[:, :, None] * cand
    images = local_inner(cand, jnp.concatenate([cand, g_image, c_image], axis=-1))
    gram, g_raw, c_raw = images[:, :width], images[:, width:2 * width], images[:, 2 * width:]
    packed = allsum_exchange(fold(gram, g_raw, c_raw), ("gx", "gy")) / nodes
    basis_flat, reduced_g, reduced_c = orthonormalize(packed, cand.reshape(-1, width))
    new_basis = basis_flat.reshape(cand.shape)
    return (new_basis, reduced_g, reduced_c)


def solution(mesh):
    placed = (P("gx", "gy", None), P("gx", "gy"), P("gx", "gy"), P("gx", "gy"), P("gx", "gy"), P())
    return jax.shard_map(
        per_device,
        mesh=mesh,
        in_specs=placed,
        out_specs=(P("gx", "gy", None), P(), P()),
        check_vma=False,
    )
```

```python
import jax
import jax.numpy as jnp
from jax import lax
from jax.experimental import pallas as pl
from jax.experimental.pallas import tpu as pltpu
from jax.sharding import PartitionSpec as P

SWEEPS = 4


shift_point = 0.5
supply_conductance = 4.0
port_current = 8.0
highest = lax.Precision.HIGHEST


def shifted(shard, axis, by):
    devices = lax.axis_size(axis)
    pairs = [(i, i + by) for i in range(devices) if 0 <= i + by < devices]
    return lax.ppermute(shard, axis, pairs)


def allsum(value, axes):
    for axis in axes:
        count = lax.axis_size(axis)
        if count & (count - 1):
            value = lax.psum(value, axis)
            continue
        step = 1
        while step < count:
            other = lax.ppermute(value, axis, [(i, i ^ step) for i in range(count)])
            value = value + other
            step *= 2
    return value


def allsum_exchange(value, axes):
    count = 1
    for axis in axes:
        count *= lax.axis_size(axis)
    flat = value.reshape(-1, value.shape[-1])
    if flat.shape[0] % count:
        return allsum(value, axes)
    parts = flat.reshape(count, -1, flat.shape[-1])
    got = lax.all_to_all(parts, axes, 0, 0, tiled=False)
    total = got[0]
    for k in range(1, count):
        total = total + got[k]
    spread = jnp.broadcast_to(total[None], (count,) + total.shape)
    back = lax.all_to_all(spread, axes, 0, 0, tiled=False)
    return back.reshape(value.shape)


def allsum_quad(value, axes):
    for axis in axes:
        count = lax.axis_size(axis)
        if count & (count - 1):
            value = lax.psum(value, axis)
            continue
        index = lax.axis_index(axis)
        stride, doublings = 1, 0
        while stride < count:
            stride, doublings = stride * 2, doublings + 1
        if doublings % 2:
            value = value + lax.ppermute(value, axis, [(i, i ^ (count // 2)) for i in range(count)])
            count_left = count // 2
        else:
            count_left = count
        step = 1
        while step < count_left:
            if step * 4 <= count_left:
                own = (index // step) % 4
                got = [value] + [
                    lax.ppermute(value, axis, [(i, i ^ (k * step)) for i in range(count)])
                    for k in (1, 2, 3)
                ]
                stack = jnp.stack(got)
                total = lax.dynamic_index_in_dim(stack, own, keepdims=False)
                for member in (1, 2, 3):
                    total = total + lax.dynamic_index_in_dim(stack, own ^ member, keepdims=False)
                value = total
                step *= 4
            else:
                other = lax.ppermute(value, axis, [(i, i ^ step) for i in range(count)])
                value = value + other
                step *= 2
    return value


def pack(block, coefs):
    width = block.shape[-1]
    flat = coefs.reshape(-1)
    spare = (-flat.shape[0]) % width
    flat = jnp.pad(flat, (0, spare))
    return jnp.concatenate([block.reshape(-1, width), flat.reshape(-1, width)], axis=0)


def unpack(packed, block_shape, coef_shape):
    count = block_shape[0] * block_shape[1]
    block = packed[:count].reshape(block_shape)
    size = coef_shape[0] * coef_shape[1] * coef_shape[2]
    coefs = packed[count:].reshape(-1)[:size].reshape(coef_shape)
    return block, coefs


def widen(block, coefs, axis, dim, depth, cdepth):
    head = lax.slice_in_dim(block, 0, depth, axis=dim)
    tail = lax.slice_in_dim(block, block.shape[dim] - depth, block.shape[dim], axis=dim)
    chead = lax.slice_in_dim(coefs, 0, cdepth, axis=dim + 1)
    ctail = lax.slice_in_dim(coefs, coefs.shape[dim + 1] - cdepth, coefs.shape[dim + 1], axis=dim + 1)
    before = shifted(pack(tail, ctail), axis, 1)
    after = shifted(pack(head, chead), axis, -1)
    before_b, before_c = unpack(before, head.shape, chead.shape)
    after_b, after_c = unpack(after, head.shape, chead.shape)
    block = jnp.concatenate([before_b, block, after_b], axis=dim)
    coefs = jnp.concatenate([before_c, coefs, after_c], axis=dim + 1)
    return block, coefs


def inset(cells, by):
    if by == 0:
        return cells
    return cells[by:cells.shape[0] - by, by:cells.shape[1] - by]


def neighbors(cells, links):
    cx, cy, cx_up, cy_left = links
    total = cx[:, :, None] * cells[2:, 1:-1] + cx_up[:, :, None] * cells[:-2, 1:-1]
    return total + cy[:, :, None] * cells[1:-1, 2:] + cy_left[:, :, None] * cells[1:-1, :-2]


def local_inner(left, right):
    a = left.reshape(-1, left.shape[-1])
    b = right.reshape(-1, right.shape[-1])
    return jnp.einsum("cp,cq->pq", a, b, precision=highest, preferred_element_type=jnp.float32)


def fold(first, second, third):
    size = first.shape[0]
    row = lax.broadcasted_iota(jnp.int32, first.shape, 0)
    col = lax.broadcasted_iota(jnp.int32, first.shape, 1)
    upper = row <= col
    on_diag = jnp.where(row == col, third, jnp.float32(0.0))
    across = jnp.sum(on_diag, axis=0, keepdims=True)
    down = jnp.sum(on_diag, axis=1, keepdims=True)
    spill = jnp.where(row == col + 1, across, jnp.float32(0.0))
    spill = jnp.where((row == size - 1) & (col == 0), down, spill)
    return jnp.stack([jnp.where(upper, first, third), jnp.where(upper, second, spill)])


def unfold(one, two):
    size = one.shape[0]
    row = lax.broadcasted_iota(jnp.int32, one.shape, 0)
    col = lax.broadcasted_iota(jnp.int32, one.shape, 1)
    upper = row <= col
    first = jnp.where(upper, one, jnp.transpose(one))
    second = jnp.where(upper, two, jnp.transpose(two))
    low = jnp.where(row > col, one, jnp.float32(0.0))
    across = jnp.sum(jnp.where(row == col + 1, two, jnp.float32(0.0)), axis=0, keepdims=True)
    lane = lax.broadcasted_iota(jnp.int32, (1, size), 1)
    across = jnp.where(lane == size - 1, two[size - 1:size, 0:1], across)
    third = low + jnp.transpose(low) + jnp.where(row == col, across, jnp.float32(0.0))
    return first, second, third


def _factor_kernel(packed_ref, cand_ref, basis_ref, g_out_ref, c_out_ref, work_ref, inv_ref):
    size = packed_ref.shape[1]
    gram, g_block, c_block = unfold(packed_ref[0], packed_ref[1])
    work_ref[...] = gram
    rows = lax.broadcasted_iota(jnp.int32, (size, size), 0)
    cols = lax.broadcasted_iota(jnp.int32, (size, size), 1)
    inv_ref[...] = jnp.where(rows == cols, jnp.float32(1.0), jnp.float32(0.0))
    lane = lax.broadcasted_iota(jnp.int32, (1, size), 1)
    chunk = 8
    for lo in range(0, size, chunk):
        span = size - lo
        cols_s = lax.broadcasted_iota(jnp.int32, (span, size), 1)
        sub = lo + lax.broadcasted_iota(jnp.int32, (span, 1), 0)

        def step(j, carry, lo=lo, cols_s=cols_s, sub=sub):
            whole = work_ref[lo:, :]
            row = work_ref[pl.ds(j, 1), :]
            column = jnp.sum(jnp.where(cols_s == j, whole, jnp.float32(0.0)), axis=1, keepdims=True)
            pivot = jnp.sum(jnp.where(lane == j, row, jnp.float32(0.0)), axis=1, keepdims=True)
            scale = lax.rsqrt(pivot)
            right = jnp.where(lane >= j, row * scale, jnp.float32(0.0))
            left = jnp.where(sub >= j, column * scale, jnp.float32(0.0))
            head = inv_ref[pl.ds(j, 1), :] * scale
            work_ref[lo:, :] = whole - left * right
            inv_ref[lo:, :] = inv_ref[lo:, :] - left * head
            inv_ref[pl.ds(j, 1), :] = head
            return carry

        lax.fori_loop(lo, min(lo + chunk, size), step, 0)

    inverse = inv_ref[...]
    by_rows = (((1,), (1,)), ((), ()))
    basis_ref[...] = lax.dot_general(
        cand_ref[...], inverse, by_rows, precision=highest, preferred_element_type=jnp.float32
    )
    for block, out_ref in ((g_block, g_out_ref), (c_block, c_out_ref)):
        half = jnp.dot(inverse, block, precision=highest, preferred_element_type=jnp.float32)
        out_ref[...] = lax.dot_general(
            half, inverse, by_rows, precision=highest, preferred_element_type=jnp.float32
        )


def orthonormalize(packed, cand):
    size = packed.shape[1]
    return pl.pallas_call(
        _factor_kernel,
        out_shape=(
            jax.ShapeDtypeStruct(cand.shape, jnp.float32),
            jax.ShapeDtypeStruct((size, size), jnp.float32),
            jax.ShapeDtypeStruct((size, size), jnp.float32),
        ),
        scratch_shapes=[pltpu.VMEM((size, size), jnp.float32), pltpu.VMEM((size, size), jnp.float32)],
    )(packed, cand)


def per_device(prior_basis, cond_x, cond_y, capacitance, pad_mask, port_nodes):
    rows_dev, cols_dev = cond_x.shape
    width = port_nodes.shape[0]
    count_x = lax.axis_size("gx")
    count_y = lax.axis_size("gy")
    total_rows = rows_dev * count_x
    total_cols = cols_dev * count_y
    nodes = total_rows * total_cols
    bdepth = SWEEPS + 1
    depth = SWEEPS + 2

    coefs = jnp.stack([cond_x, cond_y, capacitance, pad_mask.astype(jnp.float32)])
    basis_e, coefs_e = widen(prior_basis, coefs, "gx", 0, bdepth, depth)
    basis_e, coefs_e = widen(basis_e, coefs_e, "gy", 1, bdepth, depth)

    row_start = lax.axis_index("gx") * rows_dev - depth
    col_start = lax.axis_index("gy") * cols_dev - depth
    shape_e = (rows_dev + 2 * depth, cols_dev + 2 * depth)
    grows = row_start + lax.broadcasted_iota(jnp.int32, shape_e, 0)
    gcols = col_start + lax.broadcasted_iota(jnp.int32, shape_e, 1)
    inside = (grows >= 0) & (grows < total_rows) & (gcols >= 0) & (gcols < total_cols)
    cx_e = jnp.where(grows < total_rows - 1, coefs_e[0], jnp.float32(0.0))
    cy_e = jnp.where(gcols < total_cols - 1, coefs_e[1], jnp.float32(0.0))
    cap_e = coefs_e[2]
    pad_e = coefs_e[3]

    def at(cells, margin):
        return inset(cells, depth - margin)

    def at_basis(margin):
        return inset(basis_e, bdepth - margin)

    top = depth - 1
    cx_t = at(cx_e, top)
    cy_t = at(cy_e, top)
    cx_up_t = cx_e[0:-2, 1:-1]
    cy_left_t = cy_e[1:-1, 0:-2]
    diag_g_t = cx_t + cx_up_t + cy_t + cy_left_t + supply_conductance * at(pad_e, top)
    diag_t = diag_g_t + shift_point * at(cap_e, top)
    diag_t = jnp.where(at(inside, top), diag_t, jnp.float32(1.0))

    def links_at(margin):
        cut = top - margin
        return tuple(inset(c, cut) for c in (cx_t, cy_t, cx_up_t, cy_left_t))

    first = SWEEPS + 1
    node_ids = at(grows, first) * total_cols + at(gcols, first)
    onehot = (node_ids[:, :, None] == port_nodes[None, None, :]) & at(inside, first)[:, :, None]
    rhs = at(cap_e, first)[:, :, None] * at_basis(first) + port_current * onehot.astype(jnp.float32)
    diag_f = inset(diag_t, top - first)[:, :, None]

    field = rhs / diag_f
    for sweep in range(SWEEPS):
        margin = first - 1 - sweep
        field = (inset(rhs, first - margin) + neighbors(field, links_at(margin))) / inset(diag_f, first - margin)

    tile_basis = at_basis(0)
    proj = allsum_quad(local_inner(tile_basis, inset(field, 1)), ("gx", "gy")) / nodes
    cand_1 = field - jnp.einsum("xyk,kp->xyp", at_basis(1), proj, precision=highest)
    cand = inset(cand_1, 1)
    diag_g = inset(diag_g_t, top)[:, :, None]
    g_image = diag_g * cand - neighbors(cand_1, links_at(0))
    c_image = at(cap_e, 0)[:, :, None] * cand
    images = local_inner(cand, jnp.concatenate([cand, g_image, c_image], axis=-1))
    gram, g_raw, c_raw = images[:, :width], images[:, width:2 * width], images[:, 2 * width:]
    packed = allsum_exchange(fold(gram, g_raw, c_raw), ("gx", "gy")) / nodes
    basis_flat, reduced_g, reduced_c = orthonormalize(packed, cand.reshape(-1, width))
    new_basis = basis_flat.reshape(cand.shape)
    return (new_basis, reduced_g, reduced_c)


def solution(mesh):
    placed = (P("gx", "gy", None), P("gx", "gy"), P("gx", "gy"), P("gx", "gy"), P("gx", "gy"), P())
    return jax.shard_map(
        per_device,
        mesh=mesh,
        in_specs=placed,
        out_specs=(P("gx", "gy", None), P(), P()),
        check_vma=False,
    )
```

```python
import jax
import jax.numpy as jnp
from jax import lax
from jax.experimental import pallas as pl
from jax.experimental.pallas import tpu as pltpu
from jax.sharding import PartitionSpec as P

SWEEPS = 4


shift_point = 0.5
supply_conductance = 4.0
port_current = 8.0
highest = lax.Precision.HIGHEST


def shifted(shard, axis, by):
    devices = lax.axis_size(axis)
    pairs = [(i, i + by) for i in range(devices) if 0 <= i + by < devices]
    return lax.ppermute(shard, axis, pairs)


def allsum(value, axes):
    for axis in axes:
        count = lax.axis_size(axis)
        if count & (count - 1):
            value = lax.psum(value, axis)
            continue
        step = 1
        while step < count:
            other = lax.ppermute(value, axis, [(i, i ^ step) for i in range(count)])
            value = value + other
            step *= 2
    return value


def allsum_exchange(value, axes):
    count = 1
    for axis in axes:
        count *= lax.axis_size(axis)
    flat = value.reshape(-1, value.shape[-1])
    if flat.shape[0] % count:
        return allsum(value, axes)
    parts = flat.reshape(count, -1, flat.shape[-1])
    got = lax.all_to_all(parts, axes, 0, 0, tiled=False)
    total = got[0]
    for k in range(1, count):
        total = total + got[k]
    spread = jnp.broadcast_to(total[None], (count,) + total.shape)
    back = lax.all_to_all(spread, axes, 0, 0, tiled=False)
    return back.reshape(value.shape)


def allsum_quad(value, axes):
    for axis in axes:
        count = lax.axis_size(axis)
        if count & (count - 1):
            value = lax.psum(value, axis)
            continue
        index = lax.axis_index(axis)
        step = 1
        while step < count:
            if step * 4 <= count:
                own = (index // step) % 4
                got = [value] + [
                    lax.ppermute(value, axis, [(i, i ^ (k * step)) for i in range(count)])
                    for k in (1, 2, 3)
                ]
                stack = jnp.stack(got)
                total = lax.dynamic_index_in_dim(stack, own, keepdims=False)
                for member in (1, 2, 3):
                    total = total + lax.dynamic_index_in_dim(stack, own ^ member, keepdims=False)
                value = total
                step *= 4
            else:
                other = lax.ppermute(value, axis, [(i, i ^ step) for i in range(count)])
                value = value + other
                step *= 2
    return value


def pack(block, coefs):
    width = block.shape[-1]
    flat = coefs.reshape(-1)
    spare = (-flat.shape[0]) % width
    flat = jnp.pad(flat, (0, spare))
    return jnp.concatenate([block.reshape(-1, width), flat.reshape(-1, width)], axis=0)


def unpack(packed, block_shape, coef_shape):
    count = block_shape[0] * block_shape[1]
    block = packed[:count].reshape(block_shape)
    size = coef_shape[0] * coef_shape[1] * coef_shape[2]
    coefs = packed[count:].reshape(-1)[:size].reshape(coef_shape)
    return block, coefs


def widen(block, coefs, axis, dim, depth, cdepth):
    head = lax.slice_in_dim(block, 0, depth, axis=dim)
    tail = lax.slice_in_dim(block, block.shape[dim] - depth, block.shape[dim], axis=dim)
    chead = lax.slice_in_dim(coefs, 0, cdepth, axis=dim + 1)
    ctail = lax.slice_in_dim(coefs, coefs.shape[dim + 1] - cdepth, coefs.shape[dim + 1], axis=dim + 1)
    before = shifted(pack(tail, ctail), axis, 1)
    after = shifted(pack(head, chead), axis, -1)
    before_b, before_c = unpack(before, head.shape, chead.shape)
    after_b, after_c = unpack(after, head.shape, chead.shape)
    block = jnp.concatenate([before_b, block, after_b], axis=dim)
    coefs = jnp.concatenate([before_c, coefs, after_c], axis=dim + 1)
    return block, coefs


def inset(cells, by):
    if by == 0:
        return cells
    return cells[by:cells.shape[0] - by, by:cells.shape[1] - by]


def neighbors(cells, links):
    cx, cy, cx_up, cy_left = links
    total = cx[:, :, None] * cells[2:, 1:-1] + cx_up[:, :, None] * cells[:-2, 1:-1]
    return total + cy[:, :, None] * cells[1:-1, 2:] + cy_left[:, :, None] * cells[1:-1, :-2]


def local_inner(left, right):
    a = left.reshape(-1, left.shape[-1])
    b = right.reshape(-1, right.shape[-1])
    return jnp.einsum("cp,cq->pq", a, b, precision=highest, preferred_element_type=jnp.float32)


def fold(first, second, third):
    size = first.shape[0]
    row = lax.broadcasted_iota(jnp.int32, first.shape, 0)
    col = lax.broadcasted_iota(jnp.int32, first.shape, 1)
    upper = row <= col
    on_diag = jnp.where(row == col, third, jnp.float32(0.0))
    across = jnp.sum(on_diag, axis=0, keepdims=True)
    down = jnp.sum(on_diag, axis=1, keepdims=True)
    spill = jnp.where(row == col + 1, across, jnp.float32(0.0))
    spill = jnp.where((row == size - 1) & (col == 0), down, spill)
    return jnp.stack([jnp.where(upper, first, third), jnp.where(upper, second, spill)])


def unfold(one, two):
    size = one.shape[0]
    row = lax.broadcasted_iota(jnp.int32, one.shape, 0)
    col = lax.broadcasted_iota(jnp.int32, one.shape, 1)
    upper = row <= col
    first = jnp.where(upper, one, jnp.transpose(one))
    second = jnp.where(upper, two, jnp.transpose(two))
    low = jnp.where(row > col, one, jnp.float32(0.0))
    across = jnp.sum(jnp.where(row == col + 1, two, jnp.float32(0.0)), axis=0, keepdims=True)
    lane = lax.broadcasted_iota(jnp.int32, (1, size), 1)
    across = jnp.where(lane == size - 1, two[size - 1:size, 0:1], across)
    third = low + jnp.transpose(low) + jnp.where(row == col, across, jnp.float32(0.0))
    return first, second, third


def _factor_kernel(packed_ref, cand_ref, basis_ref, g_out_ref, c_out_ref, work_ref, inv_ref):
    size = packed_ref.shape[1]
    gram, g_block, c_block = unfold(packed_ref[0], packed_ref[1])
    work_ref[...] = gram
    rows = lax.broadcasted_iota(jnp.int32, (size, size), 0)
    cols = lax.broadcasted_iota(jnp.int32, (size, size), 1)
    inv_ref[...] = jnp.where(rows == cols, jnp.float32(1.0), jnp.float32(0.0))
    lane = lax.broadcasted_iota(jnp.int32, (1, size), 1)
    chunk = 8
    for lo in range(0, size, chunk):
        span = size - lo
        cols_s = lax.broadcasted_iota(jnp.int32, (span, size), 1)
        sub = lo + lax.broadcasted_iota(jnp.int32, (span, 1), 0)

        def step(j, carry, lo=lo, cols_s=cols_s, sub=sub):
            whole = work_ref[lo:, :]
            row = work_ref[pl.ds(j, 1), :]
            column = jnp.sum(jnp.where(cols_s == j, whole, jnp.float32(0.0)), axis=1, keepdims=True)
            pivot = jnp.sum(jnp.where(lane == j, row, jnp.float32(0.0)), axis=1, keepdims=True)
            scale = lax.rsqrt(pivot)
            right = jnp.where(lane >= j, row * scale, jnp.float32(0.0))
            left = jnp.where(sub >= j, column * scale, jnp.float32(0.0))
            head = inv_ref[pl.ds(j, 1), :] * scale
            work_ref[lo:, :] = whole - left * right
            inv_ref[lo:, :] = inv_ref[lo:, :] - left * head
            inv_ref[pl.ds(j, 1), :] = head
            return carry

        lax.fori_loop(lo, min(lo + chunk, size), step, 0)

    inverse = inv_ref[...]
    by_rows = (((1,), (1,)), ((), ()))
    basis_ref[...] = lax.dot_general(
        cand_ref[...], inverse, by_rows, precision=highest, preferred_element_type=jnp.float32
    )
    for block, out_ref in ((g_block, g_out_ref), (c_block, c_out_ref)):
        half = jnp.dot(inverse, block, precision=highest, preferred_element_type=jnp.float32)
        out_ref[...] = lax.dot_general(
            half, inverse, by_rows, precision=highest, preferred_element_type=jnp.float32
        )


def orthonormalize(packed, cand):
    size = packed.shape[1]
    return pl.pallas_call(
        _factor_kernel,
        out_shape=(
            jax.ShapeDtypeStruct(cand.shape, jnp.float32),
            jax.ShapeDtypeStruct((size, size), jnp.float32),
            jax.ShapeDtypeStruct((size, size), jnp.float32),
        ),
        scratch_shapes=[pltpu.VMEM((size, size), jnp.float32), pltpu.VMEM((size, size), jnp.float32)],
    )(packed, cand)


def per_device(prior_basis, cond_x, cond_y, capacitance, pad_mask, port_nodes):
    rows_dev, cols_dev = cond_x.shape
    width = port_nodes.shape[0]
    count_x = lax.axis_size("gx")
    count_y = lax.axis_size("gy")
    total_rows = rows_dev * count_x
    total_cols = cols_dev * count_y
    nodes = total_rows * total_cols
    bdepth = SWEEPS + 1
    depth = SWEEPS + 2

    coefs = jnp.stack([cond_x, cond_y, capacitance, pad_mask.astype(jnp.float32)])
    basis_e, coefs_e = widen(prior_basis, coefs, "gx", 0, bdepth, depth)
    basis_e, coefs_e = widen(basis_e, coefs_e, "gy", 1, bdepth, depth)

    row_start = lax.axis_index("gx") * rows_dev - depth
    col_start = lax.axis_index("gy") * cols_dev - depth
    shape_e = (rows_dev + 2 * depth, cols_dev + 2 * depth)
    grows = row_start + lax.broadcasted_iota(jnp.int32, shape_e, 0)
    gcols = col_start + lax.broadcasted_iota(jnp.int32, shape_e, 1)
    inside = (grows >= 0) & (grows < total_rows) & (gcols >= 0) & (gcols < total_cols)
    cx_e = jnp.where(grows < total_rows - 1, coefs_e[0], jnp.float32(0.0))
    cy_e = jnp.where(gcols < total_cols - 1, coefs_e[1], jnp.float32(0.0))
    cap_e = coefs_e[2]
    pad_e = coefs_e[3]

    def at(cells, margin):
        return inset(cells, depth - margin)

    def at_basis(margin):
        return inset(basis_e, bdepth - margin)

    top = depth - 1
    cx_t = at(cx_e, top)
    cy_t = at(cy_e, top)
    cx_up_t = cx_e[0:-2, 1:-1]
    cy_left_t = cy_e[1:-1, 0:-2]
    diag_g_t = cx_t + cx_up_t + cy_t + cy_left_t + supply_conductance * at(pad_e, top)
    diag_t = diag_g_t + shift_point * at(cap_e, top)
    diag_t = jnp.where(at(inside, top), diag_t, jnp.float32(1.0))

    def links_at(margin):
        cut = top - margin
        return tuple(inset(c, cut) for c in (cx_t, cy_t, cx_up_t, cy_left_t))

    first = SWEEPS + 1
    node_ids = at(grows, first) * total_cols + at(gcols, first)
    onehot = (node_ids[:, :, None] == port_nodes[None, None, :]) & at(inside, first)[:, :, None]
    rhs = at(cap_e, first)[:, :, None] * at_basis(first) + port_current * onehot.astype(jnp.float32)
    diag_f = inset(diag_t, top - first)[:, :, None]

    field = rhs / diag_f
    for sweep in range(SWEEPS):
        margin = first - 1 - sweep
        field = (inset(rhs, first - margin) + neighbors(field, links_at(margin))) / inset(diag_f, first - margin)

    tile_basis = at_basis(0)
    proj = allsum_quad(local_inner(tile_basis, inset(field, 1)), ("gx", "gy")) / nodes
    cand_1 = field - jnp.einsum("xyk,kp->xyp", at_basis(1), proj, precision=highest)
    cand = inset(cand_1, 1)
    diag_g = inset(diag_g_t, top)[:, :, None]
    g_image = diag_g * cand - neighbors(cand_1, links_at(0))
    c_image = at(cap_e, 0)[:, :, None] * cand
    images = local_inner(cand, jnp.concatenate([cand, g_image, c_image], axis=-1))
    gram, g_raw, c_raw = images[:, :width], images[:, width:2 * width], images[:, 2 * width:]
    packed = allsum_exchange(fold(gram, g_raw, c_raw), ("gy", "gx")) / nodes
    basis_flat, reduced_g, reduced_c = orthonormalize(packed, cand.reshape(-1, width))
    new_basis = basis_flat.reshape(cand.shape)
    return (new_basis, reduced_g, reduced_c)


def solution(mesh):
    placed = (P("gx", "gy", None), P("gx", "gy"), P("gx", "gy"), P("gx", "gy"), P("gx", "gy"), P())
    return jax.shard_map(
        per_device,
        mesh=mesh,
        in_specs=placed,
        out_specs=(P("gx", "gy", None), P(), P()),
        check_vma=False,
    )
```

```python
import jax
import jax.numpy as jnp
from jax import lax
from jax.experimental import pallas as pl
from jax.experimental.pallas import tpu as pltpu
from jax.sharding import PartitionSpec as P

SWEEPS = 4


shift_point = 0.5
supply_conductance = 4.0
port_current = 8.0
highest = lax.Precision.HIGHEST


def shifted(shard, axis, by):
    devices = lax.axis_size(axis)
    pairs = [(i, i + by) for i in range(devices) if 0 <= i + by < devices]
    return lax.ppermute(shard, axis, pairs)


def allsum(value, axes):
    for axis in axes:
        count = lax.axis_size(axis)
        if count & (count - 1):
            value = lax.psum(value, axis)
            continue
        step = 1
        while step < count:
            other = lax.ppermute(value, axis, [(i, i ^ step) for i in range(count)])
            value = value + other
            step *= 2
    return value


def allsum_exchange(value, axes):
    count = 1
    for axis in axes:
        count *= lax.axis_size(axis)
    flat = value.reshape(-1, value.shape[-1])
    if flat.shape[0] % count:
        return allsum(value, axes)
    parts = flat.reshape(count, -1, flat.shape[-1])
    got = lax.all_to_all(parts, axes, 0, 0, tiled=False)
    total = got[0]
    for k in range(1, count):
        total = total + got[k]
    spread = jnp.broadcast_to(total[None], (count,) + total.shape)
    back = lax.all_to_all(spread, axes, 0, 0, tiled=False)
    return back.reshape(value.shape)


def allsum_quad(value, axes):
    for axis in axes:
        count = lax.axis_size(axis)
        if count & (count - 1):
            value = lax.psum(value, axis)
            continue
        index = lax.axis_index(axis)
        step = 1
        while step < count:
            if step * 4 <= count:
                own = (index // step) % 4
                got = [value] + [
                    lax.ppermute(value, axis, [(i, i ^ (k * step)) for i in range(count)])
                    for k in (1, 2, 3)
                ]
                stack = jnp.stack(got)
                total = lax.dynamic_index_in_dim(stack, own, keepdims=False)
                for member in (1, 2, 3):
                    total = total + lax.dynamic_index_in_dim(stack, own ^ member, keepdims=False)
                value = total
                step *= 4
            else:
                other = lax.ppermute(value, axis, [(i, i ^ step) for i in range(count)])
                value = value + other
                step *= 2
    return value


def pack(block, coefs):
    width = block.shape[-1]
    flat = coefs.reshape(-1)
    spare = (-flat.shape[0]) % width
    flat = jnp.pad(flat, (0, spare))
    return jnp.concatenate([block.reshape(-1, width), flat.reshape(-1, width)], axis=0)


def unpack(packed, block_shape, coef_shape):
    count = block_shape[0] * block_shape[1]
    block = packed[:count].reshape(block_shape)
    size = coef_shape[0] * coef_shape[1] * coef_shape[2]
    coefs = packed[count:].reshape(-1)[:size].reshape(coef_shape)
    return block, coefs


def widen(block, coefs, axis, dim, depth, cdepth):
    head = lax.slice_in_dim(block, 0, depth, axis=dim)
    tail = lax.slice_in_dim(block, block.shape[dim] - depth, block.shape[dim], axis=dim)
    chead = lax.slice_in_dim(coefs, 0, cdepth, axis=dim + 1)
    ctail = lax.slice_in_dim(coefs, coefs.shape[dim + 1] - cdepth, coefs.shape[dim + 1], axis=dim + 1)
    before = shifted(pack(tail, ctail), axis, 1)
    after = shifted(pack(head, chead), axis, -1)
    before_b, before_c = unpack(before, head.shape, chead.shape)
    after_b, after_c = unpack(after, head.shape, chead.shape)
    block = jnp.concatenate([before_b, block, after_b], axis=dim)
    coefs = jnp.concatenate([before_c, coefs, after_c], axis=dim + 1)
    return block, coefs


def inset(cells, by):
    if by == 0:
        return cells
    return cells[by:cells.shape[0] - by, by:cells.shape[1] - by]


def neighbors(cells, links):
    cx, cy, cx_up, cy_left = links
    total = cx[:, :, None] * cells[2:, 1:-1] + cx_up[:, :, None] * cells[:-2, 1:-1]
    return total + cy[:, :, None] * cells[1:-1, 2:] + cy_left[:, :, None] * cells[1:-1, :-2]


def local_inner(left, right):
    a = left.reshape(-1, left.shape[-1])
    b = right.reshape(-1, right.shape[-1])
    return jnp.einsum("cp,cq->pq", a, b, precision=highest, preferred_element_type=jnp.float32)


def fold(first, second, third):
    size = first.shape[0]
    row = lax.broadcasted_iota(jnp.int32, first.shape, 0)
    col = lax.broadcasted_iota(jnp.int32, first.shape, 1)
    upper = row <= col
    on_diag = jnp.where(row == col, third, jnp.float32(0.0))
    across = jnp.sum(on_diag, axis=0, keepdims=True)
    down = jnp.sum(on_diag, axis=1, keepdims=True)
    spill = jnp.where(row == col + 1, across, jnp.float32(0.0))
    spill = jnp.where((row == size - 1) & (col == 0), down, spill)
    return jnp.stack([jnp.where(upper, first, third), jnp.where(upper, second, spill)])


def unfold(one, two):
    size = one.shape[0]
    row = lax.broadcasted_iota(jnp.int32, one.shape, 0)
    col = lax.broadcasted_iota(jnp.int32, one.shape, 1)
    upper = row <= col
    first = jnp.where(upper, one, jnp.transpose(one))
    second = jnp.where(upper, two, jnp.transpose(two))
    low = jnp.where(row > col, one, jnp.float32(0.0))
    across = jnp.sum(jnp.where(row == col + 1, two, jnp.float32(0.0)), axis=0, keepdims=True)
    lane = lax.broadcasted_iota(jnp.int32, (1, size), 1)
    across = jnp.where(lane == size - 1, two[size - 1:size, 0:1], across)
    third = low + jnp.transpose(low) + jnp.where(row == col, across, jnp.float32(0.0))
    return first, second, third


def _factor_kernel(packed_ref, cand_ref, basis_ref, g_out_ref, c_out_ref, work_ref, inv_ref):
    size = packed_ref.shape[1]
    gram, g_block, c_block = unfold(packed_ref[0], packed_ref[1])
    work_ref[...] = gram
    rows = lax.broadcasted_iota(jnp.int32, (size, size), 0)
    cols = lax.broadcasted_iota(jnp.int32, (size, size), 1)
    inv_ref[...] = jnp.where(rows == cols, jnp.float32(1.0), jnp.float32(0.0))
    lane = lax.broadcasted_iota(jnp.int32, (1, size), 1)
    chunk = 8
    for lo in range(0, size, chunk):
        span = size - lo
        cols_s = lax.broadcasted_iota(jnp.int32, (span, size), 1)
        sub = lo + lax.broadcasted_iota(jnp.int32, (span, 1), 0)

        def step(j, carry, lo=lo, cols_s=cols_s, sub=sub):
            whole = work_ref[lo:, :]
            row = work_ref[pl.ds(j, 1), :]
            column = jnp.sum(jnp.where(cols_s == j, whole, jnp.float32(0.0)), axis=1, keepdims=True)
            pivot = jnp.sum(jnp.where(lane == j, row, jnp.float32(0.0)), axis=1, keepdims=True)
            scale = lax.rsqrt(pivot)
            right = jnp.where(lane >= j, row * scale, jnp.float32(0.0))
            left = jnp.where(sub >= j, column * scale, jnp.float32(0.0))
            head = inv_ref[pl.ds(j, 1), :] * scale
            work_ref[lo:, :] = whole - left * right
            inv_ref[lo:, :] = inv_ref[lo:, :] - left * head
            inv_ref[pl.ds(j, 1), :] = head
            return carry

        lax.fori_loop(lo, min(lo + chunk, size), step, 0)

    inverse = inv_ref[...]
    by_rows = (((1,), (1,)), ((), ()))
    basis_ref[...] = lax.dot_general(
        cand_ref[...], inverse, by_rows, precision=highest, preferred_element_type=jnp.float32
    )
    for block, out_ref in ((g_block, g_out_ref), (c_block, c_out_ref)):
        half = jnp.dot(inverse, block, precision=highest, preferred_element_type=jnp.float32)
        out_ref[...] = lax.dot_general(
            half, inverse, by_rows, precision=highest, preferred_element_type=jnp.float32
        )


def orthonormalize(packed, cand):
    size = packed.shape[1]
    return pl.pallas_call(
        _factor_kernel,
        out_shape=(
            jax.ShapeDtypeStruct(cand.shape, jnp.float32),
            jax.ShapeDtypeStruct((size, size), jnp.float32),
            jax.ShapeDtypeStruct((size, size), jnp.float32),
        ),
        scratch_shapes=[pltpu.VMEM((size, size), jnp.float32), pltpu.VMEM((size, size), jnp.float32)],
    )(packed, cand)


def per_device(prior_basis, cond_x, cond_y, capacitance, pad_mask, port_nodes):
    rows_dev, cols_dev = cond_x.shape
    width = port_nodes.shape[0]
    count_x = lax.axis_size("gx")
    count_y = lax.axis_size("gy")
    total_rows = rows_dev * count_x
    total_cols = cols_dev * count_y
    nodes = total_rows * total_cols
    bdepth = SWEEPS + 1
    depth = SWEEPS + 2

    coefs = jnp.stack([cond_x, cond_y, capacitance, pad_mask.astype(jnp.float32)])
    basis_e, coefs_e = widen(prior_basis, coefs, "gy", 1, bdepth, depth)
    basis_e, coefs_e = widen(basis_e, coefs_e, "gx", 0, bdepth, depth)

    row_start = lax.axis_index("gx") * rows_dev - depth
    col_start = lax.axis_index("gy") * cols_dev - depth
    shape_e = (rows_dev + 2 * depth, cols_dev + 2 * depth)
    grows = row_start + lax.broadcasted_iota(jnp.int32, shape_e, 0)
    gcols = col_start + lax.broadcasted_iota(jnp.int32, shape_e, 1)
    inside = (grows >= 0) & (grows < total_rows) & (gcols >= 0) & (gcols < total_cols)
    cx_e = jnp.where(grows < total_rows - 1, coefs_e[0], jnp.float32(0.0))
    cy_e = jnp.where(gcols < total_cols - 1, coefs_e[1], jnp.float32(0.0))
    cap_e = coefs_e[2]
    pad_e = coefs_e[3]

    def at(cells, margin):
        return inset(cells, depth - margin)

    def at_basis(margin):
        return inset(basis_e, bdepth - margin)

    top = depth - 1
    cx_t = at(cx_e, top)
    cy_t = at(cy_e, top)
    cx_up_t = cx_e[0:-2, 1:-1]
    cy_left_t = cy_e[1:-1, 0:-2]
    diag_g_t = cx_t + cx_up_t + cy_t + cy_left_t + supply_conductance * at(pad_e, top)
    diag_t = diag_g_t + shift_point * at(cap_e, top)
    diag_t = jnp.where(at(inside, top), diag_t, jnp.float32(1.0))

    def links_at(margin):
        cut = top - margin
        return tuple(inset(c, cut) for c in (cx_t, cy_t, cx_up_t, cy_left_t))

    first = SWEEPS + 1
    node_ids = at(grows, first) * total_cols + at(gcols, first)
    onehot = (node_ids[:, :, None] == port_nodes[None, None, :]) & at(inside, first)[:, :, None]
    rhs = at(cap_e, first)[:, :, None] * at_basis(first) + port_current * onehot.astype(jnp.float32)
    diag_f = inset(diag_t, top - first)[:, :, None]

    field = rhs / diag_f
    for sweep in range(SWEEPS):
        margin = first - 1 - sweep
        field = (inset(rhs, first - margin) + neighbors(field, links_at(margin))) / inset(diag_f, first - margin)

    tile_basis = at_basis(0)
    proj = allsum_quad(local_inner(tile_basis, inset(field, 1)), ("gx", "gy")) / nodes
    cand_1 = field - jnp.einsum("xyk,kp->xyp", at_basis(1), proj, precision=highest)
    cand = inset(cand_1, 1)
    diag_g = inset(diag_g_t, top)[:, :, None]
    g_image = diag_g * cand - neighbors(cand_1, links_at(0))
    c_image = at(cap_e, 0)[:, :, None] * cand
    images = local_inner(cand, jnp.concatenate([cand, g_image, c_image], axis=-1))
    gram, g_raw, c_raw = images[:, :width], images[:, width:2 * width], images[:, 2 * width:]
    packed = allsum_exchange(fold(gram, g_raw, c_raw), ("gy", "gx")) / nodes
    basis_flat, reduced_g, reduced_c = orthonormalize(packed, cand.reshape(-1, width))
    new_basis = basis_flat.reshape(cand.shape)
    return (new_basis, reduced_g, reduced_c)


def solution(mesh):
    placed = (P("gx", "gy", None), P("gx", "gy"), P("gx", "gy"), P("gx", "gy"), P("gx", "gy"), P())
    return jax.shard_map(
        per_device,
        mesh=mesh,
        in_specs=placed,
        out_specs=(P("gx", "gy", None), P(), P()),
        check_vma=False,
    )
```

```python
import jax
import jax.numpy as jnp
from jax import lax
from jax.experimental import pallas as pl
from jax.experimental.pallas import tpu as pltpu
from jax.sharding import PartitionSpec as P

SWEEPS = 4


shift_point = 0.5
supply_conductance = 4.0
port_current = 8.0
highest = lax.Precision.HIGHEST


def shifted(shard, axis, by):
    devices = lax.axis_size(axis)
    pairs = [(i, i + by) for i in range(devices) if 0 <= i + by < devices]
    return lax.ppermute(shard, axis, pairs)


def allsum(value, axes):
    for axis in axes:
        count = lax.axis_size(axis)
        if count & (count - 1):
            value = lax.psum(value, axis)
            continue
        step = 1
        while step < count:
            other = lax.ppermute(value, axis, [(i, i ^ step) for i in range(count)])
            value = value + other
            step *= 2
    return value


def allsum_exchange(value, axes):
    count = 1
    for axis in axes:
        count *= lax.axis_size(axis)
    flat = value.reshape(-1, value.shape[-1])
    if flat.shape[0] % count:
        return allsum(value, axes)
    parts = flat.reshape(count, -1, flat.shape[-1])
    got = lax.all_to_all(parts, axes, 0, 0, tiled=False)
    total = got[0]
    for k in range(1, count):
        total = total + got[k]
    spread = jnp.broadcast_to(total[None], (count,) + total.shape)
    back = lax.all_to_all(spread, axes, 0, 0, tiled=False)
    return back.reshape(value.shape)


def allsum_quad(value, axes):
    for axis in axes:
        count = lax.axis_size(axis)
        if count & (count - 1):
            value = lax.psum(value, axis)
            continue
        index = lax.axis_index(axis)
        step = 1
        while step < count:
            if step * 4 <= count:
                own = (index // step) % 4
                got = [value] + [
                    lax.ppermute(value, axis, [(i, i ^ (k * step)) for i in range(count)])
                    for k in (1, 2, 3)
                ]
                stack = jnp.stack(got)
                total = lax.dynamic_index_in_dim(stack, own, keepdims=False)
                for member in (1, 2, 3):
                    total = total + lax.dynamic_index_in_dim(stack, own ^ member, keepdims=False)
                value = total
                step *= 4
            else:
                other = lax.ppermute(value, axis, [(i, i ^ step) for i in range(count)])
                value = value + other
                step *= 2
    return value


def pack(block, coefs):
    width = block.shape[-1]
    flat = coefs.reshape(-1)
    spare = (-flat.shape[0]) % width
    flat = jnp.pad(flat, (0, spare))
    return jnp.concatenate([block.reshape(-1, width), flat.reshape(-1, width)], axis=0)


def unpack(packed, block_shape, coef_shape):
    count = block_shape[0] * block_shape[1]
    block = packed[:count].reshape(block_shape)
    size = coef_shape[0] * coef_shape[1] * coef_shape[2]
    coefs = packed[count:].reshape(-1)[:size].reshape(coef_shape)
    return block, coefs


def widen(block, coefs, axis, dim, depth, cdepth):
    head = lax.slice_in_dim(block, 0, depth, axis=dim)
    tail = lax.slice_in_dim(block, block.shape[dim] - depth, block.shape[dim], axis=dim)
    chead = lax.slice_in_dim(coefs, 0, cdepth, axis=dim + 1)
    ctail = lax.slice_in_dim(coefs, coefs.shape[dim + 1] - cdepth, coefs.shape[dim + 1], axis=dim + 1)
    before = shifted(pack(tail, ctail), axis, 1)
    after = shifted(pack(head, chead), axis, -1)
    before_b, before_c = unpack(before, head.shape, chead.shape)
    after_b, after_c = unpack(after, head.shape, chead.shape)
    block = jnp.concatenate([before_b, block, after_b], axis=dim)
    coefs = jnp.concatenate([before_c, coefs, after_c], axis=dim + 1)
    return block, coefs


def inset(cells, by):
    if by == 0:
        return cells
    return cells[by:cells.shape[0] - by, by:cells.shape[1] - by]


def neighbors(cells, links):
    cx, cy, cx_up, cy_left = links
    total = cx[:, :, None] * cells[2:, 1:-1] + cx_up[:, :, None] * cells[:-2, 1:-1]
    return total + cy[:, :, None] * cells[1:-1, 2:] + cy_left[:, :, None] * cells[1:-1, :-2]


def local_inner(left, right):
    a = left.reshape(-1, left.shape[-1])
    b = right.reshape(-1, right.shape[-1])
    return jnp.einsum("cp,cq->pq", a, b, precision=highest, preferred_element_type=jnp.float32)


def fold(first, second, third):
    size = first.shape[0]
    row = lax.broadcasted_iota(jnp.int32, first.shape, 0)
    col = lax.broadcasted_iota(jnp.int32, first.shape, 1)
    upper = row <= col
    on_diag = jnp.where(row == col, third, jnp.float32(0.0))
    across = jnp.sum(on_diag, axis=0, keepdims=True)
    down = jnp.sum(on_diag, axis=1, keepdims=True)
    spill = jnp.where(row == col + 1, across, jnp.float32(0.0))
    spill = jnp.where((row == size - 1) & (col == 0), down, spill)
    return jnp.stack([jnp.where(upper, first, third), jnp.where(upper, second, spill)])


def unfold(one, two):
    size = one.shape[0]
    row = lax.broadcasted_iota(jnp.int32, one.shape, 0)
    col = lax.broadcasted_iota(jnp.int32, one.shape, 1)
    upper = row <= col
    first = jnp.where(upper, one, jnp.transpose(one))
    second = jnp.where(upper, two, jnp.transpose(two))
    low = jnp.where(row > col, one, jnp.float32(0.0))
    across = jnp.sum(jnp.where(row == col + 1, two, jnp.float32(0.0)), axis=0, keepdims=True)
    lane = lax.broadcasted_iota(jnp.int32, (1, size), 1)
    across = jnp.where(lane == size - 1, two[size - 1:size, 0:1], across)
    third = low + jnp.transpose(low) + jnp.where(row == col, across, jnp.float32(0.0))
    return first, second, third


def _factor_kernel(packed_ref, cand_ref, basis_ref, g_out_ref, c_out_ref, work_ref, inv_ref):
    size = packed_ref.shape[1]
    gram, g_block, c_block = unfold(packed_ref[0], packed_ref[1])
    work_ref[...] = gram
    rows = lax.broadcasted_iota(jnp.int32, (size, size), 0)
    cols = lax.broadcasted_iota(jnp.int32, (size, size), 1)
    inv_ref[...] = jnp.where(rows == cols, jnp.float32(1.0), jnp.float32(0.0))
    lane = lax.broadcasted_iota(jnp.int32, (1, size), 1)
    chunk = 16
    for lo in range(0, size, chunk):
        span = size - lo
        cols_s = lax.broadcasted_iota(jnp.int32, (span, size), 1)
        sub = lo + lax.broadcasted_iota(jnp.int32, (span, 1), 0)

        def step(j, carry, lo=lo, cols_s=cols_s, sub=sub):
            whole = work_ref[lo:, :]
            row = work_ref[pl.ds(j, 1), :]
            column = jnp.sum(jnp.where(cols_s == j, whole, jnp.float32(0.0)), axis=1, keepdims=True)
            pivot = jnp.sum(jnp.where(lane == j, row, jnp.float32(0.0)), axis=1, keepdims=True)
            scale = lax.rsqrt(pivot)
            right = jnp.where(lane >= j, row * scale, jnp.float32(0.0))
            left = jnp.where(sub >= j, column * scale, jnp.float32(0.0))
            head = inv_ref[pl.ds(j, 1), :] * scale
            work_ref[lo:, :] = whole - left * right
            inv_ref[lo:, :] = inv_ref[lo:, :] - left * head
            inv_ref[pl.ds(j, 1), :] = head
            return carry

        lax.fori_loop(lo, min(lo + chunk, size), step, 0)

    inverse = inv_ref[...]
    by_rows = (((1,), (1,)), ((), ()))
    basis_ref[...] = lax.dot_general(
        cand_ref[...], inverse, by_rows, precision=highest, preferred_element_type=jnp.float32
    )
    for block, out_ref in ((g_block, g_out_ref), (c_block, c_out_ref)):
        half = jnp.dot(inverse, block, precision=highest, preferred_element_type=jnp.float32)
        out_ref[...] = lax.dot_general(
            half, inverse, by_rows, precision=highest, preferred_element_type=jnp.float32
        )


def orthonormalize(packed, cand):
    size = packed.shape[1]
    return pl.pallas_call(
        _factor_kernel,
        out_shape=(
            jax.ShapeDtypeStruct(cand.shape, jnp.float32),
            jax.ShapeDtypeStruct((size, size), jnp.float32),
            jax.ShapeDtypeStruct((size, size), jnp.float32),
        ),
        scratch_shapes=[pltpu.VMEM((size, size), jnp.float32), pltpu.VMEM((size, size), jnp.float32)],
    )(packed, cand)


def per_device(prior_basis, cond_x, cond_y, capacitance, pad_mask, port_nodes):
    rows_dev, cols_dev = cond_x.shape
    width = port_nodes.shape[0]
    count_x = lax.axis_size("gx")
    count_y = lax.axis_size("gy")
    total_rows = rows_dev * count_x
    total_cols = cols_dev * count_y
    nodes = total_rows * total_cols
    bdepth = SWEEPS + 1
    depth = SWEEPS + 2

    coefs = jnp.stack([cond_x, cond_y, capacitance, pad_mask.astype(jnp.float32)])
    basis_e, coefs_e = widen(prior_basis, coefs, "gx", 0, bdepth, depth)
    basis_e, coefs_e = widen(basis_e, coefs_e, "gy", 1, bdepth, depth)

    row_start = lax.axis_index("gx") * rows_dev - depth
    col_start = lax.axis_index("gy") * cols_dev - depth
    shape_e = (rows_dev + 2 * depth, cols_dev + 2 * depth)
    grows = row_start + lax.broadcasted_iota(jnp.int32, shape_e, 0)
    gcols = col_start + lax.broadcasted_iota(jnp.int32, shape_e, 1)
    inside = (grows >= 0) & (grows < total_rows) & (gcols >= 0) & (gcols < total_cols)
    cx_e = jnp.where(grows < total_rows - 1, coefs_e[0], jnp.float32(0.0))
    cy_e = jnp.where(gcols < total_cols - 1, coefs_e[1], jnp.float32(0.0))
    cap_e = coefs_e[2]
    pad_e = coefs_e[3]

    def at(cells, margin):
        return inset(cells, depth - margin)

    def at_basis(margin):
        return inset(basis_e, bdepth - margin)

    top = depth - 1
    cx_t = at(cx_e, top)
    cy_t = at(cy_e, top)
    cx_up_t = cx_e[0:-2, 1:-1]
    cy_left_t = cy_e[1:-1, 0:-2]
    diag_g_t = cx_t + cx_up_t + cy_t + cy_left_t + supply_conductance * at(pad_e, top)
    diag_t = diag_g_t + shift_point * at(cap_e, top)
    diag_t = jnp.where(at(inside, top), diag_t, jnp.float32(1.0))

    def links_at(margin):
        cut = top - margin
        return tuple(inset(c, cut) for c in (cx_t, cy_t, cx_up_t, cy_left_t))

    first = SWEEPS + 1
    node_ids = at(grows, first) * total_cols + at(gcols, first)
    onehot = (node_ids[:, :, None] == port_nodes[None, None, :]) & at(inside, first)[:, :, None]
    rhs = at(cap_e, first)[:, :, None] * at_basis(first) + port_current * onehot.astype(jnp.float32)
    diag_f = inset(diag_t, top - first)[:, :, None]

    field = rhs / diag_f
    for sweep in range(SWEEPS):
        margin = first - 1 - sweep
        field = (inset(rhs, first - margin) + neighbors(field, links_at(margin))) / inset(diag_f, first - margin)

    tile_basis = at_basis(0)
    proj = allsum_quad(local_inner(tile_basis, inset(field, 1)), ("gx", "gy")) / nodes
    cand_1 = field - jnp.einsum("xyk,kp->xyp", at_basis(1), proj, precision=highest)
    cand = inset(cand_1, 1)
    diag_g = inset(diag_g_t, top)[:, :, None]
    g_image = diag_g * cand - neighbors(cand_1, links_at(0))
    c_image = at(cap_e, 0)[:, :, None] * cand
    images = local_inner(cand, jnp.concatenate([cand, g_image, c_image], axis=-1))
    gram, g_raw, c_raw = images[:, :width], images[:, width:2 * width], images[:, 2 * width:]
    packed = allsum_exchange(fold(gram, g_raw, c_raw), ("gy", "gx")) / nodes
    basis_flat, reduced_g, reduced_c = orthonormalize(packed, cand.reshape(-1, width))
    new_basis = basis_flat.reshape(cand.shape)
    return (new_basis, reduced_g, reduced_c)


def solution(mesh):
    placed = (P("gx", "gy", None), P("gx", "gy"), P("gx", "gy"), P("gx", "gy"), P("gx", "gy"), P())
    return jax.shard_map(
        per_device,
        mesh=mesh,
        in_specs=placed,
        out_specs=(P("gx", "gy", None), P(), P()),
        check_vma=False,
    )
```
